32 devices in a mesh: gx: 4 (over z), gy: 4 (over x, core), sa: 2 (over y).
Axes of the slice: x: 2, y: 2, z: 4, core: 2. Of those that a mesh axis runs over, the one named last changes fastest.
Arguments:
- source: float32 [16, 256, 1024], P('sa', 'gx', 'gy'), parts along dimension 0, may hold values from -6 to 6
- sample_seeds: int32 [16], P('sa'), parts along dimension 0, may hold values from 0 to 7, each once
- perm_levels: float32 [16, 8], P('sa'), parts along dimension 0, may hold values from 0.1 to 10
- perm_classes: int32 [256, 1024], P('gx', 'gy'), may hold values from 0 to 7
Outputs:
- solution: float32 [16, 256, 1024], P('sa', 'gx', 'gy'), parts along dimension 0
- correction: float32 [16, 128, 512], P('sa', 'gx', 'gy'), parts along dimension 0
The draws below stay inside these ranges and needn't reach their ends.
There are 2 independent parts, one for each index of `sa`. The reference program is written for one: setup_inputs(seed, part) draws one part's arguments, and reference() takes and returns one part's arrays. A program takes and returns all parts, laid end to end along the dimension named above; an argument that names none is the same for every part. Nothing has to cross between parts.
Inputs may be any that keep to these rules, and one draw needn't show every extreme that they name: `sample_seeds`: each of 0 to 7 appears once.
All inputs are finite; a program needn't handle non-finite values.
Results may differ from the reference program's by a relative error of at most 0.0003.
Values sent between devices are 32-bit elements; how exact they have to be, the bound alone decides.
No kernel may reach another device: no remote copies, remote signals or barrier semaphores. Data moves between devices by JAX's collectives and lax.ppermute only.
A program may use at most 128 MiB of HBM per device.

```python
import math
import jax
import jax.numpy as jnp
from jax import lax

S = 8
CLASSES = 8
SWEEPS = 4
NX = 256
NY = 1024


def set_ends(drawn, key, least, largest):
    longest = drawn.shape.index(max(drawn.shape))
    spots = []
    for shift in (0, 1):
        where = [jax.random.randint(jax.random.fold_in(key, axis), (), 0, length) for axis, length in enumerate(drawn.shape)]
        where[longest] = (where[longest] + shift) % drawn.shape[longest]
        spots.append(tuple(where))
    return drawn.at[spots[0]].set(least).at[spots[1]].set(largest)


def steps_of(key, extent, cuts, least, high):
    def one(axis_at, blocks):
        heights = jax.random.uniform(jax.random.fold_in(jax.random.fold_in(key, 6), axis_at), (blocks,), jnp.float32, least / len(cuts), high / len(cuts))
        return jnp.repeat(jnp.exp(heights), extent[axis_at] // blocks).reshape((-1,) + (1,) * (len(extent) - axis_at - 1))

    level = one(*cuts[0])
    for cut in cuts[1:]:
        level = level * one(*cut)
    return level


def scatter_about(own_key, shape, spread, bound, shards=(), kind=jnp.bfloat16):
    drawn = spread * jax.random.normal(own_key, shape, jnp.float32)
    if shards:
        drawn = drawn * steps_of(own_key, shape, shards, -0.22, 0.18)
    return jnp.clip(drawn, -bound, bound).astype(kind)


def setup_inputs(seed: int = 0, part: int = 0) -> dict:
    streams_of = jax.random.split(jax.random.key(seed), 5)
    part_splits = jax.random.split(jax.random.fold_in(streams_of[4], part), 5)
    source = scatter_about(part_splits[0], (S, NX, NY), 1.0, 6.0, ((1, 4), (2, 4)), jnp.float32)
    sample_seeds = jax.random.permutation(part_splits[1], S).astype(jnp.int32)
    perm_levels = jnp.clip(jnp.exp(jax.random.uniform(part_splits[2], (S, CLASSES), jnp.float32, math.log(0.1), math.log(10.0))), 0.1, 10.0)
    perm_classes = set_ends(jax.random.randint(streams_of[3], (NX, NY), 0, CLASSES), jax.random.fold_in(streams_of[3], 1), 0, CLASSES - 1).astype(jnp.int32)
    return {"source": source, "sample_seeds": sample_seeds, "perm_levels": perm_levels, "perm_classes": perm_classes}


DAMPING = 0.8


def neighbours(padded):
    return (padded[..., 2:, 1:-1], padded[..., :-2, 1:-1], padded[..., 1:-1, 2:], padded[..., 1:-1, :-2])


def couplings(perm_padded):
    middle = perm_padded[..., 1:-1, 1:-1]
    linkage = tuple(jnp.where(beside > 0.0, 2.0 * middle * beside / (middle + beside), 2.0 * middle) for beside in neighbours(perm_padded))
    diagonal = linkage[0] + linkage[1] + linkage[2] + linkage[3]
    return linkage, diagonal


def operator(linkage, diagonal, current, padded):
    beside_all = neighbours(padded)
    return diagonal * current - (linkage[0] * beside_all[0] + linkage[1] * beside_all[1] + linkage[2] * beside_all[2] + linkage[3] * beside_all[3])


def permeability(sample_seeds, perm_levels, perm_classes):
    choose = (sample_seeds[:, None] == jnp.arange(perm_levels.shape[0], dtype=jnp.int32)[None, :]).astype(jnp.float32)
    sample_levels = jnp.sum(choose[:, :, None] * perm_levels[None, :, :], axis=1)
    result = jnp.zeros((sample_seeds.shape[0],) + perm_classes.shape, jnp.float32)
    for category in range(perm_levels.shape[1]):
        result = result + jnp.where(perm_classes[None] == category, sample_levels[:, category, None, None], 0.0)
    return result


def pad_edges(values):
    return jnp.pad(values, ((0, 0), (1, 1), (1, 1)))


def restrict(values):
    return values.reshape(values.shape[0], values.shape[1] // 2, 2, values.shape[2] // 2, 2).sum(axis=(2, 4))


def reference(source, sample_seeds, perm_levels, perm_classes):
    def one_pair(item):
        source_one, seed_one = item
        perm_field = permeability(seed_one[None], perm_levels, perm_classes)
        rhs_one = source_one[None]
        linkage, diagonal = couplings(pad_edges(perm_field))
        current = DAMPING * rhs_one / diagonal
        for sweep_index in range(SWEEPS):
            residual = rhs_one - operator(linkage, diagonal, current, pad_edges(current))
            if sweep_index + 1 < SWEEPS:
                current = current + DAMPING * residual / diagonal
        coarse_rhs = restrict(residual)
        coarse_perm = 0.25 * restrict(perm_field)
        coarse_links, coarse_diagonal = couplings(pad_edges(coarse_perm))
        first = DAMPING * coarse_rhs / coarse_diagonal
        correction = first + DAMPING * (coarse_rhs - operator(coarse_links, coarse_diagonal, first, pad_edges(first))) / coarse_diagonal
        updated = current + jnp.repeat(jnp.repeat(correction, 2, axis=1), 2, axis=2)
        return updated[0], correction[0]

    solution, correction = lax.map(one_pair, (source, sample_seeds))
    return solution, correction
```

```python
import jax
import jax.numpy as jnp
from jax import lax
from jax.sharding import PartitionSpec as P

SWEEPS = 4
DAMPING = 0.8
HALO = 8


def with_halo(block, sides, width):
    for axis, dim in sides:
        count = lax.axis_size(axis)
        forward = [(i, i + 1) for i in range(count - 1)]
        backward = [(target, source) for source, target in forward]
        low = lax.ppermute(
            lax.slice_in_dim(block, block.shape[dim] - width, None, axis=dim), axis, forward
        )
        high = lax.ppermute(lax.slice_in_dim(block, 0, width, axis=dim), axis, backward)
        block = jnp.concatenate([low, block, high], axis=dim)
    return block


def neighbours(padded):
    return (
        padded[..., 2:, 1:-1],
        padded[..., :-2, 1:-1],
        padded[..., 1:-1, 2:],
        padded[..., 1:-1, :-2],
    )


def pad_edges(values):
    return jnp.pad(values, ((0, 0), (1, 1), (1, 1)))


def couplings(perm_padded):
    middle = perm_padded[..., 1:-1, 1:-1]
    linkage = tuple(
        (
            jnp.where(beside > 0.0, 2.0 * middle * beside / (middle + beside), 2.0 * middle)
            for beside in neighbours(perm_padded)
        )
    )
    diagonal = linkage[0] + linkage[1] + linkage[2] + linkage[3]
    return (linkage, diagonal)


def operator(linkage, diagonal, current, padded):
    beside_all = neighbours(padded)
    return diagonal * current - (
        linkage[0] * beside_all[0]
        + linkage[1] * beside_all[1]
        + linkage[2] * beside_all[2]
        + linkage[3] * beside_all[3]
    )


def permeability(sample_seeds, perm_levels, classes):
    choose = (
        sample_seeds[:, None] == jnp.arange(perm_levels.shape[0], dtype=jnp.int32)[None, :]
    ).astype(jnp.float32)
    sample_levels = jnp.sum(choose[:, :, None] * perm_levels[None, :, :], axis=1)
    result = jnp.zeros((sample_seeds.shape[0],) + classes.shape, jnp.float32)
    for category in range(perm_levels.shape[1]):
        result = result + jnp.where(
            classes[None] == category, sample_levels[:, category, None, None], 0.0
        )
    return result


def inside_mask(rows, cols, width):
    own_x = rows - 2 * width
    own_y = cols - 2 * width
    r = lax.broadcasted_iota(jnp.int32, (rows, cols), 0) - width + lax.axis_index("gx") * own_x
    c = lax.broadcasted_iota(jnp.int32, (rows, cols), 1) - width + lax.axis_index("gy") * own_y
    return (r >= 0) & (r < lax.axis_size("gx") * own_x) & (c >= 0) & (c < lax.axis_size("gy") * own_y)


def pair_matrix(fine, coarse):
    f = lax.broadcasted_iota(jnp.int32, (fine, coarse), 0)
    c = lax.broadcasted_iota(jnp.int32, (fine, coarse), 1)
    return (f // 2 == c).astype(jnp.float32)


def restrict(values):
    rows, cols = values.shape[1], values.shape[2]
    ry = pair_matrix(cols, cols // 2)
    rx = pair_matrix(rows, rows // 2)
    hi = lax.Precision.HIGHEST
    half = jnp.einsum("sxy,yj->sxj", values, ry, precision=hi)
    return jnp.einsum("xi,sxj->sij", rx, half, precision=hi)


def prolong(values):
    rows, cols = values.shape[1], values.shape[2]
    ey = pair_matrix(2 * cols, cols)
    ex = pair_matrix(2 * rows, rows)
    hi = lax.Precision.HIGHEST
    wide = jnp.einsum("sij,yj->siy", values, ey, precision=hi)
    return jnp.einsum("xi,siy->sxy", ex, wide, precision=hi)


def shards(source, sample_seeds, perm_levels, perm_classes):
    h = HALO
    count, rows, cols = source.shape
    stacked = jnp.concatenate([source, perm_classes.astype(jnp.float32)[None]], axis=0)
    wide = with_halo(stacked, (("gx", 1), ("gy", 2)), h)
    source_wide = wide[:count]
    classes_wide = wide[count].astype(jnp.int32)
    inside = inside_mask(rows + 2 * h, cols + 2 * h, h)
    perm_field = jnp.where(
        inside[None], permeability(sample_seeds, perm_levels, classes_wide), 0.0
    )
    linkage, diagonal = couplings(pad_edges(perm_field))
    safe_diagonal = jnp.where(inside[None], diagonal, 1.0)
    current = DAMPING * source_wide / safe_diagonal
    for sweep_index in range(SWEEPS):
        residual = source_wide - operator(linkage, diagonal, current, pad_edges(current))
        if sweep_index + 1 < SWEEPS:
            current = current + DAMPING * residual / safe_diagonal
    coarse_rhs = restrict(residual)
    coarse_perm = 0.25 * restrict(perm_field)
    coarse_inside = inside_mask((rows + 2 * h) // 2, (cols + 2 * h) // 2, h // 2)
    coarse_links, coarse_diagonal = couplings(pad_edges(coarse_perm))
    coarse_safe = jnp.where(coarse_inside[None], coarse_diagonal, 1.0)
    first = DAMPING * coarse_rhs / coarse_safe
    correction = (
        first
        + DAMPING
        * (coarse_rhs - operator(coarse_links, coarse_diagonal, first, pad_edges(first)))
        / coarse_safe
    )
    c = h // 2
    correction = correction[:, c : c + rows // 2, c : c + cols // 2]
    updated = current[:, h : h + rows, h : h + cols] + prolong(correction)
    return (updated, correction)


def solution(mesh):
    placed = (P("sa", "gx", "gy"), P("sa"), P("sa", None), P("gx", "gy"))
    return jax.shard_map(
        shards,
        mesh=mesh,
        in_specs=placed,
        out_specs=(P("sa", "gx", "gy"), P("sa", "gx", "gy")),
        check_vma=False,
    )
```

```python
import jax
import jax.numpy as jnp
from jax import lax
from jax.sharding import PartitionSpec as P

SWEEPS = 4
DAMPING = 0.8
HALO = 8


def shifted(piece, dx, dy):
    nx = lax.axis_size("gx")
    ny = lax.axis_size("gy")
    pairs = [
        (i * ny + j, (i + dx) * ny + (j + dy))
        for i in range(nx)
        for j in range(ny)
        if 0 <= i + dx < nx and 0 <= j + dy < ny
    ]
    return lax.ppermute(piece, ("gx", "gy"), pairs)


def with_halo(block, width):
    rows, cols = block.shape[1], block.shape[2]
    low_x = slice(rows - width, rows)
    high_x = slice(0, width)
    low_y = slice(cols - width, cols)
    high_y = slice(0, width)
    every = slice(None)
    grid = []
    for dx, sx in ((1, low_x), (0, every), (-1, high_x)):
        line = []
        for dy, sy in ((1, low_y), (0, every), (-1, high_y)):
            piece = block[:, sx, sy]
            line.append(block if dx == 0 and dy == 0 else shifted(piece, dx, dy))
        grid.append(jnp.concatenate(line, axis=2))
    return jnp.concatenate(grid, axis=1)


def neighbours(padded):
    return (
        padded[..., 2:, 1:-1],
        padded[..., :-2, 1:-1],
        padded[..., 1:-1, 2:],
        padded[..., 1:-1, :-2],
    )


def pad_edges(values):
    return jnp.pad(values, ((0, 0), (1, 1), (1, 1)))


def couplings(perm_padded):
    middle = perm_padded[..., 1:-1, 1:-1]
    linkage = tuple(
        (
            jnp.where(beside > 0.0, 2.0 * middle * beside / (middle + beside), 2.0 * middle)
            for beside in neighbours(perm_padded)
        )
    )
    diagonal = linkage[0] + linkage[1] + linkage[2] + linkage[3]
    return (linkage, diagonal)


def operator(linkage, diagonal, current, padded):
    beside_all = neighbours(padded)
    return diagonal * current - (
        linkage[0] * beside_all[0]
        + linkage[1] * beside_all[1]
        + linkage[2] * beside_all[2]
        + linkage[3] * beside_all[3]
    )


def permeability(sample_seeds, perm_levels, classes):
    choose = (
        sample_seeds[:, None] == jnp.arange(perm_levels.shape[0], dtype=jnp.int32)[None, :]
    ).astype(jnp.float32)
    sample_levels = jnp.sum(choose[:, :, None] * perm_levels[None, :, :], axis=1)
    result = jnp.zeros((sample_seeds.shape[0],) + classes.shape, jnp.float32)
    for category in range(perm_levels.shape[1]):
        result = result + jnp.where(
            classes[None] == category, sample_levels[:, category, None, None], 0.0
        )
    return result


def inside_mask(rows, cols, width):
    own_x = rows - 2 * width
    own_y = cols - 2 * width
    r = lax.broadcasted_iota(jnp.int32, (rows, cols), 0) - width + lax.axis_index("gx") * own_x
    c = lax.broadcasted_iota(jnp.int32, (rows, cols), 1) - width + lax.axis_index("gy") * own_y
    return (r >= 0) & (r < lax.axis_size("gx") * own_x) & (c >= 0) & (c < lax.axis_size("gy") * own_y)


def pair_matrix(fine, coarse):
    f = lax.broadcasted_iota(jnp.int32, (fine, coarse), 0)
    c = lax.broadcasted_iota(jnp.int32, (fine, coarse), 1)
    return (f // 2 == c).astype(jnp.float32)


def restrict(values):
    rows, cols = values.shape[1], values.shape[2]
    ry = pair_matrix(cols, cols // 2)
    rx = pair_matrix(rows, rows // 2)
    hi = lax.Precision.HIGHEST
    half = jnp.einsum("sxy,yj->sxj", values, ry, precision=hi)
    return jnp.einsum("xi,sxj->sij", rx, half, precision=hi)


def prolong(values):
    rows, cols = values.shape[1], values.shape[2]
    ey = pair_matrix(2 * cols, cols)
    ex = pair_matrix(2 * rows, rows)
    hi = lax.Precision.HIGHEST
    wide = jnp.einsum("sij,yj->siy", values, ey, precision=hi)
    return jnp.einsum("xi,siy->sxy", ex, wide, precision=hi)


def shards(source, sample_seeds, perm_levels, perm_classes):
    h = HALO
    count, rows, cols = source.shape
    stacked = jnp.concatenate([source, perm_classes.astype(jnp.float32)[None]], axis=0)
    wide = with_halo(stacked, h)
    source_wide = wide[:count]
    classes_wide = wide[count].astype(jnp.int32)
    inside = inside_mask(rows + 2 * h, cols + 2 * h, h)
    perm_field = jnp.where(
        inside[None], permeability(sample_seeds, perm_levels, classes_wide), 0.0
    )
    linkage, diagonal = couplings(pad_edges(perm_field))
    safe_diagonal = jnp.where(inside[None], diagonal, 1.0)
    current = DAMPING * source_wide / safe_diagonal
    for sweep_index in range(SWEEPS):
        residual = source_wide - operator(linkage, diagonal, current, pad_edges(current))
        if sweep_index + 1 < SWEEPS:
            current = current + DAMPING * residual / safe_diagonal
    coarse_rhs = restrict(residual)
    coarse_perm = 0.25 * restrict(perm_field)
    coarse_inside = inside_mask((rows + 2 * h) // 2, (cols + 2 * h) // 2, h // 2)
    coarse_links, coarse_diagonal = couplings(pad_edges(coarse_perm))
    coarse_safe = jnp.where(coarse_inside[None], coarse_diagonal, 1.0)
    first = DAMPING * coarse_rhs / coarse_safe
    correction = (
        first
        + DAMPING
        * (coarse_rhs - operator(coarse_links, coarse_diagonal, first, pad_edges(first)))
        / coarse_safe
    )
    c = h // 2
    correction = correction[:, c : c + rows // 2, c : c + cols // 2]
    updated = current[:, h : h + rows, h : h + cols] + prolong(correction)
    return (updated, correction)


def solution(mesh):
    placed = (P("sa", "gx", "gy"), P("sa"), P("sa", None), P("gx", "gy"))
    return jax.shard_map(
        shards,
        mesh=mesh,
        in_specs=placed,
        out_specs=(P("sa", "gx", "gy"), P("sa", "gx", "gy")),
        check_vma=False,
    )
```

```python
import jax
import jax.numpy as jnp
from jax import lax
from jax.experimental import pallas as pl
from jax.experimental.pallas import tpu as pltpu
from jax.sharding import PartitionSpec as P

SWEEPS = 4
DAMPING = 0.8
HALO = 8
LANE_PAD = 128
HI = lax.Precision.HIGHEST


def exchange(block, axis, dim, width):
    count = lax.axis_size(axis)
    forward = [(i, i + 1) for i in range(count - 1)]
    backward = [(target, source) for source, target in forward]
    low = lax.ppermute(
        lax.slice_in_dim(block, block.shape[dim] - width, None, axis=dim), axis, forward
    )
    high = lax.ppermute(lax.slice_in_dim(block, 0, width, axis=dim), axis, backward)
    return low, high


def periodic_halo(block, width):
    low, high = exchange(block, "gx", 1, width)
    block = jnp.concatenate([block, high, low], axis=1)
    low, high = exchange(block, "gy", 2, width)
    gap = jnp.zeros(block.shape[:2] + (LANE_PAD - 2 * width,), block.dtype)
    return jnp.concatenate([block, high, gap, low], axis=2)


def neighbours(v):
    rows, cols = v.shape
    return (
        pltpu.roll(v, rows - 1, 0),
        pltpu.roll(v, 1, 0),
        pltpu.roll(v, cols - 1, 1),
        pltpu.roll(v, 1, 1),
    )


def couplings(perm):
    linkage = tuple(
        jnp.where(beside > 0.0, 2.0 * perm * beside / (perm + beside), 2.0 * perm)
        for beside in neighbours(perm)
    )
    diagonal = linkage[0] + linkage[1] + linkage[2] + linkage[3]
    return linkage, diagonal


def operator(linkage, diagonal, current):
    beside_all = neighbours(current)
    return diagonal * current - (
        linkage[0] * beside_all[0]
        + linkage[1] * beside_all[1]
        + linkage[2] * beside_all[2]
        + linkage[3] * beside_all[3]
    )


def dot(a, b):
    return jnp.dot(a, b, precision=HI, preferred_element_type=jnp.float32)


def smooth_kernel(
    levels_ref, src_ref, cls_ref, mask_ref, cmask_ref, rx_ref, ry_ref, ex_ref, ey_ref,
    sol_ref, corr_ref,
):
    s = pl.program_id(0)
    classes = cls_ref[0]
    valid = mask_ref[...] > 0.5
    perm = jnp.zeros(classes.shape, jnp.float32)
    for category in range(levels_ref.shape[1]):
        perm = perm + jnp.where(classes == float(category), levels_ref[s, category], 0.0)
    perm = jnp.where(valid, perm, 0.0)
    source = src_ref[0]
    linkage, diagonal = couplings(perm)
    safe_diagonal = jnp.where(valid, diagonal, 1.0)
    current = DAMPING * source / safe_diagonal
    for sweep_index in range(SWEEPS):
        residual = source - operator(linkage, diagonal, current)
        if sweep_index + 1 < SWEEPS:
            current = current + DAMPING * residual / safe_diagonal
    rx = rx_ref[...]
    ry = ry_ref[...]
    coarse_rhs = dot(dot(rx, residual), ry)
    coarse_perm = 0.25 * dot(dot(rx, perm), ry)
    coarse_valid = cmask_ref[...] > 0.5
    coarse_links, coarse_diagonal = couplings(coarse_perm)
    coarse_safe = jnp.where(coarse_valid, coarse_diagonal, 1.0)
    first = DAMPING * coarse_rhs / coarse_safe
    correction = (
        first
        + DAMPING * (coarse_rhs - operator(coarse_links, coarse_diagonal, first)) / coarse_safe
    )
    rows, cols = sol_ref.shape[1], sol_ref.shape[2]
    own = correction[: rows // 2, : cols // 2]
    corr_ref[0] = own
    sol_ref[0] = current[:rows, :cols] + dot(dot(ex_ref[...], own), ey_ref[...])


def offsets(n, wrap_at):
    f = jnp.arange(n, dtype=jnp.int32)
    return jnp.where(f < wrap_at, f, f - n)


def region(n, own, halo, wrap_at, index, count):
    g = offsets(n, wrap_at)
    near = (g >= -halo) & (g < own + halo)
    glob = g + index * own
    return near & (glob >= 0) & (glob < count * own)


def shards(source, sample_seeds, perm_levels, perm_classes):
    h = HALO
    count, rows, cols = source.shape
    ext_x, ext_y = rows + 2 * h, cols + LANE_PAD
    coarse_x = ext_x // 2
    coarse_y = -(-(ext_y // 2) // 128) * 128
    stacked = jnp.concatenate([source, perm_classes.astype(jnp.float32)[None]], axis=0)
    wide = periodic_halo(stacked, h)

    gx, gy = lax.axis_index("gx"), lax.axis_index("gy")
    nx, ny = lax.axis_size("gx"), lax.axis_size("gy")
    fine_r = region(ext_x, rows, h, rows + h, gx, nx)
    fine_c = region(ext_y, cols, h, cols + LANE_PAD // 2, gy, ny)
    mask = (fine_r[:, None] & fine_c[None, :]).astype(jnp.float32)
    coarse_r = region(coarse_x, rows // 2, h // 2, rows // 2 + h // 2, gx, nx)
    coarse_c = region(coarse_y, cols // 2, h // 2, cols // 2 + LANE_PAD // 4, gy, ny)
    cmask = (coarse_r[:, None] & coarse_c[None, :]).astype(jnp.float32)

    fr = jnp.arange(ext_x, dtype=jnp.int32)
    rx = (fr[None, :] // 2 == jnp.arange(coarse_x, dtype=jnp.int32)[:, None]).astype(jnp.float32)
    gcol = offsets(ext_y, cols + LANE_PAD // 2)
    near = (gcol >= -h) & (gcol < cols + h)
    target = jnp.mod(jnp.floor_divide(gcol, 2), coarse_y)
    ry = near[:, None] & (target[:, None] == jnp.arange(coarse_y, dtype=jnp.int32)[None, :])
    ry = ry.astype(jnp.float32)
    ex = (
        jnp.arange(rows, dtype=jnp.int32)[:, None] // 2
        == jnp.arange(rows // 2, dtype=jnp.int32)[None, :]
    ).astype(jnp.float32)
    ey = (
        jnp.arange(cols, dtype=jnp.int32)[None, :] // 2
        == jnp.arange(cols // 2, dtype=jnp.int32)[:, None]
    ).astype(jnp.float32)

    choose = (
        sample_seeds[:, None] == jnp.arange(perm_levels.shape[0], dtype=jnp.int32)[None, :]
    ).astype(jnp.float32)
    sample_levels = jnp.sum(choose[:, :, None] * perm_levels[None, :, :], axis=1)

    full = lambda shape: pl.BlockSpec(shape, lambda s: (0,) * len(shape))
    solution_block, correction_block = pl.pallas_call(
        smooth_kernel,
        grid=(count,),
        in_specs=[
            pl.BlockSpec(memory_space=pltpu.MemorySpace.SMEM),
            pl.BlockSpec((1, ext_x, ext_y), lambda s: (s, 0, 0)),
            pl.BlockSpec((1, ext_x, ext_y), lambda s: (count, 0, 0)),
            full((ext_x, ext_y)),
            full((coarse_x, coarse_y)),
            full((coarse_x, ext_x)),
            full((ext_y, coarse_y)),
            full((rows, rows // 2)),
            full((cols // 2, cols)),
        ],
        out_specs=[
            pl.BlockSpec((1, rows, cols), lambda s: (s, 0, 0)),
            pl.BlockSpec((1, rows // 2, cols // 2), lambda s: (s, 0, 0)),
        ],
        out_shape=[
            jax.ShapeDtypeStruct((count, rows, cols), jnp.float32),
            jax.ShapeDtypeStruct((count, rows // 2, cols // 2), jnp.float32),
        ],
    )(sample_levels, wide, wide, mask, cmask, rx, ry, ex, ey)
    return solution_block, correction_block


def solution(mesh):
    placed = (P("sa", "gx", "gy"), P("sa"), P("sa", None), P("gx", "gy"))
    return jax.shard_map(
        shards,
        mesh=mesh,
        in_specs=placed,
        out_specs=(P("sa", "gx", "gy"), P("sa", "gx", "gy")),
        check_vma=False,
    )
```

```python
import jax
import jax.numpy as jnp
from jax import lax
from jax.experimental import pallas as pl
from jax.experimental.pallas import tpu as pltpu
from jax.sharding import PartitionSpec as P

SWEEPS = 4
DAMPING = 0.8
HALO = 8
LANE_PAD = 128
HI = lax.Precision.HIGHEST


def exchange(block, axis, dim, width):
    count = lax.axis_size(axis)
    forward = [(i, i + 1) for i in range(count - 1)]
    backward = [(target, source) for source, target in forward]
    low = lax.ppermute(
        lax.slice_in_dim(block, block.shape[dim] - width, None, axis=dim), axis, forward
    )
    high = lax.ppermute(lax.slice_in_dim(block, 0, width, axis=dim), axis, backward)
    return low, high


def periodic_halo(block, width):
    low, high = exchange(block, "gx", 1, width)
    block = jnp.concatenate([block, high, low], axis=1)
    low, high = exchange(block, "gy", 2, width)
    gap = jnp.zeros(block.shape[:2] + (LANE_PAD - 2 * width,), block.dtype)
    return jnp.concatenate([block, high, gap, low], axis=2)


def rolled(v, step):
    rows, cols = v.shape
    return (
        pltpu.roll(v, rows - step, 0),
        pltpu.roll(v, step, 0),
        pltpu.roll(v, cols - step, 1),
        pltpu.roll(v, step, 1),
    )


def couplings(perm, step):
    down, up, right, left = rolled(perm, step)
    rows, cols = perm.shape
    twice = 2.0 * perm
    south = twice * down / (perm + down)
    east = twice * right / (perm + right)
    linkage = (
        jnp.where(down > 0.0, south, twice),
        jnp.where(up > 0.0, pltpu.roll(south, step, 0), twice),
        jnp.where(right > 0.0, east, twice),
        jnp.where(left > 0.0, pltpu.roll(east, step, 1), twice),
    )
    diagonal = linkage[0] + linkage[1] + linkage[2] + linkage[3]
    return linkage, diagonal


def operator(linkage, diagonal, current, step):
    beside_all = rolled(current, step)
    return diagonal * current - (
        linkage[0] * beside_all[0]
        + linkage[1] * beside_all[1]
        + linkage[2] * beside_all[2]
        + linkage[3] * beside_all[3]
    )


def smooth_kernel(levels_ref, src_ref, cls_ref, mask_ref, cmask_ref, sy_ref, sol_ref, corr_ref, spare):
    s = pl.program_id(0)
    classes = cls_ref[0]
    valid = mask_ref[...] > 0.5
    ext_x, ext_y = classes.shape
    perm = jnp.zeros(classes.shape, jnp.float32)
    for category in range(levels_ref.shape[1]):
        perm = perm + jnp.where(classes == float(category), levels_ref[s, category], 0.0)
    perm = jnp.where(valid, perm, 0.0)
    source = src_ref[0]
    linkage, diagonal = couplings(perm, 1)
    inverse = 1.0 / jnp.where(valid, diagonal, 1.0)
    current = (DAMPING * source) * inverse
    for sweep_index in range(SWEEPS):
        residual = source - operator(linkage, diagonal, current, 1)
        if sweep_index + 1 < SWEEPS:
            current = current + (DAMPING * residual) * inverse
    pairs = residual + pltpu.roll(residual, ext_x - 1, 0)
    coarse_rhs = pairs + pltpu.roll(pairs, ext_y - 1, 1)
    pairs = perm + pltpu.roll(perm, ext_x - 1, 0)
    coarse_perm = 0.25 * (pairs + pltpu.roll(pairs, ext_y - 1, 1))
    coarse_valid = cmask_ref[...] > 0.5
    coarse_links, coarse_diagonal = couplings(coarse_perm, 2)
    coarse_inverse = 1.0 / jnp.where(coarse_valid, coarse_diagonal, 1.0)
    first = (DAMPING * coarse_rhs) * coarse_inverse
    correction = first + (
        DAMPING * (coarse_rhs - operator(coarse_links, coarse_diagonal, first, 2))
    ) * coarse_inverse
    rows, cols = sol_ref.shape[1], sol_ref.shape[2]
    odd_row = (lax.broadcasted_iota(jnp.int32, classes.shape, 0) & 1) == 1
    odd_col = (lax.broadcasted_iota(jnp.int32, classes.shape, 1) & 1) == 1
    spread = jnp.where(odd_row, pltpu.roll(correction, 1, 0), correction)
    spread = jnp.where(odd_col, pltpu.roll(spread, 1, 1), spread)
    sol_ref[0] = current[:rows, :cols] + spread[:rows, :cols]
    pieces = []
    for k in range(cols // 128):
        spare[k] = correction[:, k * 128 : (k + 1) * 128]
        pieces.append(spare[k, pl.ds(0, rows // 2, stride=2), :])
    even_rows = jnp.concatenate(pieces, axis=1)
    corr_ref[0] = jnp.dot(even_rows, sy_ref[...], precision=HI, preferred_element_type=jnp.float32)


def offsets(n, wrap_at):
    f = jnp.arange(n, dtype=jnp.int32)
    return jnp.where(f < wrap_at, f, f - n)


def region(n, own, halo, wrap_at, index, count):
    g = offsets(n, wrap_at)
    near = (g >= -halo) & (g < own + halo)
    glob = g + index * own
    return near & (glob >= 0) & (glob < count * own)


def shards(source, sample_seeds, perm_levels, perm_classes):
    h = HALO
    count, rows, cols = source.shape
    ext_x, ext_y = rows + 2 * h, cols + LANE_PAD
    stacked = jnp.concatenate([source, perm_classes.astype(jnp.float32)[None]], axis=0)
    wide = periodic_halo(stacked, h)

    gx, gy = lax.axis_index("gx"), lax.axis_index("gy")
    nx, ny = lax.axis_size("gx"), lax.axis_size("gy")
    fine_r = region(ext_x, rows, h, rows + h, gx, nx)
    fine_c = region(ext_y, cols, h, cols + LANE_PAD // 2, gy, ny)
    mask = (fine_r[:, None] & fine_c[None, :]).astype(jnp.float32)
    fr = jnp.arange(ext_x, dtype=jnp.int32)
    fc = jnp.arange(ext_y, dtype=jnp.int32)
    even = ((fr[:, None] & 1) == 0) & ((fc[None, :] & 1) == 0)
    cmask = ((fine_r[:, None] & fine_c[None, :]) & even).astype(jnp.float32)
    sy = (fc[:cols, None] == 2 * jnp.arange(cols // 2, dtype=jnp.int32)[None, :]).astype(jnp.float32)

    choose = (
        sample_seeds[:, None] == jnp.arange(perm_levels.shape[0], dtype=jnp.int32)[None, :]
    ).astype(jnp.float32)
    sample_levels = jnp.sum(choose[:, :, None] * perm_levels[None, :, :], axis=1)

    full = lambda shape: pl.BlockSpec(shape, lambda s: (0,) * len(shape))
    solution_block, correction_block = pl.pallas_call(
        smooth_kernel,
        grid=(count,),
        in_specs=[
            pl.BlockSpec(memory_space=pltpu.MemorySpace.SMEM),
            pl.BlockSpec((1, ext_x, ext_y), lambda s: (s, 0, 0)),
            pl.BlockSpec((1, ext_x, ext_y), lambda s: (count, 0, 0)),
            full((ext_x, ext_y)),
            full((ext_x, ext_y)),
            full((cols, cols // 2)),
        ],
        out_specs=[
            pl.BlockSpec((1, rows, cols), lambda s: (s, 0, 0)),
            pl.BlockSpec((1, rows // 2, cols // 2), lambda s: (s, 0, 0)),
        ],
        out_shape=[
            jax.ShapeDtypeStruct((count, rows, cols), jnp.float32),
            jax.ShapeDtypeStruct((count, rows // 2, cols // 2), jnp.float32),
        ],
        scratch_shapes=[pltpu.VMEM((cols // 128, ext_x, 128), jnp.float32)],
    )(sample_levels, wide, wide, mask, cmask, sy)
    return solution_block, correction_block


def solution(mesh):
    placed = (P("sa", "gx", "gy"), P("sa"), P("sa", None), P("gx", "gy"))
    return jax.shard_map(
        shards,
        mesh=mesh,
        in_specs=placed,
        out_specs=(P("sa", "gx", "gy"), P("sa", "gx", "gy")),
        check_vma=False,
    )
```

```python
import jax
import jax.numpy as jnp
from jax import lax
from jax.experimental import pallas as pl
from jax.experimental.pallas import tpu as pltpu
from jax.sharding import PartitionSpec as P

SWEEPS = 4
DAMPING = 0.8
HALO = 8
LANE_PAD = 128
HI = lax.Precision.HIGHEST


def halo_pieces(source, classes, width):
    stack = lambda a, b: jnp.concatenate([a, b[None]], axis=0)
    low = lax.ppermute(
        stack(source[:, -width:, :], classes[-width:, :]), "gx",
        [(i, i + 1) for i in range(lax.axis_size("gx") - 1)],
    )
    high = lax.ppermute(
        stack(source[:, :width, :], classes[:width, :]), "gx",
        [(i + 1, i) for i in range(lax.axis_size("gx") - 1)],
    )
    rows_halo = jnp.concatenate([high, low], axis=1)
    last = jnp.concatenate([stack(source[:, :, -width:], classes[:, -width:]), rows_halo[:, :, -width:]], axis=1)
    first = jnp.concatenate([stack(source[:, :, :width], classes[:, :width]), rows_halo[:, :, :width]], axis=1)
    low = lax.ppermute(last, "gy", [(i, i + 1) for i in range(lax.axis_size("gy") - 1)])
    high = lax.ppermute(first, "gy", [(i + 1, i) for i in range(lax.axis_size("gy") - 1)])
    gap = jnp.zeros(high.shape[:2] + (LANE_PAD - 2 * width,), high.dtype)
    return rows_halo, jnp.concatenate([high, gap, low], axis=2)


def rolled(v, step):
    rows, cols = v.shape
    return (
        pltpu.roll(v, rows - step, 0),
        pltpu.roll(v, step, 0),
        pltpu.roll(v, cols - step, 1),
        pltpu.roll(v, step, 1),
    )


def couplings(perm, step):
    down, up, right, left = rolled(perm, step)
    rows, cols = perm.shape
    twice = 2.0 * perm
    south = twice * down / (perm + down)
    east = twice * right / (perm + right)
    linkage = (
        jnp.where(down > 0.0, south, twice),
        jnp.where(up > 0.0, pltpu.roll(south, step, 0), twice),
        jnp.where(right > 0.0, east, twice),
        jnp.where(left > 0.0, pltpu.roll(east, step, 1), twice),
    )
    diagonal = linkage[0] + linkage[1] + linkage[2] + linkage[3]
    return linkage, diagonal


def operator(linkage, diagonal, current, step):
    beside_all = rolled(current, step)
    return diagonal * current - (
        linkage[0] * beside_all[0]
        + linkage[1] * beside_all[1]
        + linkage[2] * beside_all[2]
        + linkage[3] * beside_all[3]
    )


def inside(shape, own_x, own_y, place_ref):
    ext_x, ext_y = shape
    r = lax.broadcasted_iota(jnp.int32, shape, 0)
    c = lax.broadcasted_iota(jnp.int32, shape, 1)
    g_r = jnp.where(r < own_x + HALO, r, r - ext_x)
    g_c = jnp.where(c < own_y + LANE_PAD // 2, c, c - ext_y)
    glob_r = g_r + place_ref[0] * own_x
    glob_c = g_c + place_ref[1] * own_y
    near = (g_c >= -HALO) & (g_c < own_y + HALO)
    return (
        near
        & (glob_r >= 0) & (glob_r < place_ref[2] * own_x)
        & (glob_c >= 0) & (glob_c < place_ref[3] * own_y)
    ), r, c


def smooth_kernel(
    levels_ref, place_ref, src_ref, cls_ref, rows_ref, crows_ref, tile_ref, ctile_ref,
    sol_ref, corr_ref, source_ext, classes_ext, mask_ext, cmask_ext, spare,
):
    s = pl.program_id(0)
    rows, cols = sol_ref.shape[1], sol_ref.shape[2]
    ext_x, ext_y = source_ext.shape

    @pl.when(s == 0)
    def _():
        valid, r, c = inside((ext_x, ext_y), rows, cols, place_ref)
        even = ((r & 1) == 0) & ((c & 1) == 0)
        mask_ext[...] = valid.astype(jnp.float32)
        cmask_ext[...] = (valid & even).astype(jnp.float32)
        classes_ext[:rows, :cols] = cls_ref[...]
        classes_ext[rows:, :cols] = crows_ref[0].astype(jnp.int32)
        classes_ext[:, cols:] = ctile_ref[0].astype(jnp.int32)

    source_ext[:rows, :cols] = src_ref[0]
    source_ext[rows:, :cols] = rows_ref[0]
    source_ext[:, cols:] = tile_ref[0]
    source = source_ext[...]
    classes = classes_ext[...]
    valid = mask_ext[...] > 0.5
    level = [levels_ref[s, category] for category in range(levels_ref.shape[1])]
    bit0 = (classes & 1) != 0
    bit1 = (classes & 2) != 0
    bit2 = (classes & 4) != 0
    low = jnp.where(bit1, jnp.where(bit0, level[3], level[2]), jnp.where(bit0, level[1], level[0]))
    high = jnp.where(bit1, jnp.where(bit0, level[7], level[6]), jnp.where(bit0, level[5], level[4]))
    perm = jnp.where(valid, jnp.where(bit2, high, low), 0.0)
    linkage, diagonal = couplings(perm, 1)
    inverse = 1.0 / jnp.where(valid, diagonal, 1.0)
    current = (DAMPING * source) * inverse
    for sweep_index in range(SWEEPS):
        residual = source - operator(linkage, diagonal, current, 1)
        if sweep_index + 1 < SWEEPS:
            current = current + (DAMPING * residual) * inverse
    pairs = residual + pltpu.roll(residual, ext_x - 1, 0)
    coarse_rhs = pairs + pltpu.roll(pairs, ext_y - 1, 1)
    pairs = perm + pltpu.roll(perm, ext_x - 1, 0)
    coarse_perm = 0.25 * (pairs + pltpu.roll(pairs, ext_y - 1, 1))
    coarse_valid = cmask_ext[...] > 0.5
    coarse_links, coarse_diagonal = couplings(coarse_perm, 2)
    coarse_inverse = 1.0 / jnp.where(coarse_valid, coarse_diagonal, 1.0)
    first = (DAMPING * coarse_rhs) * coarse_inverse
    correction = first + (
        DAMPING * (coarse_rhs - operator(coarse_links, coarse_diagonal, first, 2))
    ) * coarse_inverse
    odd_row = (lax.broadcasted_iota(jnp.int32, (ext_x, ext_y), 0) & 1) == 1
    odd_col = (lax.broadcasted_iota(jnp.int32, (ext_x, ext_y), 1) & 1) == 1
    spread = jnp.where(odd_row, pltpu.roll(correction, 1, 0), correction)
    spread = jnp.where(odd_col, pltpu.roll(spread, 1, 1), spread)
    sol_ref[0] = current[:rows, :cols] + spread[:rows, :cols]
    pieces = []
    for k in range(cols // 128):
        spare[k] = correction[:, k * 128 : (k + 1) * 128]
        pieces.append(spare[k, pl.ds(0, rows // 2, stride=2), :])
    even_rows = jnp.concatenate(pieces, axis=1)
    pick = (
        lax.broadcasted_iota(jnp.int32, (cols, cols // 2), 0)
        == 2 * lax.broadcasted_iota(jnp.int32, (cols, cols // 2), 1)
    ).astype(jnp.float32)
    corr_ref[0] = jnp.dot(even_rows, pick, precision=HI, preferred_element_type=jnp.float32)


def shards(source, sample_seeds, perm_levels, perm_classes):
    h = HALO
    count, rows, cols = source.shape
    ext_x, ext_y = rows + 2 * h, cols + LANE_PAD
    rows_halo, lane_tile = halo_pieces(source, perm_classes.astype(jnp.float32), h)
    place = jnp.stack(
        [lax.axis_index("gx"), lax.axis_index("gy"), lax.axis_size("gx"), lax.axis_size("gy")]
    ).astype(jnp.int32)
    choose = (
        sample_seeds[:, None] == jnp.arange(perm_levels.shape[0], dtype=jnp.int32)[None, :]
    ).astype(jnp.float32)
    sample_levels = jnp.sum(choose[:, :, None] * perm_levels[None, :, :], axis=1)

    smem = pl.BlockSpec(memory_space=pltpu.MemorySpace.SMEM)
    solution_block, correction_block = pl.pallas_call(
        smooth_kernel,
        grid=(count,),
        in_specs=[
            smem,
            smem,
            pl.BlockSpec((1, rows, cols), lambda s: (s, 0, 0)),
            pl.BlockSpec((rows, cols), lambda s: (0, 0)),
            pl.BlockSpec((1, 2 * h, cols), lambda s: (s, 0, 0)),
            pl.BlockSpec((1, 2 * h, cols), lambda s: (count, 0, 0)),
            pl.BlockSpec((1, ext_x, LANE_PAD), lambda s: (s, 0, 0)),
            pl.BlockSpec((1, ext_x, LANE_PAD), lambda s: (count, 0, 0)),
        ],
        out_specs=[
            pl.BlockSpec((1, rows, cols), lambda s: (s, 0, 0)),
            pl.BlockSpec((1, rows // 2, cols // 2), lambda s: (s, 0, 0)),
        ],
        out_shape=[
            jax.ShapeDtypeStruct((count, rows, cols), jnp.float32),
            jax.ShapeDtypeStruct((count, rows // 2, cols // 2), jnp.float32),
        ],
        scratch_shapes=[
            pltpu.VMEM((ext_x, ext_y), jnp.float32),
            pltpu.VMEM((ext_x, ext_y), jnp.int32),
            pltpu.VMEM((ext_x, ext_y), jnp.float32),
            pltpu.VMEM((ext_x, ext_y), jnp.float32),
            pltpu.VMEM((cols // 128, ext_x, 128), jnp.float32),
        ],
        compiler_params=pltpu.CompilerParams(dimension_semantics=("arbitrary",)),
    )(sample_levels, place, source, perm_classes, rows_halo, rows_halo, lane_tile, lane_tile)
    return solution_block, correction_block


def solution(mesh):
    placed = (P("sa", "gx", "gy"), P("sa"), P("sa", None), P("gx", "gy"))
    return jax.shard_map(
        shards,
        mesh=mesh,
        in_specs=placed,
        out_specs=(P("sa", "gx", "gy"), P("sa", "gx", "gy")),
        check_vma=False,
    )
```

```python
import jax
import jax.numpy as jnp
from jax import lax
from jax.experimental import pallas as pl
from jax.experimental.pallas import tpu as pltpu
from jax.sharding import PartitionSpec as P

SWEEPS = 4
DAMPING = 0.8
HALO = 8
LANE_PAD = 128
HI = lax.Precision.HIGHEST


def halo_pieces(source, codes, width):
    stack = lambda a, b: jnp.concatenate([a, b[None]], axis=0)
    low = lax.ppermute(
        stack(source[:, -width:, :], codes[-width:, :]), "gx",
        [(i, i + 1) for i in range(lax.axis_size("gx") - 1)],
    )
    high = lax.ppermute(
        stack(source[:, :width, :], codes[:width, :]), "gx",
        [(i + 1, i) for i in range(lax.axis_size("gx") - 1)],
    )
    rows_halo = jnp.concatenate([high, low], axis=1)

    def packed(strip, halo_strip):
        planes = jnp.concatenate([strip, halo_strip], axis=1)
        count, rows, _ = planes.shape
        flat = jnp.transpose(planes, (1, 0, 2)).reshape(rows, count * width)
        return jnp.pad(flat, ((0, 0), (0, LANE_PAD - count * width)))

    last = packed(stack(source[:, :, -width:], codes[:, -width:]), rows_halo[:, :, -width:])
    first = packed(stack(source[:, :, :width], codes[:, :width]), rows_halo[:, :, :width])
    low = lax.ppermute(last, "gy", [(i, i + 1) for i in range(lax.axis_size("gy") - 1)])
    high = lax.ppermute(first, "gy", [(i + 1, i) for i in range(lax.axis_size("gy") - 1)])
    return rows_halo, high, low


def rolled(v, step):
    rows, cols = v.shape
    return (
        pltpu.roll(v, rows - step, 0),
        pltpu.roll(v, step, 0),
        pltpu.roll(v, cols - step, 1),
        pltpu.roll(v, step, 1),
    )


def couplings(perm, step):
    down, up, right, left = rolled(perm, step)
    rows, cols = perm.shape
    twice = 2.0 * perm
    south = twice * down / (perm + down)
    east = twice * right / (perm + right)
    linkage = (
        jnp.where(down > 0.0, south, twice),
        jnp.where(up > 0.0, pltpu.roll(south, step, 0), twice),
        jnp.where(right > 0.0, east, twice),
        jnp.where(left > 0.0, pltpu.roll(east, step, 1), twice),
    )
    diagonal = linkage[0] + linkage[1] + linkage[2] + linkage[3]
    return linkage, diagonal


def operator(linkage, diagonal, current, step):
    beside_all = rolled(current, step)
    return diagonal * current - (
        linkage[0] * beside_all[0]
        + linkage[1] * beside_all[1]
        + linkage[2] * beside_all[2]
        + linkage[3] * beside_all[3]
    )


def lane_tile(high_ref, low_ref, plane):
    high = high_ref[...]
    low = low_ref[...]
    lane = lax.broadcasted_iota(jnp.int32, high.shape, 1)
    after = pltpu.roll(high, (LANE_PAD - HALO * plane) % LANE_PAD, 1)
    before = pltpu.roll(low, (LANE_PAD - HALO - HALO * plane) % LANE_PAD, 1)
    return jnp.where(lane < HALO, after, jnp.where(lane >= LANE_PAD - HALO, before, 0.0))


def smooth_kernel(
    seeds_ref, levels_ref, src_ref, cls_ref, rows_ref, crows_ref, high_ref, low_ref,
    sol_ref, corr_ref, source_ext, codes_ext, spare,
):
    s = pl.program_id(0)
    count = pl.num_programs(0)
    rows, cols = sol_ref.shape[1], sol_ref.shape[2]
    ext_x, ext_y = source_ext.shape

    @pl.when(s == 0)
    def _():
        codes_ext[:rows, :cols] = cls_ref[...] + 1
        codes_ext[rows:, :cols] = crows_ref[0].astype(jnp.int32)
        codes_ext[:, cols:] = lane_tile(high_ref, low_ref, count).astype(jnp.int32)

    source_ext[:rows, :cols] = src_ref[0]
    source_ext[rows:, :cols] = rows_ref[0]
    source_ext[:, cols:] = lane_tile(high_ref, low_ref, s)
    source = source_ext[...]
    codes = codes_ext[...]
    valid = codes > 0
    classes = codes - 1
    seed = seeds_ref[s]
    level = [levels_ref[seed, category] for category in range(levels_ref.shape[1])]
    bit0 = (classes & 1) != 0
    bit1 = (classes & 2) != 0
    bit2 = (classes & 4) != 0
    low = jnp.where(bit1, jnp.where(bit0, level[3], level[2]), jnp.where(bit0, level[1], level[0]))
    high = jnp.where(bit1, jnp.where(bit0, level[7], level[6]), jnp.where(bit0, level[5], level[4]))
    perm = jnp.where(valid, jnp.where(bit2, high, low), 0.0)
    linkage, diagonal = couplings(perm, 1)
    inverse = 1.0 / jnp.where(valid, diagonal, 1.0)
    current = (DAMPING * source) * inverse
    for sweep_index in range(SWEEPS):
        residual = source - operator(linkage, diagonal, current, 1)
        if sweep_index + 1 < SWEEPS:
            current = current + (DAMPING * residual) * inverse
    pairs = residual + pltpu.roll(residual, ext_x - 1, 0)
    coarse_rhs = pairs + pltpu.roll(pairs, ext_y - 1, 1)
    pairs = perm + pltpu.roll(perm, ext_x - 1, 0)
    coarse_perm = 0.25 * (pairs + pltpu.roll(pairs, ext_y - 1, 1))
    odd_row = (lax.broadcasted_iota(jnp.int32, (ext_x, ext_y), 0) & 1) == 1
    odd_col = (lax.broadcasted_iota(jnp.int32, (ext_x, ext_y), 1) & 1) == 1
    coarse_valid = valid & jnp.logical_not(odd_row | odd_col)
    coarse_links, coarse_diagonal = couplings(coarse_perm, 2)
    coarse_inverse = 1.0 / jnp.where(coarse_valid, coarse_diagonal, 1.0)
    first = (DAMPING * coarse_rhs) * coarse_inverse
    correction = first + (
        DAMPING * (coarse_rhs - operator(coarse_links, coarse_diagonal, first, 2))
    ) * coarse_inverse
    spread = jnp.where(odd_row, pltpu.roll(correction, 1, 0), correction)
    spread = jnp.where(odd_col, pltpu.roll(spread, 1, 1), spread)
    sol_ref[0] = current[:rows, :cols] + spread[:rows, :cols]
    pieces = []
    for k in range(cols // 128):
        spare[k] = correction[:, k * 128 : (k + 1) * 128]
        pieces.append(spare[k, pl.ds(0, rows // 2, stride=2), :])
    even_rows = jnp.concatenate(pieces, axis=1)
    pick = (
        lax.broadcasted_iota(jnp.int32, (cols, cols // 2), 0)
        == 2 * lax.broadcasted_iota(jnp.int32, (cols, cols // 2), 1)
    ).astype(jnp.float32)
    corr_ref[0] = jnp.dot(even_rows, pick, precision=HI, preferred_element_type=jnp.float32)


def shards(source, sample_seeds, perm_levels, perm_classes):
    h = HALO
    count, rows, cols = source.shape
    ext_x, ext_y = rows + 2 * h, cols + LANE_PAD
    rows_halo, high, low = halo_pieces(source, (perm_classes + 1).astype(jnp.float32), h)
    smem = pl.BlockSpec(memory_space=pltpu.MemorySpace.SMEM)
    whole = lambda shape: pl.BlockSpec(shape, lambda s: (0,) * len(shape))
    solution_block, correction_block = pl.pallas_call(
        smooth_kernel,
        grid=(count,),
        in_specs=[
            smem,
            smem,
            pl.BlockSpec((1, rows, cols), lambda s: (s, 0, 0)),
            whole((rows, cols)),
            pl.BlockSpec((1, 2 * h, cols), lambda s: (s, 0, 0)),
            pl.BlockSpec((1, 2 * h, cols), lambda s: (count, 0, 0)),
            whole((ext_x, LANE_PAD)),
            whole((ext_x, LANE_PAD)),
        ],
        out_specs=[
            pl.BlockSpec((1, rows, cols), lambda s: (s, 0, 0)),
            pl.BlockSpec((1, rows // 2, cols // 2), lambda s: (s, 0, 0)),
        ],
        out_shape=[
            jax.ShapeDtypeStruct((count, rows, cols), jnp.float32),
            jax.ShapeDtypeStruct((count, rows // 2, cols // 2), jnp.float32),
        ],
        scratch_shapes=[
            pltpu.VMEM((ext_x, ext_y), jnp.float32),
            pltpu.VMEM((ext_x, ext_y), jnp.int32),
            pltpu.VMEM((cols // 128, ext_x, 128), jnp.float32),
        ],
        compiler_params=pltpu.CompilerParams(dimension_semantics=("arbitrary",)),
    )(sample_seeds, perm_levels, source, perm_classes, rows_halo, rows_halo, high, low)
    return solution_block, correction_block


def solution(mesh):
    placed = (P("sa", "gx", "gy"), P("sa"), P("sa", None), P("gx", "gy"))
    return jax.shard_map(
        shards,
        mesh=mesh,
        in_specs=placed,
        out_specs=(P("sa", "gx", "gy"), P("sa", "gx", "gy")),
        check_vma=False,
    )
```

```python
import jax
import jax.numpy as jnp
from jax import lax
from jax.experimental import pallas as pl
from jax.experimental.pallas import tpu as pltpu
from jax.sharding import PartitionSpec as P

SWEEPS = 4
DAMPING = 0.8
HALO = 8
LANE_PAD = 128
HI = lax.Precision.HIGHEST


def halo_pieces(source, codes, width):
    stack = lambda a, b: jnp.concatenate([a, b[None]], axis=0)
    low = lax.ppermute(
        stack(source[:, -width:, :], codes[-width:, :]), "gx",
        [(i, i + 1) for i in range(lax.axis_size("gx") - 1)],
    )
    high = lax.ppermute(
        stack(source[:, :width, :], codes[:width, :]), "gx",
        [(i + 1, i) for i in range(lax.axis_size("gx") - 1)],
    )
    rows_halo = jnp.concatenate([high, low], axis=1)

    def packed(strip, halo_strip):
        planes = jnp.concatenate([strip, halo_strip], axis=1)
        count, rows, _ = planes.shape
        flat = jnp.transpose(planes, (1, 0, 2)).reshape(rows, count * width)
        return jnp.pad(flat, ((0, 0), (0, LANE_PAD - count * width)))

    last = packed(stack(source[:, :, -width:], codes[:, -width:]), rows_halo[:, :, -width:])
    first = packed(stack(source[:, :, :width], codes[:, :width]), rows_halo[:, :, :width])
    low = lax.ppermute(last, "gy", [(i, i + 1) for i in range(lax.axis_size("gy") - 1)])
    high = lax.ppermute(first, "gy", [(i + 1, i) for i in range(lax.axis_size("gy") - 1)])
    return rows_halo, high, low


def rolled(v, step):
    rows, cols = v.shape
    down, across = step
    return (
        pltpu.roll(v, rows - down, 0),
        pltpu.roll(v, down, 0),
        pltpu.roll(v, cols - across, 1),
        pltpu.roll(v, across, 1),
    )


def couplings(perm, step):
    down, up, right, left = rolled(perm, step)
    twice = 2.0 * perm
    south = twice * down / (perm + down)
    east = twice * right / (perm + right)
    linkage = (
        jnp.where(down > 0.0, south, twice),
        jnp.where(up > 0.0, pltpu.roll(south, step[0], 0), twice),
        jnp.where(right > 0.0, east, twice),
        jnp.where(left > 0.0, pltpu.roll(east, step[1], 1), twice),
    )
    diagonal = linkage[0] + linkage[1] + linkage[2] + linkage[3]
    return linkage, diagonal


def operator(linkage, diagonal, current, step):
    beside_all = rolled(current, step)
    return diagonal * current - (
        linkage[0] * beside_all[0]
        + linkage[1] * beside_all[1]
        + linkage[2] * beside_all[2]
        + linkage[3] * beside_all[3]
    )


def lane_tile(high_ref, low_ref, plane):
    high = high_ref[...]
    low = low_ref[...]
    lane = lax.broadcasted_iota(jnp.int32, high.shape, 1)
    after = pltpu.roll(high, (LANE_PAD - HALO * plane) % LANE_PAD, 1)
    before = pltpu.roll(low, (LANE_PAD - HALO - HALO * plane) % LANE_PAD, 1)
    return jnp.where(lane < HALO, after, jnp.where(lane >= LANE_PAD - HALO, before, 0.0))


def smooth_kernel(
    seeds_ref, levels_ref, src_ref, cls_ref, rows_ref, crows_ref, high_ref, low_ref,
    sol_ref, corr_ref, source_ext, codes_ext, spare, wide,
):
    s = pl.program_id(0)
    count = pl.num_programs(0)
    rows, cols = sol_ref.shape[1], sol_ref.shape[2]
    ext_x, ext_y = source_ext.shape

    @pl.when(s == 0)
    def _():
        codes_ext[:rows, :cols] = cls_ref[...] + 1
        codes_ext[rows:, :cols] = crows_ref[0].astype(jnp.int32)
        codes_ext[:, cols:] = lane_tile(high_ref, low_ref, count).astype(jnp.int32)

    source_ext[:rows, :cols] = src_ref[0]
    source_ext[rows:, :cols] = rows_ref[0]
    source_ext[:, cols:] = lane_tile(high_ref, low_ref, s)
    source = source_ext[...]
    codes = codes_ext[...]
    valid = codes > 0
    classes = codes - 1
    seed = seeds_ref[s]
    level = [levels_ref[seed, category] for category in range(levels_ref.shape[1])]
    bit0 = (classes & 1) != 0
    bit1 = (classes & 2) != 0
    bit2 = (classes & 4) != 0
    low = jnp.where(bit1, jnp.where(bit0, level[3], level[2]), jnp.where(bit0, level[1], level[0]))
    high = jnp.where(bit1, jnp.where(bit0, level[7], level[6]), jnp.where(bit0, level[5], level[4]))
    perm = jnp.where(valid, jnp.where(bit2, high, low), 0.0)
    linkage, diagonal = couplings(perm, (1, 1))
    inverse = 1.0 / jnp.where(valid, diagonal, 1.0)
    current = (DAMPING * source) * inverse
    for sweep_index in range(SWEEPS):
        residual = source - operator(linkage, diagonal, current, (1, 1))
        if sweep_index + 1 < SWEEPS:
            current = current + (DAMPING * residual) * inverse

    def even_rows(v):
        pieces = []
        for k in range(ext_y // 128):
            spare[k] = v[:, k * 128 : (k + 1) * 128]
            pieces.append(spare[k, pl.ds(0, ext_x // 2, stride=2), :])
        return jnp.concatenate(pieces, axis=1)

    pairs = residual + pltpu.roll(residual, ext_x - 1, 0)
    coarse_rhs = even_rows(pairs + pltpu.roll(pairs, ext_y - 1, 1))
    pairs = perm + pltpu.roll(perm, ext_x - 1, 0)
    coarse_perm = 0.25 * even_rows(pairs + pltpu.roll(pairs, ext_y - 1, 1))
    coarse_links, coarse_diagonal = couplings(coarse_perm, (1, 2))
    coarse_inverse = 1.0 / jnp.where(coarse_perm > 0.0, coarse_diagonal, 1.0)
    first = (DAMPING * coarse_rhs) * coarse_inverse
    correction = first + (
        DAMPING * (coarse_rhs - operator(coarse_links, coarse_diagonal, first, (1, 2)))
    ) * coarse_inverse
    own = correction[: rows // 2, :cols]
    pick = (
        lax.broadcasted_iota(jnp.int32, (cols, cols // 2), 0)
        == 2 * lax.broadcasted_iota(jnp.int32, (cols, cols // 2), 1)
    ).astype(jnp.float32)
    corr_ref[0] = jnp.dot(own, pick, precision=HI, preferred_element_type=jnp.float32)
    for k in range(cols // 128):
        piece = own[:, k * 128 : (k + 1) * 128]
        wide[k, pl.ds(0, rows // 2, stride=2), :] = piece
        wide[k, pl.ds(1, rows // 2, stride=2), :] = piece
    spread = jnp.concatenate([wide[k] for k in range(cols // 128)], axis=1)
    odd_col = (lax.broadcasted_iota(jnp.int32, (rows, cols), 1) & 1) == 1
    spread = jnp.where(odd_col, pltpu.roll(spread, 1, 1), spread)
    sol_ref[0] = current[:rows, :cols] + spread


def shards(source, sample_seeds, perm_levels, perm_classes):
    h = HALO
    count, rows, cols = source.shape
    ext_x, ext_y = rows + 2 * h, cols + LANE_PAD
    rows_halo, high, low = halo_pieces(source, (perm_classes + 1).astype(jnp.float32), h)
    smem = pl.BlockSpec(memory_space=pltpu.MemorySpace.SMEM)
    whole = lambda shape: pl.BlockSpec(shape, lambda s: (0,) * len(shape))
    solution_block, correction_block = pl.pallas_call(
        smooth_kernel,
        grid=(count,),
        in_specs=[
            smem,
            smem,
            pl.BlockSpec((1, rows, cols), lambda s: (s, 0, 0)),
            whole((rows, cols)),
            pl.BlockSpec((1, 2 * h, cols), lambda s: (s, 0, 0)),
            pl.BlockSpec((1, 2 * h, cols), lambda s: (count, 0, 0)),
            whole((ext_x, LANE_PAD)),
            whole((ext_x, LANE_PAD)),
        ],
        out_specs=[
            pl.BlockSpec((1, rows, cols), lambda s: (s, 0, 0)),
            pl.BlockSpec((1, rows // 2, cols // 2), lambda s: (s, 0, 0)),
        ],
        out_shape=[
            jax.ShapeDtypeStruct((count, rows, cols), jnp.float32),
            jax.ShapeDtypeStruct((count, rows // 2, cols // 2), jnp.float32),
        ],
        scratch_shapes=[
            pltpu.VMEM((ext_x, ext_y), jnp.float32),
            pltpu.VMEM((ext_x, ext_y), jnp.int32),
            pltpu.VMEM((ext_y // 128, ext_x, 128), jnp.float32),
            pltpu.VMEM((cols // 128, rows, 128), jnp.float32),
        ],
        compiler_params=pltpu.CompilerParams(dimension_semantics=("arbitrary",)),
    )(sample_seeds, perm_levels, source, perm_classes, rows_halo, rows_halo, high, low)
    return solution_block, correction_block


def solution(mesh):
    placed = (P("sa", "gx", "gy"), P("sa"), P("sa", None), P("gx", "gy"))
    return jax.shard_map(
        shards,
        mesh=mesh,
        in_specs=placed,
        out_specs=(P("sa", "gx", "gy"), P("sa", "gx", "gy")),
        check_vma=False,
    )
```

```python
import jax
import jax.numpy as jnp
from jax import lax
from jax.experimental import pallas as pl
from jax.experimental.pallas import tpu as pltpu
from jax.sharding import PartitionSpec as P

SWEEPS = 4
DAMPING = 0.8
HALO = 8
LANE_PAD = 128
HI = lax.Precision.HIGHEST
PER_STEP = 2


def halo_pieces(source, classes, width):
    stack = lambda a, b: jnp.concatenate([a, (b + 1).astype(a.dtype)[None]], axis=0)
    low = lax.ppermute(
        stack(source[:, -width:, :], classes[-width:, :]), "gx",
        [(i, i + 1) for i in range(lax.axis_size("gx") - 1)],
    )
    high = lax.ppermute(
        stack(source[:, :width, :], classes[:width, :]), "gx",
        [(i + 1, i) for i in range(lax.axis_size("gx") - 1)],
    )
    rows_halo = jnp.concatenate([high, low], axis=1)

    def packed(strip, halo_strip):
        planes = jnp.concatenate([strip, halo_strip], axis=1)
        count, rows, _ = planes.shape
        flat = jnp.transpose(planes, (1, 0, 2)).reshape(rows, count * width)
        return jnp.pad(flat, ((0, 0), (0, LANE_PAD - count * width)))

    last = packed(stack(source[:, :, -width:], classes[:, -width:]), rows_halo[:, :, -width:])
    first = packed(stack(source[:, :, :width], classes[:, :width]), rows_halo[:, :, :width])
    low = lax.ppermute(last, "gy", [(i, i + 1) for i in range(lax.axis_size("gy") - 1)])
    high = lax.ppermute(first, "gy", [(i + 1, i) for i in range(lax.axis_size("gy") - 1)])
    return rows_halo, high, low


def rolled(v, step):
    rows, cols = v.shape
    down, across = step
    return (
        pltpu.roll(v, rows - down, 0),
        pltpu.roll(v, down, 0),
        pltpu.roll(v, cols - across, 1),
        pltpu.roll(v, across, 1),
    )


def couplings(perm, step):
    down, up, right, left = rolled(perm, step)
    twice = 2.0 * perm
    south = twice * down / (perm + down)
    east = twice * right / (perm + right)
    linkage = (
        jnp.where(down > 0.0, south, twice),
        jnp.where(up > 0.0, pltpu.roll(south, step[0], 0), twice),
        jnp.where(right > 0.0, east, twice),
        jnp.where(left > 0.0, pltpu.roll(east, step[1], 1), twice),
    )
    diagonal = linkage[0] + linkage[1] + linkage[2] + linkage[3]
    return linkage, diagonal


def operator(linkage, diagonal, current, step):
    beside_all = rolled(current, step)
    return diagonal * current - (
        linkage[0] * beside_all[0]
        + linkage[1] * beside_all[1]
        + linkage[2] * beside_all[2]
        + linkage[3] * beside_all[3]
    )


def lane_tile(high_ref, low_ref, plane):
    high = high_ref[...]
    low = low_ref[...]
    lane = lax.broadcasted_iota(jnp.int32, high.shape, 1)
    after = pltpu.roll(high, (LANE_PAD - HALO * plane) % LANE_PAD, 1)
    before = pltpu.roll(low, (LANE_PAD - HALO - HALO * plane) % LANE_PAD, 1)
    return jnp.where(lane < HALO, after, jnp.where(lane >= LANE_PAD - HALO, before, 0.0))


def smooth_kernel(
    seeds_ref, levels_ref, src_ref, cls_ref, rows_ref, crows_ref, high_ref, low_ref,
    sol_ref, corr_ref, source_ext, codes_ext, spare, wide,
):
    s = pl.program_id(0)
    count = PER_STEP * pl.num_programs(0)
    rows, cols = sol_ref.shape[1], sol_ref.shape[2]
    ext_x, ext_y = source_ext.shape

    @pl.when(s == 0)
    def _():
        codes_ext[:rows, :cols] = cls_ref[...] + 1
        codes_ext[rows:, :cols] = crows_ref[0].astype(jnp.int32)
        codes_ext[:, cols:] = lane_tile(high_ref, low_ref, count).astype(jnp.int32)

    for j in range(PER_STEP):
        one_sample(
            PER_STEP * s + j, j, seeds_ref, levels_ref, src_ref, rows_ref, high_ref, low_ref,
            sol_ref, corr_ref, source_ext, codes_ext, spare, wide,
        )


def one_sample(
    plane, j, seeds_ref, levels_ref, src_ref, rows_ref, high_ref, low_ref,
    sol_ref, corr_ref, source_ext, codes_ext, spare, wide,
):
    rows, cols = sol_ref.shape[1], sol_ref.shape[2]
    ext_x, ext_y = source_ext.shape
    source_ext[:rows, :cols] = src_ref[j]
    source_ext[rows:, :cols] = rows_ref[j]
    source_ext[:, cols:] = lane_tile(high_ref, low_ref, plane)
    source = source_ext[...]
    codes = codes_ext[...]
    valid = codes > 0
    classes = codes - 1
    seed = seeds_ref[plane]
    level = [levels_ref[seed, category] for category in range(levels_ref.shape[1])]
    bit0 = (classes & 1) != 0
    bit1 = (classes & 2) != 0
    bit2 = (classes & 4) != 0
    low = jnp.where(bit1, jnp.where(bit0, level[3], level[2]), jnp.where(bit0, level[1], level[0]))
    high = jnp.where(bit1, jnp.where(bit0, level[7], level[6]), jnp.where(bit0, level[5], level[4]))
    perm = jnp.where(valid, jnp.where(bit2, high, low), 0.0)
    linkage, diagonal = couplings(perm, (1, 1))
    inverse = 1.0 / jnp.where(valid, diagonal, 1.0)
    current = (DAMPING * source) * inverse
    for sweep_index in range(SWEEPS):
        residual = source - operator(linkage, diagonal, current, (1, 1))
        if sweep_index + 1 < SWEEPS:
            current = current + (DAMPING * residual) * inverse

    def even_rows(v):
        pieces = []
        for k in range(ext_y // 128):
            spare[k] = v[:, k * 128 : (k + 1) * 128]
            pieces.append(spare[k, pl.ds(0, ext_x // 2, stride=2), :])
        return jnp.concatenate(pieces, axis=1)

    pairs = residual + pltpu.roll(residual, ext_x - 1, 0)
    coarse_rhs = even_rows(pairs + pltpu.roll(pairs, ext_y - 1, 1))
    pairs = perm + pltpu.roll(perm, ext_x - 1, 0)
    coarse_perm = 0.25 * even_rows(pairs + pltpu.roll(pairs, ext_y - 1, 1))
    coarse_links, coarse_diagonal = couplings(coarse_perm, (1, 2))
    coarse_inverse = 1.0 / jnp.where(coarse_perm > 0.0, coarse_diagonal, 1.0)
    first = (DAMPING * coarse_rhs) * coarse_inverse
    correction = first + (
        DAMPING * (coarse_rhs - operator(coarse_links, coarse_diagonal, first, (1, 2)))
    ) * coarse_inverse
    own = correction[: rows // 2, :cols]
    pick = (
        lax.broadcasted_iota(jnp.int32, (cols, cols // 2), 0)
        == 2 * lax.broadcasted_iota(jnp.int32, (cols, cols // 2), 1)
    ).astype(jnp.float32)
    corr_ref[j] = jnp.dot(own, pick, precision=HI, preferred_element_type=jnp.float32)
    for k in range(cols // 128):
        piece = own[:, k * 128 : (k + 1) * 128]
        wide[k, pl.ds(0, rows // 2, stride=2), :] = piece
        wide[k, pl.ds(1, rows // 2, stride=2), :] = piece
    spread = jnp.concatenate([wide[k] for k in range(cols // 128)], axis=1)
    odd_col = (lax.broadcasted_iota(jnp.int32, (rows, cols), 1) & 1) == 1
    spread = jnp.where(odd_col, pltpu.roll(spread, 1, 1), spread)
    sol_ref[j] = current[:rows, :cols] + spread


def shards(source, sample_seeds, perm_levels, perm_classes):
    h = HALO
    count, rows, cols = source.shape
    ext_x, ext_y = rows + 2 * h, cols + LANE_PAD
    rows_halo, high, low = halo_pieces(source, perm_classes, h)
    smem = pl.BlockSpec(memory_space=pltpu.MemorySpace.SMEM)
    whole = lambda shape: pl.BlockSpec(shape, lambda s: (0,) * len(shape))
    solution_block, correction_block = pl.pallas_call(
        smooth_kernel,
        grid=(count // PER_STEP,),
        in_specs=[
            smem,
            smem,
            pl.BlockSpec((PER_STEP, rows, cols), lambda s: (s, 0, 0)),
            whole((rows, cols)),
            pl.BlockSpec((PER_STEP, 2 * h, cols), lambda s: (s, 0, 0)),
            pl.BlockSpec((1, 2 * h, cols), lambda s: (count, 0, 0)),
            whole((ext_x, LANE_PAD)),
            whole((ext_x, LANE_PAD)),
        ],
        out_specs=[
            pl.BlockSpec((PER_STEP, rows, cols), lambda s: (s, 0, 0)),
            pl.BlockSpec((PER_STEP, rows // 2, cols // 2), lambda s: (s, 0, 0)),
        ],
        out_shape=[
            jax.ShapeDtypeStruct((count, rows, cols), jnp.float32),
            jax.ShapeDtypeStruct((count, rows // 2, cols // 2), jnp.float32),
        ],
        scratch_shapes=[
            pltpu.VMEM((ext_x, ext_y), jnp.float32),
            pltpu.VMEM((ext_x, ext_y), jnp.int32),
            pltpu.VMEM((ext_y // 128, ext_x, 128), jnp.float32),
            pltpu.VMEM((cols // 128, rows, 128), jnp.float32),
        ],
        compiler_params=pltpu.CompilerParams(dimension_semantics=("arbitrary",)),
    )(sample_seeds, perm_levels, source, perm_classes, rows_halo, rows_halo, high, low)
    return solution_block, correction_block


def solution(mesh):
    placed = (P("sa", "gx", "gy"), P("sa"), P("sa", None), P("gx", "gy"))
    return jax.shard_map(
        shards,
        mesh=mesh,
        in_specs=placed,
        out_specs=(P("sa", "gx", "gy"), P("sa", "gx", "gy")),
        check_vma=False,
    )
```

```python
import jax
import jax.numpy as jnp
from jax import lax
from jax.experimental import pallas as pl
from jax.experimental.pallas import tpu as pltpu
from jax.sharding import PartitionSpec as P

SWEEPS = 4
DAMPING = 0.8
HALO = 8
LANE_PAD = 128
HI = lax.Precision.HIGHEST
PER_STEP = 2


def halo_pieces(source, classes, width):
    stack = lambda a, b: jnp.concatenate([a, (b + 1).astype(a.dtype)[None]], axis=0)
    low = lax.ppermute(
        stack(source[:, -width:, :], classes[-width:, :]), "gx",
        [(i, i + 1) for i in range(lax.axis_size("gx") - 1)],
    )
    high = lax.ppermute(
        stack(source[:, :width, :], classes[:width, :]), "gx",
        [(i + 1, i) for i in range(lax.axis_size("gx") - 1)],
    )
    rows_halo = jnp.concatenate([high, low], axis=1)

    def packed(strip, halo_strip):
        planes = jnp.concatenate([strip, halo_strip], axis=1)
        count, rows, _ = planes.shape
        flat = jnp.transpose(planes, (1, 0, 2)).reshape(rows, count * width)
        return jnp.pad(flat, ((0, 0), (0, LANE_PAD - count * width)))

    last = packed(stack(source[:, :, -width:], classes[:, -width:]), rows_halo[:, :, -width:])
    first = packed(stack(source[:, :, :width], classes[:, :width]), rows_halo[:, :, :width])
    low = lax.ppermute(last, "gy", [(i, i + 1) for i in range(lax.axis_size("gy") - 1)])
    high = lax.ppermute(first, "gy", [(i + 1, i) for i in range(lax.axis_size("gy") - 1)])
    return rows_halo, high, low


def rolled(v, step):
    rows, cols = v.shape
    down, across = step
    return (
        pltpu.roll(v, rows - down, 0),
        pltpu.roll(v, down, 0),
        pltpu.roll(v, cols - across, 1),
        pltpu.roll(v, across, 1),
    )


def couplings(perm, step):
    down, up, right, left = rolled(perm, step)
    twice = 2.0 * perm
    south = twice * down / (perm + down)
    east = twice * right / (perm + right)
    linkage = (
        jnp.where(down > 0.0, south, twice),
        jnp.where(up > 0.0, pltpu.roll(south, step[0], 0), twice),
        jnp.where(right > 0.0, east, twice),
        jnp.where(left > 0.0, pltpu.roll(east, step[1], 1), twice),
    )
    diagonal = linkage[0] + linkage[1] + linkage[2] + linkage[3]
    return linkage, diagonal


def operator(linkage, diagonal, current, step):
    beside_all = rolled(current, step)
    return diagonal * current - (
        linkage[0] * beside_all[0]
        + linkage[1] * beside_all[1]
        + linkage[2] * beside_all[2]
        + linkage[3] * beside_all[3]
    )


def lane_tile(high_ref, low_ref, plane):
    high = high_ref[...]
    low = low_ref[...]
    lane = lax.broadcasted_iota(jnp.int32, high.shape, 1)
    after = pltpu.roll(high, (LANE_PAD - HALO * plane) % LANE_PAD, 1)
    before = pltpu.roll(low, (LANE_PAD - HALO - HALO * plane) % LANE_PAD, 1)
    return jnp.where(lane < HALO, after, jnp.where(lane >= LANE_PAD - HALO, before, 0.0))


def smooth_kernel(
    seeds_ref, levels_ref, src_ref, cls_ref, rows_ref, high_ref, low_ref,
    sol_ref, corr_ref, source_ext, codes_ext, spare, wide,
):
    s = pl.program_id(0)
    count = PER_STEP * pl.num_programs(0)
    rows, cols = sol_ref.shape[1], sol_ref.shape[2]
    ext_x, ext_y = source_ext.shape

    @pl.when(s == 0)
    def _():
        codes_ext[:rows, :cols] = cls_ref[...] + 1
        codes_ext[rows:, :cols] = rows_ref[count].astype(jnp.int32)
        codes_ext[:, cols:] = lane_tile(high_ref, low_ref, count).astype(jnp.int32)

    for j in range(PER_STEP):
        one_sample(
            PER_STEP * s + j, j, seeds_ref, levels_ref, src_ref, rows_ref, high_ref, low_ref,
            sol_ref, corr_ref, source_ext, codes_ext, spare, wide,
        )


def one_sample(
    plane, j, seeds_ref, levels_ref, src_ref, rows_ref, high_ref, low_ref,
    sol_ref, corr_ref, source_ext, codes_ext, spare, wide,
):
    rows, cols = sol_ref.shape[1], sol_ref.shape[2]
    ext_x, ext_y = source_ext.shape
    source_ext[:rows, :cols] = src_ref[j]
    source_ext[rows:, :cols] = rows_ref[plane]
    source_ext[:, cols:] = lane_tile(high_ref, low_ref, plane)
    source = source_ext[...]
    codes = codes_ext[...]
    valid = codes > 0
    classes = codes - 1
    seed = seeds_ref[plane]
    level = [levels_ref[seed, category] for category in range(levels_ref.shape[1])]
    bit0 = (classes & 1) != 0
    bit1 = (classes & 2) != 0
    bit2 = (classes & 4) != 0
    low = jnp.where(bit1, jnp.where(bit0, level[3], level[2]), jnp.where(bit0, level[1], level[0]))
    high = jnp.where(bit1, jnp.where(bit0, level[7], level[6]), jnp.where(bit0, level[5], level[4]))
    perm = jnp.where(valid, jnp.where(bit2, high, low), 0.0)
    linkage, diagonal = couplings(perm, (1, 1))
    inverse = 1.0 / jnp.where(valid, diagonal, 1.0)
    current = (DAMPING * source) * inverse
    for sweep_index in range(SWEEPS):
        residual = source - operator(linkage, diagonal, current, (1, 1))
        if sweep_index + 1 < SWEEPS:
            current = current + (DAMPING * residual) * inverse

    def even_rows(v):
        pieces = []
        for k in range(ext_y // 128):
            spare[k] = v[:, k * 128 : (k + 1) * 128]
            pieces.append(spare[k, pl.ds(0, ext_x // 2, stride=2), :])
        return jnp.concatenate(pieces, axis=1)

    pairs = residual + pltpu.roll(residual, ext_x - 1, 0)
    coarse_rhs = even_rows(pairs + pltpu.roll(pairs, ext_y - 1, 1))
    pairs = perm + pltpu.roll(perm, ext_x - 1, 0)
    coarse_perm = 0.25 * even_rows(pairs + pltpu.roll(pairs, ext_y - 1, 1))
    coarse_links, coarse_diagonal = couplings(coarse_perm, (1, 2))
    coarse_inverse = 1.0 / jnp.where(coarse_perm > 0.0, coarse_diagonal, 1.0)
    first = (DAMPING * coarse_rhs) * coarse_inverse
    correction = first + (
        DAMPING * (coarse_rhs - operator(coarse_links, coarse_diagonal, first, (1, 2)))
    ) * coarse_inverse
    own = correction[: rows // 2, :cols]
    pick = (
        lax.broadcasted_iota(jnp.int32, (cols, cols // 2), 0)
        == 2 * lax.broadcasted_iota(jnp.int32, (cols, cols // 2), 1)
    ).astype(jnp.float32)
    corr_ref[j] = jnp.dot(own, pick, precision=HI, preferred_element_type=jnp.float32)
    for k in range(cols // 128):
        piece = own[:, k * 128 : (k + 1) * 128]
        wide[k, pl.ds(0, rows // 2, stride=2), :] = piece
        wide[k, pl.ds(1, rows // 2, stride=2), :] = piece
    spread = jnp.concatenate([wide[k] for k in range(cols // 128)], axis=1)
    odd_col = (lax.broadcasted_iota(jnp.int32, (rows, cols), 1) & 1) == 1
    spread = jnp.where(odd_col, pltpu.roll(spread, 1, 1), spread)
    sol_ref[j] = current[:rows, :cols] + spread


def shards(source, sample_seeds, perm_levels, perm_classes):
    h = HALO
    count, rows, cols = source.shape
    ext_x, ext_y = rows + 2 * h, cols + LANE_PAD
    rows_halo, high, low = halo_pieces(source, perm_classes, h)
    smem = pl.BlockSpec(memory_space=pltpu.MemorySpace.SMEM)
    vmem = pl.BlockSpec(memory_space=pltpu.MemorySpace.VMEM)
    whole = lambda shape: pl.BlockSpec(shape, lambda s: (0,) * len(shape))
    solution_block, correction_block = pl.pallas_call(
        smooth_kernel,
        grid=(count // PER_STEP,),
        in_specs=[
            smem,
            smem,
            pl.BlockSpec((PER_STEP, rows, cols), lambda s: (s, 0, 0)),
            whole((rows, cols)),
            vmem,
            vmem,
            vmem,
        ],
        out_specs=[
            pl.BlockSpec((PER_STEP, rows, cols), lambda s: (s, 0, 0)),
            pl.BlockSpec((PER_STEP, rows // 2, cols // 2), lambda s: (s, 0, 0)),
        ],
        out_shape=[
            jax.ShapeDtypeStruct((count, rows, cols), jnp.float32),
            jax.ShapeDtypeStruct((count, rows // 2, cols // 2), jnp.float32),
        ],
        scratch_shapes=[
            pltpu.VMEM((ext_x, ext_y), jnp.float32),
            pltpu.VMEM((ext_x, ext_y), jnp.int32),
            pltpu.VMEM((ext_y // 128, ext_x, 128), jnp.float32),
            pltpu.VMEM((cols // 128, rows, 128), jnp.float32),
        ],
        compiler_params=pltpu.CompilerParams(dimension_semantics=("arbitrary",)),
    )(sample_seeds, perm_levels, source, perm_classes, rows_halo, high, low)
    return solution_block, correction_block


def solution(mesh):
    placed = (P("sa", "gx", "gy"), P("sa"), P("sa", None), P("gx", "gy"))
    return jax.shard_map(
        shards,
        mesh=mesh,
        in_specs=placed,
        out_specs=(P("sa", "gx", "gy"), P("sa", "gx", "gy")),
        check_vma=False,
    )
```

```python
import jax
import jax.numpy as jnp
from jax import lax
from jax.experimental import pallas as pl
from jax.experimental.pallas import tpu as pltpu
from jax.sharding import PartitionSpec as P

SWEEPS = 4
DAMPING = 0.8
HALO = 8
LANE_PAD = 128
HI = lax.Precision.HIGHEST
PER_STEP = 4


def halo_pieces(source, classes, width):
    stack = lambda a, b: jnp.concatenate([a, (b + 1).astype(a.dtype)[None]], axis=0)
    low = lax.ppermute(
        stack(source[:, -width:, :], classes[-width:, :]), "gx",
        [(i, i + 1) for i in range(lax.axis_size("gx") - 1)],
    )
    high = lax.ppermute(
        stack(source[:, :width, :], classes[:width, :]), "gx",
        [(i + 1, i) for i in range(lax.axis_size("gx") - 1)],
    )
    rows_halo = jnp.concatenate([high, low], axis=1)

    def packed(strip, halo_strip):
        planes = jnp.concatenate([strip, halo_strip], axis=1)
        count, rows, _ = planes.shape
        flat = jnp.transpose(planes, (1, 0, 2)).reshape(rows, count * width)
        return jnp.pad(flat, ((0, 0), (0, LANE_PAD - count * width)))

    last = packed(stack(source[:, :, -width:], classes[:, -width:]), rows_halo[:, :, -width:])
    first = packed(stack(source[:, :, :width], classes[:, :width]), rows_halo[:, :, :width])
    low = lax.ppermute(last, "gy", [(i, i + 1) for i in range(lax.axis_size("gy") - 1)])
    high = lax.ppermute(first, "gy", [(i + 1, i) for i in range(lax.axis_size("gy") - 1)])
    return rows_halo, high, low


def rolled(v, step):
    rows, cols = v.shape
    down, across = step
    return (
        pltpu.roll(v, rows - down, 0),
        pltpu.roll(v, down, 0),
        pltpu.roll(v, cols - across, 1),
        pltpu.roll(v, across, 1),
    )


def couplings(perm, step):
    down, up, right, left = rolled(perm, step)
    twice = 2.0 * perm
    south = twice * down / (perm + down)
    east = twice * right / (perm + right)
    linkage = (
        jnp.where(down > 0.0, south, twice),
        jnp.where(up > 0.0, pltpu.roll(south, step[0], 0), twice),
        jnp.where(right > 0.0, east, twice),
        jnp.where(left > 0.0, pltpu.roll(east, step[1], 1), twice),
    )
    diagonal = linkage[0] + linkage[1] + linkage[2] + linkage[3]
    return linkage, diagonal


def operator(linkage, diagonal, current, step):
    beside_all = rolled(current, step)
    return diagonal * current - (
        linkage[0] * beside_all[0]
        + linkage[1] * beside_all[1]
        + linkage[2] * beside_all[2]
        + linkage[3] * beside_all[3]
    )


def lane_tiles(high_ref, low_ref, plane):
    high = high_ref[...]
    low = low_ref[...]
    lane = lax.broadcasted_iota(jnp.int32, high.shape, 1)
    after = pltpu.roll(high, (LANE_PAD - HALO * plane) % LANE_PAD, 1)
    before = pltpu.roll(low, (LANE_PAD - HALO - HALO * plane) % LANE_PAD, 1)
    zero = jnp.zeros_like(high)
    return jnp.where(lane < HALO, after, zero), jnp.where(lane >= LANE_PAD - HALO, before, zero)


def base_layout(own, halo_rows, after, before, width):
    top = jnp.concatenate([own, halo_rows], axis=0)
    gap = jnp.zeros((top.shape[0], width - top.shape[1] - 2 * LANE_PAD), top.dtype)
    return jnp.concatenate([top, after, gap, before], axis=1)


def smooth_kernel(
    seeds_ref, levels_ref, src_ref, cls_ref, rows_ref, high_ref, low_ref,
    sol_ref, corr_ref, codes_pk, spare, wide,
):
    s = pl.program_id(0)
    count = PER_STEP * pl.num_programs(0)
    rows, cols = sol_ref.shape[1], sol_ref.shape[2]
    ext_x, width = codes_pk.shape
    span = cols + 2 * HALO
    lane = lax.broadcasted_iota(jnp.int32, (ext_x, width), 1)

    def packed(pieces):
        out = None
        for j, piece in enumerate(pieces):
            moved = pltpu.roll(piece, (j * span + HALO) % width, 1)
            out = moved if out is None else jnp.where(lane >= j * span, moved, out)
        return out

    @pl.when(s == 0)
    def _():
        after, before = lane_tiles(high_ref, low_ref, count)
        own = base_layout(
            cls_ref[...] + 1, rows_ref[count].astype(jnp.int32),
            after.astype(jnp.int32), before.astype(jnp.int32), width,
        )
        codes_pk[...] = packed([own] * PER_STEP)

    pieces = []
    for j in range(PER_STEP):
        plane = PER_STEP * s + j
        after, before = lane_tiles(high_ref, low_ref, plane)
        pieces.append(base_layout(src_ref[j], rows_ref[plane], after, before, width))
    source = packed(pieces)
    codes = codes_pk[...]
    valid = codes > 0
    classes = (codes - 1).reshape(ext_x // 8, 8, width)
    row_lane = lax.broadcasted_iota(jnp.int32, (8, width), 1)
    level = []
    for category in range(levels_ref.shape[1]):
        row = jnp.full((8, width), levels_ref[seeds_ref[PER_STEP * s], category], jnp.float32)
        for j in range(1, PER_STEP):
            pick_level = levels_ref[seeds_ref[PER_STEP * s + j], category]
            row = jnp.where(row_lane >= j * span, pick_level, row)
        level.append(row[None])
    bit0 = (classes & 1) != 0
    bit1 = (classes & 2) != 0
    bit2 = (classes & 4) != 0
    low = jnp.where(bit1, jnp.where(bit0, level[3], level[2]), jnp.where(bit0, level[1], level[0]))
    high = jnp.where(bit1, jnp.where(bit0, level[7], level[6]), jnp.where(bit0, level[5], level[4]))
    perm = jnp.where(valid, jnp.where(bit2, high, low).reshape(ext_x, width), 0.0)
    linkage, diagonal = couplings(perm, (1, 1))
    inverse = 1.0 / jnp.where(valid, diagonal, 1.0)
    current = (DAMPING * source) * inverse
    for sweep_index in range(SWEEPS):
        residual = source - operator(linkage, diagonal, current, (1, 1))
        if sweep_index + 1 < SWEEPS:
            current = current + (DAMPING * residual) * inverse

    def even_rows(v):
        parts = []
        for k in range(width // 128):
            spare[k] = v[:, k * 128 : (k + 1) * 128]
            parts.append(spare[k, pl.ds(0, ext_x // 2, stride=2), :])
        return jnp.concatenate(parts, axis=1)

    pairs = residual + pltpu.roll(residual, ext_x - 1, 0)
    coarse_rhs = even_rows(pairs + pltpu.roll(pairs, width - 1, 1))
    pairs = perm + pltpu.roll(perm, ext_x - 1, 0)
    coarse_perm = 0.25 * even_rows(pairs + pltpu.roll(pairs, width - 1, 1))
    coarse_links, coarse_diagonal = couplings(coarse_perm, (1, 2))
    coarse_inverse = 1.0 / jnp.where(coarse_perm > 0.0, coarse_diagonal, 1.0)
    first = (DAMPING * coarse_rhs) * coarse_inverse
    correction = first + (
        DAMPING * (coarse_rhs - operator(coarse_links, coarse_diagonal, first, (1, 2)))
    ) * coarse_inverse
    pick = (
        lax.broadcasted_iota(jnp.int32, (cols, cols // 2), 0)
        == 2 * lax.broadcasted_iota(jnp.int32, (cols, cols // 2), 1)
    ).astype(jnp.float32)
    odd_col = (lax.broadcasted_iota(jnp.int32, (rows, cols), 1) & 1) == 1
    for j in range(PER_STEP):
        back = (width - j * span - HALO) % width
        own = pltpu.roll(correction, back, 1)[: rows // 2, :cols]
        corr_ref[j] = jnp.dot(own, pick, precision=HI, preferred_element_type=jnp.float32)
        for k in range(cols // 128):
            piece = own[:, k * 128 : (k + 1) * 128]
            wide[k, pl.ds(0, rows // 2, stride=2), :] = piece
            wide[k, pl.ds(1, rows // 2, stride=2), :] = piece
        spread = jnp.concatenate([wide[k] for k in range(cols // 128)], axis=1)
        spread = jnp.where(odd_col, pltpu.roll(spread, 1, 1), spread)
        sol_ref[j] = pltpu.roll(current, back, 1)[:rows, :cols] + spread


def shards(source, sample_seeds, perm_levels, perm_classes):
    h = HALO
    count, rows, cols = source.shape
    ext_x = rows + 2 * h
    width = -(-(PER_STEP * (cols + 2 * h)) // 128) * 128
    rows_halo, high, low = halo_pieces(source, perm_classes, h)
    smem = pl.BlockSpec(memory_space=pltpu.MemorySpace.SMEM)
    vmem = pl.BlockSpec(memory_space=pltpu.MemorySpace.VMEM)
    whole = lambda shape: pl.BlockSpec(shape, lambda s: (0,) * len(shape))
    solution_block, correction_block = pl.pallas_call(
        smooth_kernel,
        grid=(count // PER_STEP,),
        in_specs=[
            smem,
            smem,
            pl.BlockSpec((PER_STEP, rows, cols), lambda s: (s, 0, 0)),
            whole((rows, cols)),
            vmem,
            vmem,
            vmem,
        ],
        out_specs=[
            pl.BlockSpec((PER_STEP, rows, cols), lambda s: (s, 0, 0)),
            pl.BlockSpec((PER_STEP, rows // 2, cols // 2), lambda s: (s, 0, 0)),
        ],
        out_shape=[
            jax.ShapeDtypeStruct((count, rows, cols), jnp.float32),
            jax.ShapeDtypeStruct((count, rows // 2, cols // 2), jnp.float32),
        ],
        scratch_shapes=[
            pltpu.VMEM((ext_x, width), jnp.int32),
            pltpu.VMEM((width // 128, ext_x, 128), jnp.float32),
            pltpu.VMEM((cols // 128, rows, 128), jnp.float32),
        ],
        compiler_params=pltpu.CompilerParams(dimension_semantics=("arbitrary",)),
    )(sample_seeds, perm_levels, source, perm_classes, rows_halo, high, low)
    return solution_block, correction_block


def solution(mesh):
    placed = (P("sa", "gx", "gy"), P("sa"), P("sa", None), P("gx", "gy"))
    return jax.shard_map(
        shards,
        mesh=mesh,
        in_specs=placed,
        out_specs=(P("sa", "gx", "gy"), P("sa", "gx", "gy")),
        check_vma=False,
    )
```

```python
import jax
import jax.numpy as jnp
from jax import lax
from jax.experimental import pallas as pl
from jax.experimental.pallas import tpu as pltpu
from jax.sharding import PartitionSpec as P

SWEEPS = 4
DAMPING = 0.8
HALO = 8
LANE_PAD = 128
HI = lax.Precision.HIGHEST
PER_STEP = 4


def edge_rows_kernel(bottom_ref, top_ref, cls_bottom_ref, cls_top_ref, low_ref, high_ref):
    count = bottom_ref.shape[0]
    low_ref[:count] = bottom_ref[...]
    low_ref[count] = (cls_bottom_ref[...] + 1).astype(jnp.float32)
    high_ref[:count] = top_ref[...]
    high_ref[count] = (cls_top_ref[...] + 1).astype(jnp.float32)


def edge_rows(source, classes, width):
    count, rows, cols = source.shape
    last = rows // width - 1
    piece = jax.ShapeDtypeStruct((count + 1, width, cols), jnp.float32)
    return pl.pallas_call(
        edge_rows_kernel,
        grid=(1,),
        in_specs=[
            pl.BlockSpec((count, width, cols), lambda i: (0, last, 0)),
            pl.BlockSpec((count, width, cols), lambda i: (0, 0, 0)),
            pl.BlockSpec((width, cols), lambda i: (last, 0)),
            pl.BlockSpec((width, cols), lambda i: (0, 0)),
        ],
        out_specs=[
            pl.BlockSpec((count + 1, width, cols), lambda i: (0, 0, 0)),
            pl.BlockSpec((count + 1, width, cols), lambda i: (0, 0, 0)),
        ],
        out_shape=[piece, piece],
    )(source, source, classes, classes)


def halo_pieces(source, classes, width):
    stack = lambda a, b: jnp.concatenate([a, (b + 1).astype(a.dtype)[None]], axis=0)
    bottom, top = edge_rows(source, classes, width)
    low = lax.ppermute(bottom, "gx", [(i, i + 1) for i in range(lax.axis_size("gx") - 1)])
    high = lax.ppermute(top, "gx", [(i + 1, i) for i in range(lax.axis_size("gx") - 1)])
    rows_halo = jnp.concatenate([high, low], axis=1)

    def packed(strip, halo_strip):
        planes = jnp.concatenate([strip, halo_strip], axis=1)
        count, rows, _ = planes.shape
        flat = jnp.transpose(planes, (1, 0, 2)).reshape(rows, count * width)
        return jnp.pad(flat, ((0, 0), (0, LANE_PAD - count * width)))

    last = packed(stack(source[:, :, -width:], classes[:, -width:]), rows_halo[:, :, -width:])
    first = packed(stack(source[:, :, :width], classes[:, :width]), rows_halo[:, :, :width])
    low = lax.ppermute(last, "gy", [(i, i + 1) for i in range(lax.axis_size("gy") - 1)])
    high = lax.ppermute(first, "gy", [(i + 1, i) for i in range(lax.axis_size("gy") - 1)])
    return rows_halo, high, low


def rolled(v, step):
    rows, cols = v.shape
    down, across = step
    return (
        pltpu.roll(v, rows - down, 0),
        pltpu.roll(v, down, 0),
        pltpu.roll(v, cols - across, 1),
        pltpu.roll(v, across, 1),
    )


def couplings(perm, step):
    down, up, right, left = rolled(perm, step)
    twice = 2.0 * perm
    south = twice * down / (perm + down)
    east = twice * right / (perm + right)
    linkage = (
        jnp.where(down > 0.0, south, twice),
        jnp.where(up > 0.0, pltpu.roll(south, step[0], 0), twice),
        jnp.where(right > 0.0, east, twice),
        jnp.where(left > 0.0, pltpu.roll(east, step[1], 1), twice),
    )
    diagonal = linkage[0] + linkage[1] + linkage[2] + linkage[3]
    return linkage, diagonal


def operator(linkage, diagonal, current, step):
    beside_all = rolled(current, step)
    return diagonal * current - (
        linkage[0] * beside_all[0]
        + linkage[1] * beside_all[1]
        + linkage[2] * beside_all[2]
        + linkage[3] * beside_all[3]
    )


def lane_tiles(high_ref, low_ref, plane):
    high = high_ref[...]
    low = low_ref[...]
    lane = lax.broadcasted_iota(jnp.int32, high.shape, 1)
    after = pltpu.roll(high, (LANE_PAD - HALO * plane) % LANE_PAD, 1)
    before = pltpu.roll(low, (LANE_PAD - HALO - HALO * plane) % LANE_PAD, 1)
    zero = jnp.zeros_like(high)
    return jnp.where(lane < HALO, after, zero), jnp.where(lane >= LANE_PAD - HALO, before, zero)


def base_layout(own, halo_rows, after, before, width):
    top = jnp.concatenate([own, halo_rows], axis=0)
    gap = jnp.zeros((top.shape[0], width - top.shape[1] - 2 * LANE_PAD), top.dtype)
    return jnp.concatenate([top, after, gap, before], axis=1)


def smooth_kernel(
    seeds_ref, levels_ref, src_ref, cls_ref, rows_ref, high_ref, low_ref,
    sol_ref, corr_ref, codes_pk, spare, wide,
):
    s = pl.program_id(0)
    count = PER_STEP * pl.num_programs(0)
    rows, cols = sol_ref.shape[1], sol_ref.shape[2]
    ext_x, width = codes_pk.shape
    span = cols + 2 * HALO
    lane = lax.broadcasted_iota(jnp.int32, (ext_x, width), 1)

    def packed(pieces):
        out = None
        for j, piece in enumerate(pieces):
            moved = pltpu.roll(piece, (j * span + HALO) % width, 1)
            out = moved if out is None else jnp.where(lane >= j * span, moved, out)
        return out

    @pl.when(s == 0)
    def _():
        after, before = lane_tiles(high_ref, low_ref, count)
        own = base_layout(
            cls_ref[...] + 1, rows_ref[count].astype(jnp.int32),
            after.astype(jnp.int32), before.astype(jnp.int32), width,
        )
        codes_pk[...] = packed([own] * PER_STEP)

    pieces = []
    for j in range(PER_STEP):
        plane = PER_STEP * s + j
        after, before = lane_tiles(high_ref, low_ref, plane)
        pieces.append(base_layout(src_ref[j], rows_ref[plane], after, before, width))
    source = packed(pieces)
    codes = codes_pk[...]
    valid = codes > 0
    classes = (codes - 1).reshape(ext_x // 8, 8, width)
    row_lane = lax.broadcasted_iota(jnp.int32, (8, width), 1)
    level = []
    for category in range(levels_ref.shape[1]):
        row = jnp.full((8, width), levels_ref[seeds_ref[PER_STEP * s], category], jnp.float32)
        for j in range(1, PER_STEP):
            pick_level = levels_ref[seeds_ref[PER_STEP * s + j], category]
            row = jnp.where(row_lane >= j * span, pick_level, row)
        level.append(row[None])
    bit0 = (classes & 1) != 0
    bit1 = (classes & 2) != 0
    bit2 = (classes & 4) != 0
    low = jnp.where(bit1, jnp.where(bit0, level[3], level[2]), jnp.where(bit0, level[1], level[0]))
    high = jnp.where(bit1, jnp.where(bit0, level[7], level[6]), jnp.where(bit0, level[5], level[4]))
    perm = jnp.where(valid, jnp.where(bit2, high, low).reshape(ext_x, width), 0.0)
    linkage, diagonal = couplings(perm, (1, 1))
    inverse = 1.0 / jnp.where(valid, diagonal, 1.0)
    current = (DAMPING * source) * inverse
    for sweep_index in range(SWEEPS):
        residual = source - operator(linkage, diagonal, current, (1, 1))
        if sweep_index + 1 < SWEEPS:
            current = current + (DAMPING * residual) * inverse

    def even_rows(v):
        parts = []
        for k in range(width // 128):
            spare[k] = v[:, k * 128 : (k + 1) * 128]
            parts.append(spare[k, pl.ds(0, ext_x // 2, stride=2), :])
        return jnp.concatenate(parts, axis=1)

    pairs = residual + pltpu.roll(residual, ext_x - 1, 0)
    coarse_rhs = even_rows(pairs + pltpu.roll(pairs, width - 1, 1))
    pairs = perm + pltpu.roll(perm, ext_x - 1, 0)
    coarse_perm = 0.25 * even_rows(pairs + pltpu.roll(pairs, width - 1, 1))
    coarse_links, coarse_diagonal = couplings(coarse_perm, (1, 2))
    coarse_inverse = 1.0 / jnp.where(coarse_perm > 0.0, coarse_diagonal, 1.0)
    first = (DAMPING * coarse_rhs) * coarse_inverse
    correction = first + (
        DAMPING * (coarse_rhs - operator(coarse_links, coarse_diagonal, first, (1, 2)))
    ) * coarse_inverse
    pick = (
        lax.broadcasted_iota(jnp.int32, (cols, cols // 2), 0)
        == 2 * lax.broadcasted_iota(jnp.int32, (cols, cols // 2), 1)
    ).astype(jnp.float32)
    odd_col = (lax.broadcasted_iota(jnp.int32, (rows, cols), 1) & 1) == 1
    for j in range(PER_STEP):
        back = (width - j * span - HALO) % width
        own = pltpu.roll(correction, back, 1)[: rows // 2, :cols]
        corr_ref[j] = jnp.dot(own, pick, precision=HI, preferred_element_type=jnp.float32)
        for k in range(cols // 128):
            piece = own[:, k * 128 : (k + 1) * 128]
            wide[k, pl.ds(0, rows // 2, stride=2), :] = piece
            wide[k, pl.ds(1, rows // 2, stride=2), :] = piece
        spread = jnp.concatenate([wide[k] for k in range(cols // 128)], axis=1)
        spread = jnp.where(odd_col, pltpu.roll(spread, 1, 1), spread)
        sol_ref[j] = pltpu.roll(current, back, 1)[:rows, :cols] + spread


def shards(source, sample_seeds, perm_levels, perm_classes):
    h = HALO
    count, rows, cols = source.shape
    ext_x = rows + 2 * h
    width = -(-(PER_STEP * (cols + 2 * h)) // 128) * 128
    rows_halo, high, low = halo_pieces(source, perm_classes, h)
    smem = pl.BlockSpec(memory_space=pltpu.MemorySpace.SMEM)
    vmem = pl.BlockSpec(memory_space=pltpu.MemorySpace.VMEM)
    whole = lambda shape: pl.BlockSpec(shape, lambda s: (0,) * len(shape))
    solution_block, correction_block = pl.pallas_call(
        smooth_kernel,
        grid=(count // PER_STEP,),
        in_specs=[
            smem,
            smem,
            pl.BlockSpec((PER_STEP, rows, cols), lambda s: (s, 0, 0)),
            whole((rows, cols)),
            vmem,
            vmem,
            vmem,
        ],
        out_specs=[
            pl.BlockSpec((PER_STEP, rows, cols), lambda s: (s, 0, 0)),
            pl.BlockSpec((PER_STEP, rows // 2, cols // 2), lambda s: (s, 0, 0)),
        ],
        out_shape=[
            jax.ShapeDtypeStruct((count, rows, cols), jnp.float32),
            jax.ShapeDtypeStruct((count, rows // 2, cols // 2), jnp.float32),
        ],
        scratch_shapes=[
            pltpu.VMEM((ext_x, width), jnp.int32),
            pltpu.VMEM((width // 128, ext_x, 128), jnp.float32),
            pltpu.VMEM((cols // 128, rows, 128), jnp.float32),
        ],
        compiler_params=pltpu.CompilerParams(dimension_semantics=("arbitrary",)),
    )(sample_seeds, perm_levels, source, perm_classes, rows_halo, high, low)
    return solution_block, correction_block


def solution(mesh):
    placed = (P("sa", "gx", "gy"), P("sa"), P("sa", None), P("gx", "gy"))
    return jax.shard_map(
        shards,
        mesh=mesh,
        in_specs=placed,
        out_specs=(P("sa", "gx", "gy"), P("sa", "gx", "gy")),
        check_vma=False,
    )
```

```python
import jax
import jax.numpy as jnp
from jax import lax
from jax.experimental import pallas as pl
from jax.experimental.pallas import tpu as pltpu
from jax.sharding import PartitionSpec as P

SWEEPS = 4
DAMPING = 0.8
HALO = 8
LANE_PAD = 128
HI = lax.Precision.HIGHEST
PER_STEP = 4


def swap_exchange(last, first, axis):
    n = lax.axis_size(axis)
    even = lax.axis_index(axis) % 2 == 0
    inner = [(k, k ^ 1) for k in range(n) if k ^ 1 < n]
    outer = [(k, k + 1) for k in range(1, n - 1, 2)] + [(k + 1, k) for k in range(1, n - 1, 2)]
    one = lax.ppermute(jnp.where(even, last, first), axis, inner)
    two = lax.ppermute(jnp.where(even, first, last), axis, outer)
    return jnp.where(even, two, one), jnp.where(even, one, two)


def halo_pieces(source, classes, width):
    stack = lambda a, b: jnp.concatenate([a, (b + 1).astype(a.dtype)[None]], axis=0)
    low, high = swap_exchange(
        stack(source[:, -width:, :], classes[-width:, :]),
        stack(source[:, :width, :], classes[:width, :]),
        "gx",
    )
    rows_halo = jnp.concatenate([high, low], axis=1)

    def packed(strip, halo_strip):
        planes = jnp.concatenate([strip, halo_strip], axis=1)
        count, rows, _ = planes.shape
        flat = jnp.transpose(planes, (1, 0, 2)).reshape(rows, count * width)
        return jnp.pad(flat, ((0, 0), (0, LANE_PAD - count * width)))

    last = packed(stack(source[:, :, -width:], classes[:, -width:]), rows_halo[:, :, -width:])
    first = packed(stack(source[:, :, :width], classes[:, :width]), rows_halo[:, :, :width])
    low, high = swap_exchange(last, first, "gy")
    return rows_halo, high, low


def rolled(v, step):
    rows, cols = v.shape
    down, across = step
    return (
        pltpu.roll(v, rows - down, 0),
        pltpu.roll(v, down, 0),
        pltpu.roll(v, cols - across, 1),
        pltpu.roll(v, across, 1),
    )


def couplings(perm, step):
    down, up, right, left = rolled(perm, step)
    twice = 2.0 * perm
    south = twice * down / (perm + down)
    east = twice * right / (perm + right)
    linkage = (
        jnp.where(down > 0.0, south, twice),
        jnp.where(up > 0.0, pltpu.roll(south, step[0], 0), twice),
        jnp.where(right > 0.0, east, twice),
        jnp.where(left > 0.0, pltpu.roll(east, step[1], 1), twice),
    )
    diagonal = linkage[0] + linkage[1] + linkage[2] + linkage[3]
    return linkage, diagonal


def operator(linkage, diagonal, current, step):
    beside_all = rolled(current, step)
    return diagonal * current - (
        linkage[0] * beside_all[0]
        + linkage[1] * beside_all[1]
        + linkage[2] * beside_all[2]
        + linkage[3] * beside_all[3]
    )


def lane_tiles(high_ref, low_ref, plane):
    high = high_ref[...]
    low = low_ref[...]
    lane = lax.broadcasted_iota(jnp.int32, high.shape, 1)
    after = pltpu.roll(high, (LANE_PAD - HALO * plane) % LANE_PAD, 1)
    before = pltpu.roll(low, (LANE_PAD - HALO - HALO * plane) % LANE_PAD, 1)
    zero = jnp.zeros_like(high)
    return jnp.where(lane < HALO, after, zero), jnp.where(lane >= LANE_PAD - HALO, before, zero)


def base_layout(own, halo_rows, after, before, width):
    top = jnp.concatenate([own, halo_rows], axis=0)
    gap = jnp.zeros((top.shape[0], width - top.shape[1] - 2 * LANE_PAD), top.dtype)
    return jnp.concatenate([top, after, gap, before], axis=1)


def smooth_kernel(
    seeds_ref, levels_ref, src_ref, cls_ref, rows_ref, high_ref, low_ref,
    sol_ref, corr_ref, codes_pk, spare, wide,
):
    s = pl.program_id(0)
    count = PER_STEP * pl.num_programs(0)
    rows, cols = sol_ref.shape[1], sol_ref.shape[2]
    ext_x, width = codes_pk.shape
    span = cols + 2 * HALO
    lane = lax.broadcasted_iota(jnp.int32, (ext_x, width), 1)

    def packed(pieces):
        out = None
        for j, piece in enumerate(pieces):
            moved = pltpu.roll(piece, (j * span + HALO) % width, 1)
            out = moved if out is None else jnp.where(lane >= j * span, moved, out)
        return out

    @pl.when(s == 0)
    def _():
        after, before = lane_tiles(high_ref, low_ref, count)
        own = base_layout(
            cls_ref[...] + 1, rows_ref[count].astype(jnp.int32),
            after.astype(jnp.int32), before.astype(jnp.int32), width,
        )
        codes_pk[...] = packed([own] * PER_STEP)

    pieces = []
    for j in range(PER_STEP):
        plane = PER_STEP * s + j
        after, before = lane_tiles(high_ref, low_ref, plane)
        pieces.append(base_layout(src_ref[j], rows_ref[plane], after, before, width))
    source = packed(pieces)
    codes = codes_pk[...]
    valid = codes > 0
    classes = (codes - 1).reshape(ext_x // 8, 8, width)
    row_lane = lax.broadcasted_iota(jnp.int32, (8, width), 1)
    level = []
    for category in range(levels_ref.shape[1]):
        row = jnp.full((8, width), levels_ref[seeds_ref[PER_STEP * s], category], jnp.float32)
        for j in range(1, PER_STEP):
            pick_level = levels_ref[seeds_ref[PER_STEP * s + j], category]
            row = jnp.where(row_lane >= j * span, pick_level, row)
        level.append(row[None])
    bit0 = (classes & 1) != 0
    bit1 = (classes & 2) != 0
    bit2 = (classes & 4) != 0
    low = jnp.where(bit1, jnp.where(bit0, level[3], level[2]), jnp.where(bit0, level[1], level[0]))
    high = jnp.where(bit1, jnp.where(bit0, level[7], level[6]), jnp.where(bit0, level[5], level[4]))
    perm = jnp.where(valid, jnp.where(bit2, high, low).reshape(ext_x, width), 0.0)
    linkage, diagonal = couplings(perm, (1, 1))
    inverse = 1.0 / jnp.where(valid, diagonal, 1.0)
    current = (DAMPING * source) * inverse
    for sweep_index in range(SWEEPS):
        residual = source - operator(linkage, diagonal, current, (1, 1))
        if sweep_index + 1 < SWEEPS:
            current = current + (DAMPING * residual) * inverse

    def even_rows(v):
        parts = []
        for k in range(width // 128):
            spare[k] = v[:, k * 128 : (k + 1) * 128]
            parts.append(spare[k, pl.ds(0, ext_x // 2, stride=2), :])
        return jnp.concatenate(parts, axis=1)

    pairs = residual + pltpu.roll(residual, ext_x - 1, 0)
    coarse_rhs = even_rows(pairs + pltpu.roll(pairs, width - 1, 1))
    pairs = perm + pltpu.roll(perm, ext_x - 1, 0)
    coarse_perm = 0.25 * even_rows(pairs + pltpu.roll(pairs, width - 1, 1))
    coarse_links, coarse_diagonal = couplings(coarse_perm, (1, 2))
    coarse_inverse = 1.0 / jnp.where(coarse_perm > 0.0, coarse_diagonal, 1.0)
    first = (DAMPING * coarse_rhs) * coarse_inverse
    correction = first + (
        DAMPING * (coarse_rhs - operator(coarse_links, coarse_diagonal, first, (1, 2)))
    ) * coarse_inverse
    pick = (
        lax.broadcasted_iota(jnp.int32, (cols, cols // 2), 0)
        == 2 * lax.broadcasted_iota(jnp.int32, (cols, cols // 2), 1)
    ).astype(jnp.float32)
    odd_col = (lax.broadcasted_iota(jnp.int32, (rows, cols), 1) & 1) == 1
    for j in range(PER_STEP):
        back = (width - j * span - HALO) % width
        own = pltpu.roll(correction, back, 1)[: rows // 2, :cols]
        corr_ref[j] = jnp.dot(own, pick, precision=HI, preferred_element_type=jnp.float32)
        for k in range(cols // 128):
            piece = own[:, k * 128 : (k + 1) * 128]
            wide[k, pl.ds(0, rows // 2, stride=2), :] = piece
            wide[k, pl.ds(1, rows // 2, stride=2), :] = piece
        spread = jnp.concatenate([wide[k] for k in range(cols // 128)], axis=1)
        spread = jnp.where(odd_col, pltpu.roll(spread, 1, 1), spread)
        sol_ref[j] = pltpu.roll(current, back, 1)[:rows, :cols] + spread


def shards(source, sample_seeds, perm_levels, perm_classes):
    h = HALO
    count, rows, cols = source.shape
    ext_x = rows + 2 * h
    width = -(-(PER_STEP * (cols + 2 * h)) // 128) * 128
    rows_halo, high, low = halo_pieces(source, perm_classes, h)
    smem = pl.BlockSpec(memory_space=pltpu.MemorySpace.SMEM)
    vmem = pl.BlockSpec(memory_space=pltpu.MemorySpace.VMEM)
    whole = lambda shape: pl.BlockSpec(shape, lambda s: (0,) * len(shape))
    solution_block, correction_block = pl.pallas_call(
        smooth_kernel,
        grid=(count // PER_STEP,),
        in_specs=[
            smem,
            smem,
            pl.BlockSpec((PER_STEP, rows, cols), lambda s: (s, 0, 0)),
            whole((rows, cols)),
            vmem,
            vmem,
            vmem,
        ],
        out_specs=[
            pl.BlockSpec((PER_STEP, rows, cols), lambda s: (s, 0, 0)),
            pl.BlockSpec((PER_STEP, rows // 2, cols // 2), lambda s: (s, 0, 0)),
        ],
        out_shape=[
            jax.ShapeDtypeStruct((count, rows, cols), jnp.float32),
            jax.ShapeDtypeStruct((count, rows // 2, cols // 2), jnp.float32),
        ],
        scratch_shapes=[
            pltpu.VMEM((ext_x, width), jnp.int32),
            pltpu.VMEM((width // 128, ext_x, 128), jnp.float32),
            pltpu.VMEM((cols // 128, rows, 128), jnp.float32),
        ],
        compiler_params=pltpu.CompilerParams(dimension_semantics=("arbitrary",)),
    )(sample_seeds, perm_levels, source, perm_classes, rows_halo, high, low)
    return solution_block, correction_block


def solution(mesh):
    placed = (P("sa", "gx", "gy"), P("sa"), P("sa", None), P("gx", "gy"))
    return jax.shard_map(
        shards,
        mesh=mesh,
        in_specs=placed,
        out_specs=(P("sa", "gx", "gy"), P("sa", "gx", "gy")),
        check_vma=False,
    )
```

```python
import jax
import jax.numpy as jnp
from jax import lax
from jax.experimental import pallas as pl
from jax.experimental.pallas import tpu as pltpu
from jax.sharding import PartitionSpec as P

SWEEPS = 4
DAMPING = 0.8
HALO = 8
LANE_PAD = 128
HI = lax.Precision.HIGHEST
PER_STEP = 4


def swap_exchange(last, first, axis):
    n = lax.axis_size(axis)
    even = lax.axis_index(axis) % 2 == 0
    inner = [(k, k ^ 1) for k in range(n) if k ^ 1 < n]
    outer = [(k, k + 1) for k in range(1, n - 1, 2)] + [(k + 1, k) for k in range(1, n - 1, 2)]
    one = lax.ppermute(jnp.where(even, last, first), axis, inner)
    two = lax.ppermute(jnp.where(even, first, last), axis, outer)
    return one, two, even


def halo_pieces(source, classes, width):
    stack = lambda a, b: jnp.concatenate([a, (b + 1).astype(a.dtype)[None]], axis=0)
    one_x, two_x, even_x = swap_exchange(
        stack(source[:, -width:, :], classes[-width:, :]),
        stack(source[:, :width, :], classes[:width, :]),
        "gx",
    )
    rows_halo = jnp.where(
        even_x, jnp.concatenate([one_x, two_x], axis=1), jnp.concatenate([two_x, one_x], axis=1)
    )

    def packed(strip, halo_strip):
        planes = jnp.concatenate([strip, halo_strip], axis=1)
        count, rows, _ = planes.shape
        flat = jnp.transpose(planes, (1, 0, 2)).reshape(rows, count * width)
        return jnp.pad(flat, ((0, 0), (0, LANE_PAD - count * width)))

    last = packed(stack(source[:, :, -width:], classes[:, -width:]), rows_halo[:, :, -width:])
    first = packed(stack(source[:, :, :width], classes[:, :width]), rows_halo[:, :, :width])
    one_y, two_y, even_y = swap_exchange(last, first, "gy")
    parity = jnp.stack([even_x, even_y]).astype(jnp.int32)
    return one_x, two_x, one_y, two_y, parity


def rolled(v, step):
    rows, cols = v.shape
    down, across = step
    return (
        pltpu.roll(v, rows - down, 0),
        pltpu.roll(v, down, 0),
        pltpu.roll(v, cols - across, 1),
        pltpu.roll(v, across, 1),
    )


def couplings(perm, step):
    down, up, right, left = rolled(perm, step)
    twice = 2.0 * perm
    south = twice * down / (perm + down)
    east = twice * right / (perm + right)
    linkage = (
        jnp.where(down > 0.0, south, twice),
        jnp.where(up > 0.0, pltpu.roll(south, step[0], 0), twice),
        jnp.where(right > 0.0, east, twice),
        jnp.where(left > 0.0, pltpu.roll(east, step[1], 1), twice),
    )
    diagonal = linkage[0] + linkage[1] + linkage[2] + linkage[3]
    return linkage, diagonal


def operator(linkage, diagonal, current, step):
    beside_all = rolled(current, step)
    return diagonal * current - (
        linkage[0] * beside_all[0]
        + linkage[1] * beside_all[1]
        + linkage[2] * beside_all[2]
        + linkage[3] * beside_all[3]
    )


def lane_tiles(high, low, plane):
    lane = lax.broadcasted_iota(jnp.int32, high.shape, 1)
    after = pltpu.roll(high, (LANE_PAD - HALO * plane) % LANE_PAD, 1)
    before = pltpu.roll(low, (LANE_PAD - HALO - HALO * plane) % LANE_PAD, 1)
    zero = jnp.zeros_like(high)
    return jnp.where(lane < HALO, after, zero), jnp.where(lane >= LANE_PAD - HALO, before, zero)


def base_layout(own, halo_rows, after, before, width):
    top = jnp.concatenate([own, halo_rows], axis=0)
    gap = jnp.zeros((top.shape[0], width - top.shape[1] - 2 * LANE_PAD), top.dtype)
    return jnp.concatenate([top, after, gap, before], axis=1)


def smooth_kernel(
    seeds_ref, levels_ref, parity_ref, src_ref, cls_ref, one_x, two_x, one_y, two_y,
    sol_ref, corr_ref, codes_pk, spare, wide,
):
    s = pl.program_id(0)
    count = PER_STEP * pl.num_programs(0)
    rows, cols = sol_ref.shape[1], sol_ref.shape[2]
    ext_x, width = codes_pk.shape
    span = cols + 2 * HALO
    lane = lax.broadcasted_iota(jnp.int32, (ext_x, width), 1)
    even_x = parity_ref[0] == 1
    even_y = parity_ref[1] == 1
    high_y = jnp.where(even_y, one_y[...], two_y[...])
    low_y = jnp.where(even_y, two_y[...], one_y[...])

    def halo_rows(plane):
        after = jnp.where(even_x, one_x[plane], two_x[plane])
        before = jnp.where(even_x, two_x[plane], one_x[plane])
        return jnp.concatenate([after, before], axis=0)

    def packed(pieces):
        out = None
        for j, piece in enumerate(pieces):
            moved = pltpu.roll(piece, (j * span + HALO) % width, 1)
            out = moved if out is None else jnp.where(lane >= j * span, moved, out)
        return out

    @pl.when(s == 0)
    def _():
        after, before = lane_tiles(high_y, low_y, count)
        own = base_layout(
            cls_ref[...] + 1, halo_rows(count).astype(jnp.int32),
            after.astype(jnp.int32), before.astype(jnp.int32), width,
        )
        codes_pk[...] = packed([own] * PER_STEP)

    pieces = []
    for j in range(PER_STEP):
        plane = PER_STEP * s + j
        after, before = lane_tiles(high_y, low_y, plane)
        pieces.append(base_layout(src_ref[j], halo_rows(plane), after, before, width))
    source = packed(pieces)
    codes = codes_pk[...]
    valid = codes > 0
    classes = (codes - 1).reshape(ext_x // 8, 8, width)
    row_lane = lax.broadcasted_iota(jnp.int32, (8, width), 1)
    level = []
    for category in range(levels_ref.shape[1]):
        row = jnp.full((8, width), levels_ref[seeds_ref[PER_STEP * s], category], jnp.float32)
        for j in range(1, PER_STEP):
            pick_level = levels_ref[seeds_ref[PER_STEP * s + j], category]
            row = jnp.where(row_lane >= j * span, pick_level, row)
        level.append(row[None])
    bit0 = (classes & 1) != 0
    bit1 = (classes & 2) != 0
    bit2 = (classes & 4) != 0
    low = jnp.where(bit1, jnp.where(bit0, level[3], level[2]), jnp.where(bit0, level[1], level[0]))
    high = jnp.where(bit1, jnp.where(bit0, level[7], level[6]), jnp.where(bit0, level[5], level[4]))
    perm = jnp.where(valid, jnp.where(bit2, high, low).reshape(ext_x, width), 0.0)
    linkage, diagonal = couplings(perm, (1, 1))
    inverse = 1.0 / jnp.where(valid, diagonal, 1.0)
    current = (DAMPING * source) * inverse
    for sweep_index in range(SWEEPS):
        residual = source - operator(linkage, diagonal, current, (1, 1))
        if sweep_index + 1 < SWEEPS:
            current = current + (DAMPING * residual) * inverse

    def even_rows(v):
        parts = []
        for k in range(width // 128):
            spare[k] = v[:, k * 128 : (k + 1) * 128]
            parts.append(spare[k, pl.ds(0, ext_x // 2, stride=2), :])
        return jnp.concatenate(parts, axis=1)

    pairs = residual + pltpu.roll(residual, ext_x - 1, 0)
    coarse_rhs = even_rows(pairs + pltpu.roll(pairs, width - 1, 1))
    pairs = perm + pltpu.roll(perm, ext_x - 1, 0)
    coarse_perm = 0.25 * even_rows(pairs + pltpu.roll(pairs, width - 1, 1))
    coarse_links, coarse_diagonal = couplings(coarse_perm, (1, 2))
    coarse_inverse = 1.0 / jnp.where(coarse_perm > 0.0, coarse_diagonal, 1.0)
    first = (DAMPING * coarse_rhs) * coarse_inverse
    correction = first + (
        DAMPING * (coarse_rhs - operator(coarse_links, coarse_diagonal, first, (1, 2)))
    ) * coarse_inverse
    pick = (
        lax.broadcasted_iota(jnp.int32, (cols, cols // 2), 0)
        == 2 * lax.broadcasted_iota(jnp.int32, (cols, cols // 2), 1)
    ).astype(jnp.float32)
    odd_col = (lax.broadcasted_iota(jnp.int32, (rows, cols), 1) & 1) == 1
    for j in range(PER_STEP):
        back = (width - j * span - HALO) % width
        own = pltpu.roll(correction, back, 1)[: rows // 2, :cols]
        corr_ref[j] = jnp.dot(own, pick, precision=HI, preferred_element_type=jnp.float32)
        for k in range(cols // 128):
            piece = own[:, k * 128 : (k + 1) * 128]
            wide[k, pl.ds(0, rows // 2, stride=2), :] = piece
            wide[k, pl.ds(1, rows // 2, stride=2), :] = piece
        spread = jnp.concatenate([wide[k] for k in range(cols // 128)], axis=1)
        spread = jnp.where(odd_col, pltpu.roll(spread, 1, 1), spread)
        sol_ref[j] = pltpu.roll(current, back, 1)[:rows, :cols] + spread


def shards(source, sample_seeds, perm_levels, perm_classes):
    h = HALO
    count, rows, cols = source.shape
    ext_x = rows + 2 * h
    width = -(-(PER_STEP * (cols + 2 * h)) // 128) * 128
    one_x, two_x, one_y, two_y, parity = halo_pieces(source, perm_classes, h)
    smem = pl.BlockSpec(memory_space=pltpu.MemorySpace.SMEM)
    vmem = pl.BlockSpec(memory_space=pltpu.MemorySpace.VMEM)
    whole = lambda shape: pl.BlockSpec(shape, lambda s: (0,) * len(shape))
    solution_block, correction_block = pl.pallas_call(
        smooth_kernel,
        grid=(count // PER_STEP,),
        in_specs=[
            smem,
            smem,
            smem,
            pl.BlockSpec((PER_STEP, rows, cols), lambda s: (s, 0, 0)),
            whole((rows, cols)),
            vmem,
            vmem,
            vmem,
            vmem,
        ],
        out_specs=[
            pl.BlockSpec((PER_STEP, rows, cols), lambda s: (s, 0, 0)),
            pl.BlockSpec((PER_STEP, rows // 2, cols // 2), lambda s: (s, 0, 0)),
        ],
        out_shape=[
            jax.ShapeDtypeStruct((count, rows, cols), jnp.float32),
            jax.ShapeDtypeStruct((count, rows // 2, cols // 2), jnp.float32),
        ],
        scratch_shapes=[
            pltpu.VMEM((ext_x, width), jnp.int32),
            pltpu.VMEM((width // 128, ext_x, 128), jnp.float32),
            pltpu.VMEM((cols // 128, rows, 128), jnp.float32),
        ],
        compiler_params=pltpu.CompilerParams(dimension_semantics=("arbitrary",)),
    )(sample_seeds, perm_levels, parity, source, perm_classes, one_x, two_x, one_y, two_y)
    return solution_block, correction_block


def solution(mesh):
    placed = (P("sa", "gx", "gy"), P("sa"), P("sa", None), P("gx", "gy"))
    return jax.shard_map(
        shards,
        mesh=mesh,
        in_specs=placed,
        out_specs=(P("sa", "gx", "gy"), P("sa", "gx", "gy")),
        check_vma=False,
    )
```

```python
import jax
import jax.numpy as jnp
from jax import lax
from jax.experimental import pallas as pl
from jax.experimental.pallas import tpu as pltpu
from jax.sharding import PartitionSpec as P

SWEEPS = 4
DAMPING = 0.8
HALO = 8
LANE_PAD = 128
HI = lax.Precision.HIGHEST
PER_STEP = 4


def swap_exchange(last, first, axis):
    n = lax.axis_size(axis)
    even = lax.axis_index(axis) % 2 == 0
    inner = [(k, k ^ 1) for k in range(n) if k ^ 1 < n]
    outer = [(k, k + 1) for k in range(1, n - 1, 2)] + [(k + 1, k) for k in range(1, n - 1, 2)]
    one = lax.ppermute(jnp.where(even, last, first), axis, inner)
    two = lax.ppermute(jnp.where(even, first, last), axis, outer)
    return one, two, even


def halo_pieces(source, classes, width):
    count, rows, cols = source.shape
    stack = lambda a, b: jnp.concatenate([a, (b + 1).astype(a.dtype)[None]], axis=0)

    def packed(planes):
        flat = jnp.transpose(planes, (1, 0, 2)).reshape(rows, (count + 1) * width)
        return jnp.pad(flat, ((0, 0), (0, LANE_PAD - (count + 1) * width)))

    one_y, two_y, even_y = swap_exchange(
        packed(stack(source[:, :, -width:], classes[:, -width:])),
        packed(stack(source[:, :, :width], classes[:, :width])),
        "gy",
    )
    high = jnp.where(even_y, one_y, two_y)
    low = jnp.where(even_y, two_y, one_y)

    def with_corners(planes, edge):
        corner = jnp.concatenate([high[edge], low[edge]], axis=1)
        corner = jnp.pad(corner, ((0, 0), (0, cols - 2 * LANE_PAD)))
        return jnp.concatenate([planes, corner[None]], axis=0)

    one_x, two_x, even_x = swap_exchange(
        with_corners(stack(source[:, -width:, :], classes[-width:, :]), slice(rows - width, rows)),
        with_corners(stack(source[:, :width, :], classes[:width, :]), slice(0, width)),
        "gx",
    )
    rows_halo = jnp.where(
        even_x, jnp.concatenate([one_x, two_x], axis=1), jnp.concatenate([two_x, one_x], axis=1)
    )
    return rows_halo, high, low


def rolled(v, step):
    rows, cols = v.shape
    down, across = step
    return (
        pltpu.roll(v, rows - down, 0),
        pltpu.roll(v, down, 0),
        pltpu.roll(v, cols - across, 1),
        pltpu.roll(v, across, 1),
    )


def couplings(perm, step):
    down, up, right, left = rolled(perm, step)
    twice = 2.0 * perm
    south = twice * down / (perm + down)
    east = twice * right / (perm + right)
    linkage = (
        jnp.where(down > 0.0, south, twice),
        jnp.where(up > 0.0, pltpu.roll(south, step[0], 0), twice),
        jnp.where(right > 0.0, east, twice),
        jnp.where(left > 0.0, pltpu.roll(east, step[1], 1), twice),
    )
    diagonal = linkage[0] + linkage[1] + linkage[2] + linkage[3]
    return linkage, diagonal


def operator(linkage, diagonal, current, step):
    beside_all = rolled(current, step)
    return diagonal * current - (
        linkage[0] * beside_all[0]
        + linkage[1] * beside_all[1]
        + linkage[2] * beside_all[2]
        + linkage[3] * beside_all[3]
    )


def lane_tiles(high, low, plane):
    lane = lax.broadcasted_iota(jnp.int32, high.shape, 1)
    after = pltpu.roll(high, (LANE_PAD - HALO * plane) % LANE_PAD, 1)
    before = pltpu.roll(low, (LANE_PAD - HALO - HALO * plane) % LANE_PAD, 1)
    zero = jnp.zeros_like(high)
    return jnp.where(lane < HALO, after, zero), jnp.where(lane >= LANE_PAD - HALO, before, zero)


def base_layout(own, halo_rows, after, before, width):
    top = jnp.concatenate([own, halo_rows], axis=0)
    gap = jnp.zeros((top.shape[0], width - top.shape[1] - 2 * LANE_PAD), top.dtype)
    return jnp.concatenate([top, after, gap, before], axis=1)


def smooth_kernel(
    seeds_ref, levels_ref, src_ref, cls_ref, rows_ref, high_ref, low_ref,
    sol_ref, corr_ref, codes_pk, spare, wide,
):
    s = pl.program_id(0)
    count = PER_STEP * pl.num_programs(0)
    rows, cols = sol_ref.shape[1], sol_ref.shape[2]
    ext_x, width = codes_pk.shape
    span = cols + 2 * HALO
    lane = lax.broadcasted_iota(jnp.int32, (ext_x, width), 1)
    corner = rows_ref[count + 1]
    high_y = jnp.concatenate([high_ref[...], corner[:, :LANE_PAD]], axis=0)
    low_y = jnp.concatenate([low_ref[...], corner[:, LANE_PAD : 2 * LANE_PAD]], axis=0)

    def packed(pieces):
        out = None
        for j, piece in enumerate(pieces):
            moved = pltpu.roll(piece, (j * span + HALO) % width, 1)
            out = moved if out is None else jnp.where(lane >= j * span, moved, out)
        return out

    @pl.when(s == 0)
    def _():
        after, before = lane_tiles(high_y, low_y, count)
        own = base_layout(
            cls_ref[...] + 1, rows_ref[count].astype(jnp.int32),
            after.astype(jnp.int32), before.astype(jnp.int32), width,
        )
        codes_pk[...] = packed([own] * PER_STEP)

    pieces = []
    for j in range(PER_STEP):
        plane = PER_STEP * s + j
        after, before = lane_tiles(high_y, low_y, plane)
        pieces.append(base_layout(src_ref[j], rows_ref[plane], after, before, width))
    source = packed(pieces)
    codes = codes_pk[...]
    valid = codes > 0
    classes = (codes - 1).reshape(ext_x // 8, 8, width)
    row_lane = lax.broadcasted_iota(jnp.int32, (8, width), 1)
    level = []
    for category in range(levels_ref.shape[1]):
        row = jnp.full((8, width), levels_ref[seeds_ref[PER_STEP * s], category], jnp.float32)
        for j in range(1, PER_STEP):
            pick_level = levels_ref[seeds_ref[PER_STEP * s + j], category]
            row = jnp.where(row_lane >= j * span, pick_level, row)
        level.append(row[None])
    bit0 = (classes & 1) != 0
    bit1 = (classes & 2) != 0
    bit2 = (classes & 4) != 0
    low = jnp.where(bit1, jnp.where(bit0, level[3], level[2]), jnp.where(bit0, level[1], level[0]))
    high = jnp.where(bit1, jnp.where(bit0, level[7], level[6]), jnp.where(bit0, level[5], level[4]))
    perm = jnp.where(valid, jnp.where(bit2, high, low).reshape(ext_x, width), 0.0)
    linkage, diagonal = couplings(perm, (1, 1))
    inverse = 1.0 / jnp.where(valid, diagonal, 1.0)
    current = (DAMPING * source) * inverse
    for sweep_index in range(SWEEPS):
        residual = source - operator(linkage, diagonal, current, (1, 1))
        if sweep_index + 1 < SWEEPS:
            current = current + (DAMPING * residual) * inverse

    def even_rows(v):
        parts = []
        for k in range(width // 128):
            spare[k] = v[:, k * 128 : (k + 1) * 128]
            parts.append(spare[k, pl.ds(0, ext_x // 2, stride=2), :])
        return jnp.concatenate(parts, axis=1)

    pairs = residual + pltpu.roll(residual, ext_x - 1, 0)
    coarse_rhs = even_rows(pairs + pltpu.roll(pairs, width - 1, 1))
    pairs = perm + pltpu.roll(perm, ext_x - 1, 0)
    coarse_perm = 0.25 * even_rows(pairs + pltpu.roll(pairs, width - 1, 1))
    coarse_links, coarse_diagonal = couplings(coarse_perm, (1, 2))
    coarse_inverse = 1.0 / jnp.where(coarse_perm > 0.0, coarse_diagonal, 1.0)
    first = (DAMPING * coarse_rhs) * coarse_inverse
    correction = first + (
        DAMPING * (coarse_rhs - operator(coarse_links, coarse_diagonal, first, (1, 2)))
    ) * coarse_inverse
    pick = (
        lax.broadcasted_iota(jnp.int32, (cols, cols // 2), 0)
        == 2 * lax.broadcasted_iota(jnp.int32, (cols, cols // 2), 1)
    ).astype(jnp.float32)
    odd_col = (lax.broadcasted_iota(jnp.int32, (rows, cols), 1) & 1) == 1
    for j in range(PER_STEP):
        back = (width - j * span - HALO) % width
        own = pltpu.roll(correction, back, 1)[: rows // 2, :cols]
        corr_ref[j] = jnp.dot(own, pick, precision=HI, preferred_element_type=jnp.float32)
        for k in range(cols // 128):
            piece = own[:, k * 128 : (k + 1) * 128]
            wide[k, pl.ds(0, rows // 2, stride=2), :] = piece
            wide[k, pl.ds(1, rows // 2, stride=2), :] = piece
        spread = jnp.concatenate([wide[k] for k in range(cols // 128)], axis=1)
        spread = jnp.where(odd_col, pltpu.roll(spread, 1, 1), spread)
        sol_ref[j] = pltpu.roll(current, back, 1)[:rows, :cols] + spread


def shards(source, sample_seeds, perm_levels, perm_classes):
    h = HALO
    count, rows, cols = source.shape
    ext_x = rows + 2 * h
    width = -(-(PER_STEP * (cols + 2 * h)) // 128) * 128
    rows_halo, high, low = halo_pieces(source, perm_classes, h)
    smem = pl.BlockSpec(memory_space=pltpu.MemorySpace.SMEM)
    vmem = pl.BlockSpec(memory_space=pltpu.MemorySpace.VMEM)
    whole = lambda shape: pl.BlockSpec(shape, lambda s: (0,) * len(shape))
    solution_block, correction_block = pl.pallas_call(
        smooth_kernel,
        grid=(count // PER_STEP,),
        in_specs=[
            smem,
            smem,
            pl.BlockSpec((PER_STEP, rows, cols), lambda s: (s, 0, 0)),
            whole((rows, cols)),
            vmem,
            vmem,
            vmem,
        ],
        out_specs=[
            pl.BlockSpec((PER_STEP, rows, cols), lambda s: (s, 0, 0)),
            pl.BlockSpec((PER_STEP, rows // 2, cols // 2), lambda s: (s, 0, 0)),
        ],
        out_shape=[
            jax.ShapeDtypeStruct((count, rows, cols), jnp.float32),
            jax.ShapeDtypeStruct((count, rows // 2, cols // 2), jnp.float32),
        ],
        scratch_shapes=[
            pltpu.VMEM((ext_x, width), jnp.int32),
            pltpu.VMEM((width // 128, ext_x, 128), jnp.float32),
            pltpu.VMEM((cols // 128, rows, 128), jnp.float32),
        ],
        compiler_params=pltpu.CompilerParams(dimension_semantics=("arbitrary",)),
    )(sample_seeds, perm_levels, source, perm_classes, rows_halo, high, low)
    return solution_block, correction_block


def solution(mesh):
    placed = (P("sa", "gx", "gy"), P("sa"), P("sa", None), P("gx", "gy"))
    return jax.shard_map(
        shards,
        mesh=mesh,
        in_specs=placed,
        out_specs=(P("sa", "gx", "gy"), P("sa", "gx", "gy")),
        check_vma=False,
    )
```

```python
import jax
import jax.numpy as jnp
from jax import lax
from jax.experimental import pallas as pl
from jax.experimental.pallas import tpu as pltpu
from jax.sharding import PartitionSpec as P

SWEEPS = 4
DAMPING = 0.8
HALO = 8
LANE_PAD = 128
HI = lax.Precision.HIGHEST
PER_STEP = 4


def swap_exchange(last, first, axis):
    n = lax.axis_size(axis)
    even = lax.axis_index(axis) % 2 == 0
    inner = [(k, k ^ 1) for k in range(n) if k ^ 1 < n]
    outer = [(k, k + 1) for k in range(1, n - 1, 2)] + [(k + 1, k) for k in range(1, n - 1, 2)]
    two = lax.ppermute(jnp.where(even, first, last), axis, outer)
    one = lax.ppermute(jnp.where(even, last, first), axis, inner)
    return jnp.where(even, two, one), jnp.where(even, one, two)


def halo_pieces(source, classes, width):
    stack = lambda a, b: jnp.concatenate([a, (b + 1).astype(a.dtype)[None]], axis=0)
    low, high = swap_exchange(
        stack(source[:, -width:, :], classes[-width:, :]),
        stack(source[:, :width, :], classes[:width, :]),
        "gx",
    )
    rows_halo = jnp.concatenate([high, low], axis=1)

    def packed(strip, halo_strip):
        planes = jnp.concatenate([strip, halo_strip], axis=1)
        count, rows, _ = planes.shape
        flat = jnp.transpose(planes, (1, 0, 2)).reshape(rows, count * width)
        return jnp.pad(flat, ((0, 0), (0, LANE_PAD - count * width)))

    last = packed(stack(source[:, :, -width:], classes[:, -width:]), rows_halo[:, :, -width:])
    first = packed(stack(source[:, :, :width], classes[:, :width]), rows_halo[:, :, :width])
    low, high = swap_exchange(last, first, "gy")
    return rows_halo, high, low


def rolled(v, step):
    rows, cols = v.shape
    down, across = step
    return (
        pltpu.roll(v, rows - down, 0),
        pltpu.roll(v, down, 0),
        pltpu.roll(v, cols - across, 1),
        pltpu.roll(v, across, 1),
    )


def couplings(perm, step):
    down, up, right, left = rolled(perm, step)
    twice = 2.0 * perm
    south = twice * down / (perm + down)
    east = twice * right / (perm + right)
    linkage = (
        jnp.where(down > 0.0, south, twice),
        jnp.where(up > 0.0, pltpu.roll(south, step[0], 0), twice),
        jnp.where(right > 0.0, east, twice),
        jnp.where(left > 0.0, pltpu.roll(east, step[1], 1), twice),
    )
    diagonal = linkage[0] + linkage[1] + linkage[2] + linkage[3]
    return linkage, diagonal


def operator(linkage, diagonal, current, step):
    beside_all = rolled(current, step)
    return diagonal * current - (
        linkage[0] * beside_all[0]
        + linkage[1] * beside_all[1]
        + linkage[2] * beside_all[2]
        + linkage[3] * beside_all[3]
    )


def lane_tiles(high_ref, low_ref, plane):
    high = high_ref[...]
    low = low_ref[...]
    lane = lax.broadcasted_iota(jnp.int32, high.shape, 1)
    after = pltpu.roll(high, (LANE_PAD - HALO * plane) % LANE_PAD, 1)
    before = pltpu.roll(low, (LANE_PAD - HALO - HALO * plane) % LANE_PAD, 1)
    zero = jnp.zeros_like(high)
    return jnp.where(lane < HALO, after, zero), jnp.where(lane >= LANE_PAD - HALO, before, zero)


def base_layout(own, halo_rows, after, before, width):
    top = jnp.concatenate([own, halo_rows], axis=0)
    gap = jnp.zeros((top.shape[0], width - top.shape[1] - 2 * LANE_PAD), top.dtype)
    return jnp.concatenate([top, after, gap, before], axis=1)


def smooth_kernel(
    seeds_ref, levels_ref, src_ref, cls_ref, rows_ref, high_ref, low_ref,
    sol_ref, corr_ref, codes_pk, spare, wide,
):
    s = pl.program_id(0)
    count = PER_STEP * pl.num_programs(0)
    rows, cols = sol_ref.shape[1], sol_ref.shape[2]
    ext_x, width = codes_pk.shape
    span = cols + 2 * HALO
    lane = lax.broadcasted_iota(jnp.int32, (ext_x, width), 1)

    def packed(pieces):
        out = None
        for j, piece in enumerate(pieces):
            moved = pltpu.roll(piece, (j * span + HALO) % width, 1)
            out = moved if out is None else jnp.where(lane >= j * span, moved, out)
        return out

    @pl.when(s == 0)
    def _():
        after, before = lane_tiles(high_ref, low_ref, count)
        own = base_layout(
            cls_ref[...] + 1, rows_ref[count].astype(jnp.int32),
            after.astype(jnp.int32), before.astype(jnp.int32), width,
        )
        codes_pk[...] = packed([own] * PER_STEP)

    pieces = []
    for j in range(PER_STEP):
        plane = PER_STEP * s + j
        after, before = lane_tiles(high_ref, low_ref, plane)
        pieces.append(base_layout(src_ref[j], rows_ref[plane], after, before, width))
    source = packed(pieces)
    codes = codes_pk[...]
    valid = codes > 0
    classes = (codes - 1).reshape(ext_x // 8, 8, width)
    row_lane = lax.broadcasted_iota(jnp.int32, (8, width), 1)
    level = []
    for category in range(levels_ref.shape[1]):
        row = jnp.full((8, width), levels_ref[seeds_ref[PER_STEP * s], category], jnp.float32)
        for j in range(1, PER_STEP):
            pick_level = levels_ref[seeds_ref[PER_STEP * s + j], category]
            row = jnp.where(row_lane >= j * span, pick_level, row)
        level.append(row[None])
    bit0 = (classes & 1) != 0
    bit1 = (classes & 2) != 0
    bit2 = (classes & 4) != 0
    low = jnp.where(bit1, jnp.where(bit0, level[3], level[2]), jnp.where(bit0, level[1], level[0]))
    high = jnp.where(bit1, jnp.where(bit0, level[7], level[6]), jnp.where(bit0, level[5], level[4]))
    perm = jnp.where(valid, jnp.where(bit2, high, low).reshape(ext_x, width), 0.0)
    linkage, diagonal = couplings(perm, (1, 1))
    inverse = 1.0 / jnp.where(valid, diagonal, 1.0)
    current = (DAMPING * source) * inverse
    for sweep_index in range(SWEEPS):
        residual = source - operator(linkage, diagonal, current, (1, 1))
        if sweep_index + 1 < SWEEPS:
            current = current + (DAMPING * residual) * inverse

    def even_rows(v):
        parts = []
        for k in range(width // 128):
            spare[k] = v[:, k * 128 : (k + 1) * 128]
            parts.append(spare[k, pl.ds(0, ext_x // 2, stride=2), :])
        return jnp.concatenate(parts, axis=1)

    pairs = residual + pltpu.roll(residual, ext_x - 1, 0)
    coarse_rhs = even_rows(pairs + pltpu.roll(pairs, width - 1, 1))
    pairs = perm + pltpu.roll(perm, ext_x - 1, 0)
    coarse_perm = 0.25 * even_rows(pairs + pltpu.roll(pairs, width - 1, 1))
    coarse_links, coarse_diagonal = couplings(coarse_perm, (1, 2))
    coarse_inverse = 1.0 / jnp.where(coarse_perm > 0.0, coarse_diagonal, 1.0)
    first = (DAMPING * coarse_rhs) * coarse_inverse
    correction = first + (
        DAMPING * (coarse_rhs - operator(coarse_links, coarse_diagonal, first, (1, 2)))
    ) * coarse_inverse
    pick = (
        lax.broadcasted_iota(jnp.int32, (cols, cols // 2), 0)
        == 2 * lax.broadcasted_iota(jnp.int32, (cols, cols // 2), 1)
    ).astype(jnp.float32)
    odd_col = (lax.broadcasted_iota(jnp.int32, (rows, cols), 1) & 1) == 1
    for j in range(PER_STEP):
        back = (width - j * span - HALO) % width
        own = pltpu.roll(correction, back, 1)[: rows // 2, :cols]
        corr_ref[j] = jnp.dot(own, pick, precision=HI, preferred_element_type=jnp.float32)
        for k in range(cols // 128):
            piece = own[:, k * 128 : (k + 1) * 128]
            wide[k, pl.ds(0, rows // 2, stride=2), :] = piece
            wide[k, pl.ds(1, rows // 2, stride=2), :] = piece
        spread = jnp.concatenate([wide[k] for k in range(cols // 128)], axis=1)
        spread = jnp.where(odd_col, pltpu.roll(spread, 1, 1), spread)
        sol_ref[j] = pltpu.roll(current, back, 1)[:rows, :cols] + spread


def shards(source, sample_seeds, perm_levels, perm_classes):
    h = HALO
    count, rows, cols = source.shape
    ext_x = rows + 2 * h
    width = -(-(PER_STEP * (cols + 2 * h)) // 128) * 128
    rows_halo, high, low = halo_pieces(source, perm_classes, h)
    smem = pl.BlockSpec(memory_space=pltpu.MemorySpace.SMEM)
    vmem = pl.BlockSpec(memory_space=pltpu.MemorySpace.VMEM)
    whole = lambda shape: pl.BlockSpec(shape, lambda s: (0,) * len(shape))
    solution_block, correction_block = pl.pallas_call(
        smooth_kernel,
        grid=(count // PER_STEP,),
        in_specs=[
            smem,
            smem,
            pl.BlockSpec((PER_STEP, rows, cols), lambda s: (s, 0, 0)),
            whole((rows, cols)),
            vmem,
            vmem,
            vmem,
        ],
        out_specs=[
            pl.BlockSpec((PER_STEP, rows, cols), lambda s: (s, 0, 0)),
            pl.BlockSpec((PER_STEP, rows // 2, cols // 2), lambda s: (s, 0, 0)),
        ],
        out_shape=[
            jax.ShapeDtypeStruct((count, rows, cols), jnp.float32),
            jax.ShapeDtypeStruct((count, rows // 2, cols // 2), jnp.float32),
        ],
        scratch_shapes=[
            pltpu.VMEM((ext_x, width), jnp.int32),
            pltpu.VMEM((width // 128, ext_x, 128), jnp.float32),
            pltpu.VMEM((cols // 128, rows, 128), jnp.float32),
        ],
        compiler_params=pltpu.CompilerParams(dimension_semantics=("arbitrary",)),
    )(sample_seeds, perm_levels, source, perm_classes, rows_halo, high, low)
    return solution_block, correction_block


def solution(mesh):
    placed = (P("sa", "gx", "gy"), P("sa"), P("sa", None), P("gx", "gy"))
    return jax.shard_map(
        shards,
        mesh=mesh,
        in_specs=placed,
        out_specs=(P("sa", "gx", "gy"), P("sa", "gx", "gy")),
        check_vma=False,
    )
```

```python
import jax
import jax.numpy as jnp
from jax import lax
from jax.experimental import pallas as pl
from jax.experimental.pallas import tpu as pltpu
from jax.sharding import PartitionSpec as P

SWEEPS = 4
DAMPING = 0.8
HALO = 8
LANE_PAD = 128
HI = lax.Precision.HIGHEST
PER_STEP = 4


def swap_exchange(last, first, axis):
    n = lax.axis_size(axis)
    even = lax.axis_index(axis) % 2 == 0
    inner = [(k, k ^ 1) for k in range(n) if k ^ 1 < n]
    outer = [(k, k + 1) for k in range(1, n - 1, 2)] + [(k + 1, k) for k in range(1, n - 1, 2)]
    one = lax.ppermute(jnp.where(even, last, first), axis, inner)
    two = lax.ppermute(jnp.where(even, first, last), axis, outer)
    return jnp.where(even, two, one), jnp.where(even, one, two)


def halo_pieces(source, classes, width):
    stack = lambda a, b: jnp.concatenate([a, (b + 1).astype(a.dtype)[None]], axis=0)
    low, high = swap_exchange(
        stack(source[:, -width:, :], classes[-width:, :]),
        stack(source[:, :width, :], classes[:width, :]),
        "gx",
    )
    rows_halo = jnp.concatenate([high, low], axis=1)

    def packed(strip, halo_strip):
        planes = jnp.concatenate([strip, halo_strip], axis=1)
        count, rows, _ = planes.shape
        flat = jnp.transpose(planes, (1, 0, 2)).reshape(rows, count * width)
        return jnp.pad(flat, ((0, 0), (0, LANE_PAD - count * width)))

    last = packed(stack(source[:, :, -width:], classes[:, -width:]), rows_halo[:, :, -width:])
    first = packed(stack(source[:, :, :width], classes[:, :width]), rows_halo[:, :, :width])
    n = lax.axis_size("gy")
    even = lax.axis_index("gy") % 2 == 0
    one = lax.ppermute(jnp.where(even, last, first), "gy", [(k, k ^ 1) for k in range(n) if k ^ 1 < n])
    two = lax.ppermute(
        jnp.where(even, first, last), "gy",
        [(k, k + 1) for k in range(1, n - 1, 2)] + [(k + 1, k) for k in range(1, n - 1, 2)],
    )
    return rows_halo, one, two, even.astype(jnp.int32)[None]


def rolled(v, step):
    rows, cols = v.shape
    down, across = step
    return (
        pltpu.roll(v, rows - down, 0),
        pltpu.roll(v, down, 0),
        pltpu.roll(v, cols - across, 1),
        pltpu.roll(v, across, 1),
    )


def couplings(perm, step):
    down, up, right, left = rolled(perm, step)
    twice = 2.0 * perm
    south = twice * down / (perm + down)
    east = twice * right / (perm + right)
    linkage = (
        jnp.where(down > 0.0, south, twice),
        jnp.where(up > 0.0, pltpu.roll(south, step[0], 0), twice),
        jnp.where(right > 0.0, east, twice),
        jnp.where(left > 0.0, pltpu.roll(east, step[1], 1), twice),
    )
    diagonal = linkage[0] + linkage[1] + linkage[2] + linkage[3]
    return linkage, diagonal


def operator(linkage, diagonal, current, step):
    beside_all = rolled(current, step)
    return diagonal * current - (
        linkage[0] * beside_all[0]
        + linkage[1] * beside_all[1]
        + linkage[2] * beside_all[2]
        + linkage[3] * beside_all[3]
    )


def lane_tiles(high, low, plane):
    lane = lax.broadcasted_iota(jnp.int32, high.shape, 1)
    after = pltpu.roll(high, (LANE_PAD - HALO * plane) % LANE_PAD, 1)
    before = pltpu.roll(low, (LANE_PAD - HALO - HALO * plane) % LANE_PAD, 1)
    zero = jnp.zeros_like(high)
    return jnp.where(lane < HALO, after, zero), jnp.where(lane >= LANE_PAD - HALO, before, zero)


def base_layout(own, halo_rows, after, before, width):
    top = jnp.concatenate([own, halo_rows], axis=0)
    gap = jnp.zeros((top.shape[0], width - top.shape[1] - 2 * LANE_PAD), top.dtype)
    return jnp.concatenate([top, after, gap, before], axis=1)


def smooth_kernel(
    seeds_ref, levels_ref, parity_ref, src_ref, cls_ref, rows_ref, one_ref, two_ref,
    sol_ref, corr_ref, codes_pk, spare, wide,
):
    s = pl.program_id(0)
    count = PER_STEP * pl.num_programs(0)
    rows, cols = sol_ref.shape[1], sol_ref.shape[2]
    ext_x, width = codes_pk.shape
    span = cols + 2 * HALO
    lane = lax.broadcasted_iota(jnp.int32, (ext_x, width), 1)
    even_y = parity_ref[0] == 1
    high_y = jnp.where(even_y, one_ref[...], two_ref[...])
    low_y = jnp.where(even_y, two_ref[...], one_ref[...])

    def packed(pieces):
        out = None
        for j, piece in enumerate(pieces):
            moved = pltpu.roll(piece, (j * span + HALO) % width, 1)
            out = moved if out is None else jnp.where(lane >= j * span, moved, out)
        return out

    @pl.when(s == 0)
    def _():
        after, before = lane_tiles(high_y, low_y, count)
        own = base_layout(
            cls_ref[...] + 1, rows_ref[count].astype(jnp.int32),
            after.astype(jnp.int32), before.astype(jnp.int32), width,
        )
        codes_pk[...] = packed([own] * PER_STEP)

    pieces = []
    for j in range(PER_STEP):
        plane = PER_STEP * s + j
        after, before = lane_tiles(high_y, low_y, plane)
        pieces.append(base_layout(src_ref[j], rows_ref[plane], after, before, width))
    source = packed(pieces)
    codes = codes_pk[...]
    valid = codes > 0
    classes = (codes - 1).reshape(ext_x // 8, 8, width)
    row_lane = lax.broadcasted_iota(jnp.int32, (8, width), 1)
    level = []
    for category in range(levels_ref.shape[1]):
        row = jnp.full((8, width), levels_ref[seeds_ref[PER_STEP * s], category], jnp.float32)
        for j in range(1, PER_STEP):
            pick_level = levels_ref[seeds_ref[PER_STEP * s + j], category]
            row = jnp.where(row_lane >= j * span, pick_level, row)
        level.append(row[None])
    bit0 = (classes & 1) != 0
    bit1 = (classes & 2) != 0
    bit2 = (classes & 4) != 0
    low = jnp.where(bit1, jnp.where(bit0, level[3], level[2]), jnp.where(bit0, level[1], level[0]))
    high = jnp.where(bit1, jnp.where(bit0, level[7], level[6]), jnp.where(bit0, level[5], level[4]))
    perm = jnp.where(valid, jnp.where(bit2, high, low).reshape(ext_x, width), 0.0)
    linkage, diagonal = couplings(perm, (1, 1))
    inverse = 1.0 / jnp.where(valid, diagonal, 1.0)
    current = (DAMPING * source) * inverse
    for sweep_index in range(SWEEPS):
        residual = source - operator(linkage, diagonal, current, (1, 1))
        if sweep_index + 1 < SWEEPS:
            current = current + (DAMPING * residual) * inverse

    def even_rows(v):
        parts = []
        for k in range(width // 128):
            spare[k] = v[:, k * 128 : (k + 1) * 128]
            parts.append(spare[k, pl.ds(0, ext_x // 2, stride=2), :])
        return jnp.concatenate(parts, axis=1)

    pairs = residual + pltpu.roll(residual, ext_x - 1, 0)
    coarse_rhs = even_rows(pairs + pltpu.roll(pairs, width - 1, 1))
    pairs = perm + pltpu.roll(perm, ext_x - 1, 0)
    coarse_perm = 0.25 * even_rows(pairs + pltpu.roll(pairs, width - 1, 1))
    coarse_links, coarse_diagonal = couplings(coarse_perm, (1, 2))
    coarse_inverse = 1.0 / jnp.where(coarse_perm > 0.0, coarse_diagonal, 1.0)
    first = (DAMPING * coarse_rhs) * coarse_inverse
    correction = first + (
        DAMPING * (coarse_rhs - operator(coarse_links, coarse_diagonal, first, (1, 2)))
    ) * coarse_inverse
    pick = (
        lax.broadcasted_iota(jnp.int32, (cols, cols // 2), 0)
        == 2 * lax.broadcasted_iota(jnp.int32, (cols, cols // 2), 1)
    ).astype(jnp.float32)
    odd_col = (lax.broadcasted_iota(jnp.int32, (rows, cols), 1) & 1) == 1
    for j in range(PER_STEP):
        back = (width - j * span - HALO) % width
        own = pltpu.roll(correction, back, 1)[: rows // 2, :cols]
        corr_ref[j] = jnp.dot(own, pick, precision=HI, preferred_element_type=jnp.float32)
        for k in range(cols // 128):
            piece = own[:, k * 128 : (k + 1) * 128]
            wide[k, pl.ds(0, rows // 2, stride=2), :] = piece
            wide[k, pl.ds(1, rows // 2, stride=2), :] = piece
        spread = jnp.concatenate([wide[k] for k in range(cols // 128)], axis=1)
        spread = jnp.where(odd_col, pltpu.roll(spread, 1, 1), spread)
        sol_ref[j] = pltpu.roll(current, back, 1)[:rows, :cols] + spread


def shards(source, sample_seeds, perm_levels, perm_classes):
    h = HALO
    count, rows, cols = source.shape
    ext_x = rows + 2 * h
    width = -(-(PER_STEP * (cols + 2 * h)) // 128) * 128
    rows_halo, one, two, parity = halo_pieces(source, perm_classes, h)
    smem = pl.BlockSpec(memory_space=pltpu.MemorySpace.SMEM)
    vmem = pl.BlockSpec(memory_space=pltpu.MemorySpace.VMEM)
    whole = lambda shape: pl.BlockSpec(shape, lambda s: (0,) * len(shape))
    solution_block, correction_block = pl.pallas_call(
        smooth_kernel,
        grid=(count // PER_STEP,),
        in_specs=[
            smem,
            smem,
            smem,
            pl.BlockSpec((PER_STEP, rows, cols), lambda s: (s, 0, 0)),
            whole((rows, cols)),
            vmem,
            vmem,
            vmem,
        ],
        out_specs=[
            pl.BlockSpec((PER_STEP, rows, cols), lambda s: (s, 0, 0)),
            pl.BlockSpec((PER_STEP, rows // 2, cols // 2), lambda s: (s, 0, 0)),
        ],
        out_shape=[
            jax.ShapeDtypeStruct((count, rows, cols), jnp.float32),
            jax.ShapeDtypeStruct((count, rows // 2, cols // 2), jnp.float32),
        ],
        scratch_shapes=[
            pltpu.VMEM((ext_x, width), jnp.int32),
            pltpu.VMEM((width // 128, ext_x, 128), jnp.float32),
            pltpu.VMEM((cols // 128, rows, 128), jnp.float32),
        ],
        compiler_params=pltpu.CompilerParams(dimension_semantics=("arbitrary",)),
    )(sample_seeds, perm_levels, parity, source, perm_classes, rows_halo, one, two)
    return solution_block, correction_block


def solution(mesh):
    placed = (P("sa", "gx", "gy"), P("sa"), P("sa", None), P("gx", "gy"))
    return jax.shard_map(
        shards,
        mesh=mesh,
        in_specs=placed,
        out_specs=(P("sa", "gx", "gy"), P("sa", "gx", "gy")),
        check_vma=False,
    )
```

```python
import jax
import jax.numpy as jnp
from jax import lax
from jax.experimental import pallas as pl
from jax.experimental.pallas import tpu as pltpu
from jax.sharding import PartitionSpec as P

SWEEPS = 4
DAMPING = 0.8
HALO = 8
LANE_PAD = 128
HI = lax.Precision.HIGHEST
PER_STEP = 4


def swap_exchange(last, first, axis):
    n = lax.axis_size(axis)
    even = lax.axis_index(axis) % 2 == 0
    inner = [(k, k ^ 1) for k in range(n) if k ^ 1 < n]
    outer = [(k, k + 1) for k in range(1, n - 1, 2)] + [(k + 1, k) for k in range(1, n - 1, 2)]
    one = lax.ppermute(jnp.where(even, last, first), axis, inner)
    two = lax.ppermute(jnp.where(even, first, last), axis, outer)
    return jnp.where(even, two, one), jnp.where(even, one, two)


def halo_pieces(source, classes, width):
    stack = lambda a, b: jnp.concatenate([a, (b + 1).astype(a.dtype)[None]], axis=0)
    low, high = swap_exchange(
        stack(source[:, -width:, :], classes[-width:, :]),
        stack(source[:, :width, :], classes[:width, :]),
        "gx",
    )
    rows_halo = jnp.concatenate([high, low], axis=1)

    def packed(strip, halo_strip):
        planes = jnp.concatenate([strip, halo_strip], axis=1)
        count, rows, _ = planes.shape
        flat = jnp.transpose(planes, (1, 0, 2)).reshape(rows, count * width)
        return jnp.pad(flat, ((0, 0), (0, LANE_PAD - count * width)))

    last = packed(stack(source[:, :, -width:], classes[:, -width:]), rows_halo[:, :, -width:])
    first = packed(stack(source[:, :, :width], classes[:, :width]), rows_halo[:, :, :width])
    rows_halo, last, first = lax.optimization_barrier((rows_halo, last, first))
    n = lax.axis_size("gy")
    even = lax.axis_index("gy") % 2 == 0
    one = lax.ppermute(jnp.where(even, last, first), "gy", [(k, k ^ 1) for k in range(n) if k ^ 1 < n])
    two = lax.ppermute(
        jnp.where(even, first, last), "gy",
        [(k, k + 1) for k in range(1, n - 1, 2)] + [(k + 1, k) for k in range(1, n - 1, 2)],
    )
    return rows_halo, one, two, even.astype(jnp.int32)[None]


def rolled(v, step):
    rows, cols = v.shape
    down, across = step
    return (
        pltpu.roll(v, rows - down, 0),
        pltpu.roll(v, down, 0),
        pltpu.roll(v, cols - across, 1),
        pltpu.roll(v, across, 1),
    )


def couplings(perm, step):
    down, up, right, left = rolled(perm, step)
    twice = 2.0 * perm
    south = twice * down / (perm + down)
    east = twice * right / (perm + right)
    linkage = (
        jnp.where(down > 0.0, south, twice),
        jnp.where(up > 0.0, pltpu.roll(south, step[0], 0), twice),
        jnp.where(right > 0.0, east, twice),
        jnp.where(left > 0.0, pltpu.roll(east, step[1], 1), twice),
    )
    diagonal = linkage[0] + linkage[1] + linkage[2] + linkage[3]
    return linkage, diagonal


def operator(linkage, diagonal, current, step):
    beside_all = rolled(current, step)
    return diagonal * current - (
        linkage[0] * beside_all[0]
        + linkage[1] * beside_all[1]
        + linkage[2] * beside_all[2]
        + linkage[3] * beside_all[3]
    )


def lane_tiles(high, low, plane):
    lane = lax.broadcasted_iota(jnp.int32, high.shape, 1)
    after = pltpu.roll(high, (LANE_PAD - HALO * plane) % LANE_PAD, 1)
    before = pltpu.roll(low, (LANE_PAD - HALO - HALO * plane) % LANE_PAD, 1)
    zero = jnp.zeros_like(high)
    return jnp.where(lane < HALO, after, zero), jnp.where(lane >= LANE_PAD - HALO, before, zero)


def base_layout(own, halo_rows, after, before, width):
    top = jnp.concatenate([own, halo_rows], axis=0)
    gap = jnp.zeros((top.shape[0], width - top.shape[1] - 2 * LANE_PAD), top.dtype)
    return jnp.concatenate([top, after, gap, before], axis=1)


def smooth_kernel(
    seeds_ref, levels_ref, parity_ref, src_ref, cls_ref, rows_ref, one_ref, two_ref,
    sol_ref, corr_ref, codes_pk, spare, wide,
):
    s = pl.program_id(0)
    count = PER_STEP * pl.num_programs(0)
    rows, cols = sol_ref.shape[1], sol_ref.shape[2]
    ext_x, width = codes_pk.shape
    span = cols + 2 * HALO
    lane = lax.broadcasted_iota(jnp.int32, (ext_x, width), 1)
    even_y = parity_ref[0] == 1
    high_y = jnp.where(even_y, one_ref[...], two_ref[...])
    low_y = jnp.where(even_y, two_ref[...], one_ref[...])

    def packed(pieces):
        out = None
        for j, piece in enumerate(pieces):
            moved = pltpu.roll(piece, (j * span + HALO) % width, 1)
            out = moved if out is None else jnp.where(lane >= j * span, moved, out)
        return out

    @pl.when(s == 0)
    def _():
        after, before = lane_tiles(high_y, low_y, count)
        own = base_layout(
            cls_ref[...] + 1, rows_ref[count].astype(jnp.int32),
            after.astype(jnp.int32), before.astype(jnp.int32), width,
        )
        codes_pk[...] = packed([own] * PER_STEP)

    pieces = []
    for j in range(PER_STEP):
        plane = PER_STEP * s + j
        after, before = lane_tiles(high_y, low_y, plane)
        pieces.append(base_layout(src_ref[j], rows_ref[plane], after, before, width))
    source = packed(pieces)
    codes = codes_pk[...]
    valid = codes > 0
    classes = (codes - 1).reshape(ext_x // 8, 8, width)
    row_lane = lax.broadcasted_iota(jnp.int32, (8, width), 1)
    level = []
    for category in range(levels_ref.shape[1]):
        row = jnp.full((8, width), levels_ref[seeds_ref[PER_STEP * s], category], jnp.float32)
        for j in range(1, PER_STEP):
            pick_level = levels_ref[seeds_ref[PER_STEP * s + j], category]
            row = jnp.where(row_lane >= j * span, pick_level, row)
        level.append(row[None])
    bit0 = (classes & 1) != 0
    bit1 = (classes & 2) != 0
    bit2 = (classes & 4) != 0
    low = jnp.where(bit1, jnp.where(bit0, level[3], level[2]), jnp.where(bit0, level[1], level[0]))
    high = jnp.where(bit1, jnp.where(bit0, level[7], level[6]), jnp.where(bit0, level[5], level[4]))
    perm = jnp.where(valid, jnp.where(bit2, high, low).reshape(ext_x, width), 0.0)
    linkage, diagonal = couplings(perm, (1, 1))
    inverse = 1.0 / jnp.where(valid, diagonal, 1.0)
    current = (DAMPING * source) * inverse
    for sweep_index in range(SWEEPS):
        residual = source - operator(linkage, diagonal, current, (1, 1))
        if sweep_index + 1 < SWEEPS:
            current = current + (DAMPING * residual) * inverse

    def even_rows(v):
        parts = []
        for k in range(width // 128):
            spare[k] = v[:, k * 128 : (k + 1) * 128]
            parts.append(spare[k, pl.ds(0, ext_x // 2, stride=2), :])
        return jnp.concatenate(parts, axis=1)

    pairs = residual + pltpu.roll(residual, ext_x - 1, 0)
    coarse_rhs = even_rows(pairs + pltpu.roll(pairs, width - 1, 1))
    pairs = perm + pltpu.roll(perm, ext_x - 1, 0)
    coarse_perm = 0.25 * even_rows(pairs + pltpu.roll(pairs, width - 1, 1))
    coarse_links, coarse_diagonal = couplings(coarse_perm, (1, 2))
    coarse_inverse = 1.0 / jnp.where(coarse_perm > 0.0, coarse_diagonal, 1.0)
    first = (DAMPING * coarse_rhs) * coarse_inverse
    correction = first + (
        DAMPING * (coarse_rhs - operator(coarse_links, coarse_diagonal, first, (1, 2)))
    ) * coarse_inverse
    pick = (
        lax.broadcasted_iota(jnp.int32, (cols, cols // 2), 0)
        == 2 * lax.broadcasted_iota(jnp.int32, (cols, cols // 2), 1)
    ).astype(jnp.float32)
    odd_col = (lax.broadcasted_iota(jnp.int32, (rows, cols), 1) & 1) == 1
    for j in range(PER_STEP):
        back = (width - j * span - HALO) % width
        own = pltpu.roll(correction, back, 1)[: rows // 2, :cols]
        corr_ref[j] = jnp.dot(own, pick, precision=HI, preferred_element_type=jnp.float32)
        for k in range(cols // 128):
            piece = own[:, k * 128 : (k + 1) * 128]
            wide[k, pl.ds(0, rows // 2, stride=2), :] = piece
            wide[k, pl.ds(1, rows // 2, stride=2), :] = piece
        spread = jnp.concatenate([wide[k] for k in range(cols // 128)], axis=1)
        spread = jnp.where(odd_col, pltpu.roll(spread, 1, 1), spread)
        sol_ref[j] = pltpu.roll(current, back, 1)[:rows, :cols] + spread


def shards(source, sample_seeds, perm_levels, perm_classes):
    h = HALO
    count, rows, cols = source.shape
    ext_x = rows + 2 * h
    width = -(-(PER_STEP * (cols + 2 * h)) // 128) * 128
    rows_halo, one, two, parity = halo_pieces(source, perm_classes, h)
    smem = pl.BlockSpec(memory_space=pltpu.MemorySpace.SMEM)
    vmem = pl.BlockSpec(memory_space=pltpu.MemorySpace.VMEM)
    whole = lambda shape: pl.BlockSpec(shape, lambda s: (0,) * len(shape))
    solution_block, correction_block = pl.pallas_call(
        smooth_kernel,
        grid=(count // PER_STEP,),
        in_specs=[
            smem,
            smem,
            smem,
            pl.BlockSpec((PER_STEP, rows, cols), lambda s: (s, 0, 0)),
            whole((rows, cols)),
            vmem,
            vmem,
            vmem,
        ],
        out_specs=[
            pl.BlockSpec((PER_STEP, rows, cols), lambda s: (s, 0, 0)),
            pl.BlockSpec((PER_STEP, rows // 2, cols // 2), lambda s: (s, 0, 0)),
        ],
        out_shape=[
            jax.ShapeDtypeStruct((count, rows, cols), jnp.float32),
            jax.ShapeDtypeStruct((count, rows // 2, cols // 2), jnp.float32),
        ],
        scratch_shapes=[
            pltpu.VMEM((ext_x, width), jnp.int32),
            pltpu.VMEM((width // 128, ext_x, 128), jnp.float32),
            pltpu.VMEM((cols // 128, rows, 128), jnp.float32),
        ],
        compiler_params=pltpu.CompilerParams(dimension_semantics=("arbitrary",)),
    )(sample_seeds, perm_levels, parity, source, perm_classes, rows_halo, one, two)
    return solution_block, correction_block


def solution(mesh):
    placed = (P("sa", "gx", "gy"), P("sa"), P("sa", None), P("gx", "gy"))
    return jax.shard_map(
        shards,
        mesh=mesh,
        in_specs=placed,
        out_specs=(P("sa", "gx", "gy"), P("sa", "gx", "gy")),
        check_vma=False,
    )
```

```python
import jax
import jax.numpy as jnp
from jax import lax
from jax.experimental import pallas as pl
from jax.experimental.pallas import tpu as pltpu
from jax.sharding import PartitionSpec as P

SWEEPS = 4
DAMPING = 0.8
HALO = 8
LANE_PAD = 128
HI = lax.Precision.HIGHEST
PER_STEP = 8


def swap_exchange(last, first, axis):
    n = lax.axis_size(axis)
    even = lax.axis_index(axis) % 2 == 0
    inner = [(k, k ^ 1) for k in range(n) if k ^ 1 < n]
    outer = [(k, k + 1) for k in range(1, n - 1, 2)] + [(k + 1, k) for k in range(1, n - 1, 2)]
    one = lax.ppermute(jnp.where(even, last, first), axis, inner)
    two = lax.ppermute(jnp.where(even, first, last), axis, outer)
    return jnp.where(even, two, one), jnp.where(even, one, two)


def halo_pieces(source, classes, width):
    stack = lambda a, b: jnp.concatenate([a, (b + 1).astype(a.dtype)[None]], axis=0)
    low, high = swap_exchange(
        stack(source[:, -width:, :], classes[-width:, :]),
        stack(source[:, :width, :], classes[:width, :]),
        "gx",
    )
    rows_halo = jnp.concatenate([high, low], axis=1)

    def packed(strip, halo_strip):
        planes = jnp.concatenate([strip, halo_strip], axis=1)
        count, rows, _ = planes.shape
        flat = jnp.transpose(planes, (1, 0, 2)).reshape(rows, count * width)
        return jnp.pad(flat, ((0, 0), (0, LANE_PAD - count * width)))

    last = packed(stack(source[:, :, -width:], classes[:, -width:]), rows_halo[:, :, -width:])
    first = packed(stack(source[:, :, :width], classes[:, :width]), rows_halo[:, :, :width])
    low, high = swap_exchange(last, first, "gy")
    return rows_halo, high, low


def rolled(v, step):
    rows, cols = v.shape
    down, across = step
    return (
        pltpu.roll(v, rows - down, 0),
        pltpu.roll(v, down, 0),
        pltpu.roll(v, cols - across, 1),
        pltpu.roll(v, across, 1),
    )


def couplings(perm, step):
    down, up, right, left = rolled(perm, step)
    twice = 2.0 * perm
    south = twice * down / (perm + down)
    east = twice * right / (perm + right)
    linkage = (
        jnp.where(down > 0.0, south, twice),
        jnp.where(up > 0.0, pltpu.roll(south, step[0], 0), twice),
        jnp.where(right > 0.0, east, twice),
        jnp.where(left > 0.0, pltpu.roll(east, step[1], 1), twice),
    )
    diagonal = linkage[0] + linkage[1] + linkage[2] + linkage[3]
    return linkage, diagonal


def operator(linkage, diagonal, current, step):
    beside_all = rolled(current, step)
    return diagonal * current - (
        linkage[0] * beside_all[0]
        + linkage[1] * beside_all[1]
        + linkage[2] * beside_all[2]
        + linkage[3] * beside_all[3]
    )


def lane_tiles(high_ref, low_ref, plane):
    high = high_ref[...]
    low = low_ref[...]
    lane = lax.broadcasted_iota(jnp.int32, high.shape, 1)
    after = pltpu.roll(high, (LANE_PAD - HALO * plane) % LANE_PAD, 1)
    before = pltpu.roll(low, (LANE_PAD - HALO - HALO * plane) % LANE_PAD, 1)
    zero = jnp.zeros_like(high)
    return jnp.where(lane < HALO, after, zero), jnp.where(lane >= LANE_PAD - HALO, before, zero)


def base_layout(own, halo_rows, after, before, width):
    top = jnp.concatenate([own, halo_rows], axis=0)
    gap = jnp.zeros((top.shape[0], width - top.shape[1] - 2 * LANE_PAD), top.dtype)
    return jnp.concatenate([top, after, gap, before], axis=1)


def smooth_kernel(
    seeds_ref, levels_ref, src_ref, cls_ref, rows_ref, high_ref, low_ref,
    sol_ref, corr_ref, codes_pk, spare, wide,
):
    s = pl.program_id(0)
    count = PER_STEP * pl.num_programs(0)
    rows, cols = sol_ref.shape[1], sol_ref.shape[2]
    ext_x, width = codes_pk.shape
    span = cols + 2 * HALO
    lane = lax.broadcasted_iota(jnp.int32, (ext_x, width), 1)

    def packed(pieces):
        out = None
        for j, piece in enumerate(pieces):
            moved = pltpu.roll(piece, (j * span + HALO) % width, 1)
            out = moved if out is None else jnp.where(lane >= j * span, moved, out)
        return out

    @pl.when(s == 0)
    def _():
        after, before = lane_tiles(high_ref, low_ref, count)
        own = base_layout(
            cls_ref[...] + 1, rows_ref[count].astype(jnp.int32),
            after.astype(jnp.int32), before.astype(jnp.int32), width,
        )
        codes_pk[...] = packed([own] * PER_STEP)

    pieces = []
    for j in range(PER_STEP):
        plane = PER_STEP * s + j
        after, before = lane_tiles(high_ref, low_ref, plane)
        pieces.append(base_layout(src_ref[j], rows_ref[plane], after, before, width))
    source = packed(pieces)
    codes = codes_pk[...]
    valid = codes > 0
    classes = (codes - 1).reshape(ext_x // 8, 8, width)
    row_lane = lax.broadcasted_iota(jnp.int32, (8, width), 1)
    level = []
    for category in range(levels_ref.shape[1]):
        row = jnp.full((8, width), levels_ref[seeds_ref[PER_STEP * s], category], jnp.float32)
        for j in range(1, PER_STEP):
            pick_level = levels_ref[seeds_ref[PER_STEP * s + j], category]
            row = jnp.where(row_lane >= j * span, pick_level, row)
        level.append(row[None])
    bit0 = (classes & 1) != 0
    bit1 = (classes & 2) != 0
    bit2 = (classes & 4) != 0
    low = jnp.where(bit1, jnp.where(bit0, level[3], level[2]), jnp.where(bit0, level[1], level[0]))
    high = jnp.where(bit1, jnp.where(bit0, level[7], level[6]), jnp.where(bit0, level[5], level[4]))
    perm = jnp.where(valid, jnp.where(bit2, high, low).reshape(ext_x, width), 0.0)
    linkage, diagonal = couplings(perm, (1, 1))
    inverse = 1.0 / jnp.where(valid, diagonal, 1.0)
    current = (DAMPING * source) * inverse
    for sweep_index in range(SWEEPS):
        residual = source - operator(linkage, diagonal, current, (1, 1))
        if sweep_index + 1 < SWEEPS:
            current = current + (DAMPING * residual) * inverse

    def even_rows(v):
        parts = []
        for k in range(width // 128):
            spare[k] = v[:, k * 128 : (k + 1) * 128]
            parts.append(spare[k, pl.ds(0, ext_x // 2, stride=2), :])
        return jnp.concatenate(parts, axis=1)

    pairs = residual + pltpu.roll(residual, ext_x - 1, 0)
    coarse_rhs = even_rows(pairs + pltpu.roll(pairs, width - 1, 1))
    pairs = perm + pltpu.roll(perm, ext_x - 1, 0)
    coarse_perm = 0.25 * even_rows(pairs + pltpu.roll(pairs, width - 1, 1))
    coarse_links, coarse_diagonal = couplings(coarse_perm, (1, 2))
    coarse_inverse = 1.0 / jnp.where(coarse_perm > 0.0, coarse_diagonal, 1.0)
    first = (DAMPING * coarse_rhs) * coarse_inverse
    correction = first + (
        DAMPING * (coarse_rhs - operator(coarse_links, coarse_diagonal, first, (1, 2)))
    ) * coarse_inverse
    pick = (
        lax.broadcasted_iota(jnp.int32, (cols, cols // 2), 0)
        == 2 * lax.broadcasted_iota(jnp.int32, (cols, cols // 2), 1)
    ).astype(jnp.float32)
    odd_col = (lax.broadcasted_iota(jnp.int32, (rows, cols), 1) & 1) == 1
    for j in range(PER_STEP):
        back = (width - j * span - HALO) % width
        own = pltpu.roll(correction, back, 1)[: rows // 2, :cols]
        corr_ref[j] = jnp.dot(own, pick, precision=HI, preferred_element_type=jnp.float32)
        for k in range(cols // 128):
            piece = own[:, k * 128 : (k + 1) * 128]
            wide[k, pl.ds(0, rows // 2, stride=2), :] = piece
            wide[k, pl.ds(1, rows // 2, stride=2), :] = piece
        spread = jnp.concatenate([wide[k] for k in range(cols // 128)], axis=1)
        spread = jnp.where(odd_col, pltpu.roll(spread, 1, 1), spread)
        sol_ref[j] = pltpu.roll(current, back, 1)[:rows, :cols] + spread


def shards(source, sample_seeds, perm_levels, perm_classes):
    h = HALO
    count, rows, cols = source.shape
    ext_x = rows + 2 * h
    width = -(-(PER_STEP * (cols + 2 * h)) // 128) * 128
    rows_halo, high, low = halo_pieces(source, perm_classes, h)
    smem = pl.BlockSpec(memory_space=pltpu.MemorySpace.SMEM)
    vmem = pl.BlockSpec(memory_space=pltpu.MemorySpace.VMEM)
    whole = lambda shape: pl.BlockSpec(shape, lambda s: (0,) * len(shape))
    solution_block, correction_block = pl.pallas_call(
        smooth_kernel,
        grid=(count // PER_STEP,),
        in_specs=[
            smem,
            smem,
            pl.BlockSpec((PER_STEP, rows, cols), lambda s: (s, 0, 0)),
            whole((rows, cols)),
            vmem,
            vmem,
            vmem,
        ],
        out_specs=[
            pl.BlockSpec((PER_STEP, rows, cols), lambda s: (s, 0, 0)),
            pl.BlockSpec((PER_STEP, rows // 2, cols // 2), lambda s: (s, 0, 0)),
        ],
        out_shape=[
            jax.ShapeDtypeStruct((count, rows, cols), jnp.float32),
            jax.ShapeDtypeStruct((count, rows // 2, cols // 2), jnp.float32),
        ],
        scratch_shapes=[
            pltpu.VMEM((ext_x, width), jnp.int32),
            pltpu.VMEM((width // 128, ext_x, 128), jnp.float32),
            pltpu.VMEM((cols // 128, rows, 128), jnp.float32),
        ],
        compiler_params=pltpu.CompilerParams(dimension_semantics=("arbitrary",)),
    )(sample_seeds, perm_levels, source, perm_classes, rows_halo, high, low)
    return solution_block, correction_block


def solution(mesh):
    placed = (P("sa", "gx", "gy"), P("sa"), P("sa", None), P("gx", "gy"))
    return jax.shard_map(
        shards,
        mesh=mesh,
        in_specs=placed,
        out_specs=(P("sa", "gx", "gy"), P("sa", "gx", "gy")),
        check_vma=False,
    )
```

```python
import jax
import jax.numpy as jnp
from jax import lax
from jax.experimental import pallas as pl
from jax.experimental.pallas import tpu as pltpu
from jax.sharding import PartitionSpec as P

SWEEPS = 4
DAMPING = 0.8
HALO = 8
LANE_PAD = 128
HI = lax.Precision.HIGHEST
PER_STEP = 8


def swap_exchange(last, first, axis):
    n = lax.axis_size(axis)
    even = lax.axis_index(axis) % 2 == 0
    inner = [(k, k ^ 1) for k in range(n) if k ^ 1 < n]
    outer = [(k, k + 1) for k in range(1, n - 1, 2)] + [(k + 1, k) for k in range(1, n - 1, 2)]
    one = lax.ppermute(jnp.where(even, last, first), axis, inner)
    two = lax.ppermute(jnp.where(even, first, last), axis, outer)
    return jnp.where(even, two, one), jnp.where(even, one, two)


def halo_pieces(source, classes, width):
    stack = lambda a, b: jnp.concatenate([a, (b + 1).astype(a.dtype)[None]], axis=0)
    low, high = swap_exchange(
        stack(source[:, -width:, :], classes[-width:, :]),
        stack(source[:, :width, :], classes[:width, :]),
        "gx",
    )
    rows_halo = jnp.concatenate([high, low], axis=1)

    def packed(strip, halo_strip):
        planes = jnp.concatenate([strip, halo_strip], axis=1)
        count, rows, _ = planes.shape
        flat = jnp.transpose(planes, (1, 0, 2)).reshape(rows, count * width)
        return jnp.pad(flat, ((0, 0), (0, LANE_PAD - count * width)))

    last = packed(stack(source[:, :, -width:], classes[:, -width:]), rows_halo[:, :, -width:])
    first = packed(stack(source[:, :, :width], classes[:, :width]), rows_halo[:, :, :width])
    n = lax.axis_size("gy")
    even = lax.axis_index("gy") % 2 == 0
    one = lax.ppermute(jnp.where(even, last, first), "gy", [(k, k ^ 1) for k in range(n) if k ^ 1 < n])
    two = lax.ppermute(
        jnp.where(even, first, last), "gy",
        [(k, k + 1) for k in range(1, n - 1, 2)] + [(k + 1, k) for k in range(1, n - 1, 2)],
    )
    return rows_halo, one, two, even.astype(jnp.int32)[None]


def rolled(v, step):
    rows, cols = v.shape
    down, across = step
    return (
        pltpu.roll(v, rows - down, 0),
        pltpu.roll(v, down, 0),
        pltpu.roll(v, cols - across, 1),
        pltpu.roll(v, across, 1),
    )


def couplings(perm, step):
    down, up, right, left = rolled(perm, step)
    twice = 2.0 * perm
    south = twice * down / (perm + down)
    east = twice * right / (perm + right)
    linkage = (
        jnp.where(down > 0.0, south, twice),
        jnp.where(up > 0.0, pltpu.roll(south, step[0], 0), twice),
        jnp.where(right > 0.0, east, twice),
        jnp.where(left > 0.0, pltpu.roll(east, step[1], 1), twice),
    )
    diagonal = linkage[0] + linkage[1] + linkage[2] + linkage[3]
    return linkage, diagonal


def operator(linkage, diagonal, current, step):
    beside_all = rolled(current, step)
    return diagonal * current - (
        linkage[0] * beside_all[0]
        + linkage[1] * beside_all[1]
        + linkage[2] * beside_all[2]
        + linkage[3] * beside_all[3]
    )


def lane_tiles(high, low, plane):
    lane = lax.broadcasted_iota(jnp.int32, high.shape, 1)
    after = pltpu.roll(high, (LANE_PAD - HALO * plane) % LANE_PAD, 1)
    before = pltpu.roll(low, (LANE_PAD - HALO - HALO * plane) % LANE_PAD, 1)
    zero = jnp.zeros_like(high)
    return jnp.where(lane < HALO, after, zero), jnp.where(lane >= LANE_PAD - HALO, before, zero)


def base_layout(own, halo_rows, after, before, width):
    top = jnp.concatenate([own, halo_rows], axis=0)
    gap = jnp.zeros((top.shape[0], width - top.shape[1] - 2 * LANE_PAD), top.dtype)
    return jnp.concatenate([top, after, gap, before], axis=1)


def smooth_kernel(
    seeds_ref, levels_ref, parity_ref, src_ref, cls_ref, rows_ref, one_ref, two_ref,
    sol_ref, corr_ref, codes_pk, spare, wide,
):
    s = pl.program_id(0)
    count = PER_STEP * pl.num_programs(0)
    rows, cols = sol_ref.shape[1], sol_ref.shape[2]
    ext_x, width = codes_pk.shape
    span = cols + 2 * HALO
    lane = lax.broadcasted_iota(jnp.int32, (ext_x, width), 1)
    even_y = parity_ref[0] == 1
    high_y = jnp.where(even_y, one_ref[...], two_ref[...])
    low_y = jnp.where(even_y, two_ref[...], one_ref[...])

    def packed(pieces):
        out = None
        for j, piece in enumerate(pieces):
            moved = pltpu.roll(piece, (j * span + HALO) % width, 1)
            out = moved if out is None else jnp.where(lane >= j * span, moved, out)
        return out

    @pl.when(s == 0)
    def _():
        after, before = lane_tiles(high_y, low_y, count)
        own = base_layout(
            cls_ref[...] + 1, rows_ref[count].astype(jnp.int32),
            after.astype(jnp.int32), before.astype(jnp.int32), width,
        )
        codes_pk[...] = packed([own] * PER_STEP)

    pieces = []
    for j in range(PER_STEP):
        plane = PER_STEP * s + j
        after, before = lane_tiles(high_y, low_y, plane)
        pieces.append(base_layout(src_ref[j], rows_ref[plane], after, before, width))
    source = packed(pieces)
    codes = codes_pk[...]
    valid = codes > 0
    classes = (codes - 1).reshape(ext_x // 8, 8, width)
    row_lane = lax.broadcasted_iota(jnp.int32, (8, width), 1)
    level = []
    for category in range(levels_ref.shape[1]):
        row = jnp.full((8, width), levels_ref[seeds_ref[PER_STEP * s], category], jnp.float32)
        for j in range(1, PER_STEP):
            pick_level = levels_ref[seeds_ref[PER_STEP * s + j], category]
            row = jnp.where(row_lane >= j * span, pick_level, row)
        level.append(row[None])
    bit0 = (classes & 1) != 0
    bit1 = (classes & 2) != 0
    bit2 = (classes & 4) != 0
    low = jnp.where(bit1, jnp.where(bit0, level[3], level[2]), jnp.where(bit0, level[1], level[0]))
    high = jnp.where(bit1, jnp.where(bit0, level[7], level[6]), jnp.where(bit0, level[5], level[4]))
    perm = jnp.where(valid, jnp.where(bit2, high, low).reshape(ext_x, width), 0.0)
    linkage, diagonal = couplings(perm, (1, 1))
    inverse = 1.0 / jnp.where(valid, diagonal, 1.0)
    current = (DAMPING * source) * inverse
    for sweep_index in range(SWEEPS):
        residual = source - operator(linkage, diagonal, current, (1, 1))
        if sweep_index + 1 < SWEEPS:
            current = current + (DAMPING * residual) * inverse

    def even_rows(v):
        parts = []
        for k in range(width // 128):
            spare[k] = v[:, k * 128 : (k + 1) * 128]
            parts.append(spare[k, pl.ds(0, ext_x // 2, stride=2), :])
        return jnp.concatenate(parts, axis=1)

    pairs = residual + pltpu.roll(residual, ext_x - 1, 0)
    coarse_rhs = even_rows(pairs + pltpu.roll(pairs, width - 1, 1))
    pairs = perm + pltpu.roll(perm, ext_x - 1, 0)
    coarse_perm = 0.25 * even_rows(pairs + pltpu.roll(pairs, width - 1, 1))
    coarse_links, coarse_diagonal = couplings(coarse_perm, (1, 2))
    coarse_inverse = 1.0 / jnp.where(coarse_perm > 0.0, coarse_diagonal, 1.0)
    first = (DAMPING * coarse_rhs) * coarse_inverse
    correction = first + (
        DAMPING * (coarse_rhs - operator(coarse_links, coarse_diagonal, first, (1, 2)))
    ) * coarse_inverse
    pick = (
        lax.broadcasted_iota(jnp.int32, (cols, cols // 2), 0)
        == 2 * lax.broadcasted_iota(jnp.int32, (cols, cols // 2), 1)
    ).astype(jnp.float32)
    odd_col = (lax.broadcasted_iota(jnp.int32, (rows, cols), 1) & 1) == 1
    for j in range(PER_STEP):
        back = (width - j * span - HALO) % width
        own = pltpu.roll(correction, back, 1)[: rows // 2, :cols]
        corr_ref[j] = jnp.dot(own, pick, precision=HI, preferred_element_type=jnp.float32)
        for k in range(cols // 128):
            piece = own[:, k * 128 : (k + 1) * 128]
            wide[k, pl.ds(0, rows // 2, stride=2), :] = piece
            wide[k, pl.ds(1, rows // 2, stride=2), :] = piece
        spread = jnp.concatenate([wide[k] for k in range(cols // 128)], axis=1)
        spread = jnp.where(odd_col, pltpu.roll(spread, 1, 1), spread)
        sol_ref[j] = pltpu.roll(current, back, 1)[:rows, :cols] + spread


def shards(source, sample_seeds, perm_levels, perm_classes):
    h = HALO
    count, rows, cols = source.shape
    ext_x = rows + 2 * h
    width = -(-(PER_STEP * (cols + 2 * h)) // 128) * 128
    rows_halo, one, two, parity = halo_pieces(source, perm_classes, h)
    smem = pl.BlockSpec(memory_space=pltpu.MemorySpace.SMEM)
    vmem = pl.BlockSpec(memory_space=pltpu.MemorySpace.VMEM)
    whole = lambda shape: pl.BlockSpec(shape, lambda s: (0,) * len(shape))
    solution_block, correction_block = pl.pallas_call(
        smooth_kernel,
        grid=(count // PER_STEP,),
        in_specs=[
            smem,
            smem,
            smem,
            pl.BlockSpec((PER_STEP, rows, cols), lambda s: (s, 0, 0)),
            whole((rows, cols)),
            vmem,
            vmem,
            vmem,
        ],
        out_specs=[
            pl.BlockSpec((PER_STEP, rows, cols), lambda s: (s, 0, 0)),
            pl.BlockSpec((PER_STEP, rows // 2, cols // 2), lambda s: (s, 0, 0)),
        ],
        out_shape=[
            jax.ShapeDtypeStruct((count, rows, cols), jnp.float32),
            jax.ShapeDtypeStruct((count, rows // 2, cols // 2), jnp.float32),
        ],
        scratch_shapes=[
            pltpu.VMEM((ext_x, width), jnp.int32),
            pltpu.VMEM((width // 128, ext_x, 128), jnp.float32),
            pltpu.VMEM((cols // 128, rows, 128), jnp.float32),
        ],
        compiler_params=pltpu.CompilerParams(dimension_semantics=("arbitrary",)),
    )(sample_seeds, perm_levels, parity, source, perm_classes, rows_halo, one, two)
    return solution_block, correction_block


def solution(mesh):
    placed = (P("sa", "gx", "gy"), P("sa"), P("sa", None), P("gx", "gy"))
    return jax.shard_map(
        shards,
        mesh=mesh,
        in_specs=placed,
        out_specs=(P("sa", "gx", "gy"), P("sa", "gx", "gy")),
        check_vma=False,
    )
```

```python
import jax
import jax.numpy as jnp
from jax import lax
from jax.experimental import pallas as pl
from jax.experimental.pallas import tpu as pltpu
from jax.sharding import PartitionSpec as P

SWEEPS = 4
DAMPING = 0.8
HALO = 8
LANE_PAD = 128
HI = lax.Precision.HIGHEST
PER_STEP = 8


def swap_exchange(last, first, axis):
    n = lax.axis_size(axis)
    even = lax.axis_index(axis) % 2 == 0
    inner = [(k, k ^ 1) for k in range(n) if k ^ 1 < n]
    outer = [(k, k + 1) for k in range(1, n - 1, 2)] + [(k + 1, k) for k in range(1, n - 1, 2)]
    one = lax.ppermute(jnp.where(even, last, first), axis, inner)
    two = lax.ppermute(jnp.where(even, first, last), axis, outer)
    return jnp.where(even, two, one), jnp.where(even, one, two)


def halo_pieces(source, classes, width):
    stack = lambda a, b: jnp.concatenate([a, (b + 1).astype(a.dtype)[None]], axis=0)
    low, high = swap_exchange(
        stack(source[:, -width:, :], classes[-width:, :]),
        stack(source[:, :width, :], classes[:width, :]),
        "gx",
    )
    rows_halo = jnp.concatenate([high, low], axis=1)

    def packed(strip, halo_strip):
        planes = jnp.concatenate([strip, halo_strip], axis=1)
        count, rows, _ = planes.shape
        flat = jnp.transpose(planes, (1, 0, 2)).reshape(rows, count * width)
        return jnp.pad(flat, ((0, 0), (0, LANE_PAD - count * width)))

    last = packed(stack(source[:, :, -width:], classes[:, -width:]), rows_halo[:, :, -width:])
    first = packed(stack(source[:, :, :width], classes[:, :width]), rows_halo[:, :, :width])
    low, high = swap_exchange(last, first, "gy")
    return rows_halo, high, low


def rolled(v, step):
    rows, cols = v.shape
    down, across = step
    return (
        pltpu.roll(v, rows - down, 0),
        pltpu.roll(v, down, 0),
        pltpu.roll(v, cols - across, 1),
        pltpu.roll(v, across, 1),
    )


def couplings(perm, step):
    down, up, right, left = rolled(perm, step)
    twice = 2.0 * perm
    south = twice * down / (perm + down)
    east = twice * right / (perm + right)
    linkage = (
        jnp.where(down > 0.0, south, twice),
        jnp.where(up > 0.0, pltpu.roll(south, step[0], 0), twice),
        jnp.where(right > 0.0, east, twice),
        jnp.where(left > 0.0, pltpu.roll(east, step[1], 1), twice),
    )
    diagonal = linkage[0] + linkage[1] + linkage[2] + linkage[3]
    return linkage, diagonal


def operator(linkage, diagonal, current, step):
    beside_all = rolled(current, step)
    return diagonal * current - (
        linkage[0] * beside_all[0]
        + linkage[1] * beside_all[1]
        + linkage[2] * beside_all[2]
        + linkage[3] * beside_all[3]
    )


def lane_tiles(high_ref, low_ref, plane):
    high = high_ref[...]
    low = low_ref[...]
    lane = lax.broadcasted_iota(jnp.int32, high.shape, 1)
    after = pltpu.roll(high, (LANE_PAD - HALO * plane) % LANE_PAD, 1)
    before = pltpu.roll(low, (LANE_PAD - HALO - HALO * plane) % LANE_PAD, 1)
    zero = jnp.zeros_like(high)
    return jnp.where(lane < HALO, after, zero), jnp.where(lane >= LANE_PAD - HALO, before, zero)


def base_layout(own, halo_rows, after, before, width):
    top = jnp.concatenate([own, halo_rows], axis=0)
    gap = jnp.zeros((top.shape[0], width - top.shape[1] - 2 * LANE_PAD), top.dtype)
    return jnp.concatenate([top, after, gap, before], axis=1)


def smooth_kernel(
    seeds_ref, levels_ref, src_ref, cls_ref, rows_ref, high_ref, low_ref,
    sol_ref, corr_ref, codes_pk, spare, wide,
):
    s = pl.program_id(0)
    count = PER_STEP * pl.num_programs(0)
    rows, cols = sol_ref.shape[1], sol_ref.shape[2]
    ext_x, width = codes_pk.shape
    span = cols + 2 * HALO
    lane = lax.broadcasted_iota(jnp.int32, (ext_x, width), 1)

    def packed(pieces):
        out = None
        for j, piece in enumerate(pieces):
            moved = pltpu.roll(piece, (j * span + HALO) % width, 1)
            out = moved if out is None else jnp.where(lane >= j * span, moved, out)
        return out

    @pl.when(s == 0)
    def _():
        after, before = lane_tiles(high_ref, low_ref, count)
        own = base_layout(
            cls_ref[...] + 1, rows_ref[count].astype(jnp.int32),
            after.astype(jnp.int32), before.astype(jnp.int32), width,
        )
        codes_pk[...] = packed([own] * PER_STEP)

    pieces = []
    for j in range(PER_STEP):
        plane = PER_STEP * s + j
        after, before = lane_tiles(high_ref, low_ref, plane)
        pieces.append(base_layout(src_ref[j], rows_ref[plane], after, before, width))
    source = packed(pieces)
    codes = codes_pk[...]
    valid = codes > 0
    classes = (codes - 1).reshape(ext_x // 8, 8, width)
    row_lane = lax.broadcasted_iota(jnp.int32, (8, width), 1)
    level = []
    for category in range(levels_ref.shape[1]):
        row = jnp.full((8, width), levels_ref[seeds_ref[PER_STEP * s], category], jnp.float32)
        for j in range(1, PER_STEP):
            pick_level = levels_ref[seeds_ref[PER_STEP * s + j], category]
            row = jnp.where(row_lane >= j * span, pick_level, row)
        level.append(row[None])
    bit0 = (classes & 1) != 0
    bit1 = (classes & 2) != 0
    bit2 = (classes & 4) != 0
    low = jnp.where(bit1, jnp.where(bit0, level[3], level[2]), jnp.where(bit0, level[1], level[0]))
    high = jnp.where(bit1, jnp.where(bit0, level[7], level[6]), jnp.where(bit0, level[5], level[4]))
    perm = jnp.where(valid, jnp.where(bit2, high, low).reshape(ext_x, width), 0.0)
    linkage, diagonal = couplings(perm, (1, 1))
    inverse = DAMPING / jnp.where(valid, diagonal, 1.0)
    current = source * inverse
    for sweep_index in range(SWEEPS):
        residual = source - operator(linkage, diagonal, current, (1, 1))
        if sweep_index + 1 < SWEEPS:
            current = current + residual * inverse

    def even_rows(v):
        parts = []
        for k in range(width // 128):
            spare[k] = v[:, k * 128 : (k + 1) * 128]
            parts.append(spare[k, pl.ds(0, ext_x // 2, stride=2), :])
        return jnp.concatenate(parts, axis=1)

    pairs = residual + pltpu.roll(residual, ext_x - 1, 0)
    coarse_rhs = even_rows(pairs + pltpu.roll(pairs, width - 1, 1))
    pairs = perm + pltpu.roll(perm, ext_x - 1, 0)
    coarse_perm = 0.25 * even_rows(pairs + pltpu.roll(pairs, width - 1, 1))
    coarse_links, coarse_diagonal = couplings(coarse_perm, (1, 2))
    coarse_inverse = DAMPING / jnp.where(coarse_perm > 0.0, coarse_diagonal, 1.0)
    first = coarse_rhs * coarse_inverse
    correction = first + (
        coarse_rhs - operator(coarse_links, coarse_diagonal, first, (1, 2))
    ) * coarse_inverse
    pick = (
        lax.broadcasted_iota(jnp.int32, (cols, cols // 2), 0)
        == 2 * lax.broadcasted_iota(jnp.int32, (cols, cols // 2), 1)
    ).astype(jnp.float32)
    odd_col = (lax.broadcasted_iota(jnp.int32, (rows, cols), 1) & 1) == 1
    for j in range(PER_STEP):
        back = (width - j * span - HALO) % width
        own = pltpu.roll(correction, back, 1)[: rows // 2, :cols]
        corr_ref[j] = jnp.dot(own, pick, precision=HI, preferred_element_type=jnp.float32)
        for k in range(cols // 128):
            piece = own[:, k * 128 : (k + 1) * 128]
            wide[k, pl.ds(0, rows // 2, stride=2), :] = piece
            wide[k, pl.ds(1, rows // 2, stride=2), :] = piece
        spread = jnp.concatenate([wide[k] for k in range(cols // 128)], axis=1)
        spread = jnp.where(odd_col, pltpu.roll(spread, 1, 1), spread)
        sol_ref[j] = pltpu.roll(current, back, 1)[:rows, :cols] + spread


def shards(source, sample_seeds, perm_levels, perm_classes):
    h = HALO
    count, rows, cols = source.shape
    ext_x = rows + 2 * h
    width = -(-(PER_STEP * (cols + 2 * h)) // 128) * 128
    rows_halo, high, low = halo_pieces(source, perm_classes, h)
    smem = pl.BlockSpec(memory_space=pltpu.MemorySpace.SMEM)
    vmem = pl.BlockSpec(memory_space=pltpu.MemorySpace.VMEM)
    whole = lambda shape: pl.BlockSpec(shape, lambda s: (0,) * len(shape))
    solution_block, correction_block = pl.pallas_call(
        smooth_kernel,
        grid=(count // PER_STEP,),
        in_specs=[
            smem,
            smem,
            pl.BlockSpec((PER_STEP, rows, cols), lambda s: (s, 0, 0)),
            whole((rows, cols)),
            vmem,
            vmem,
            vmem,
        ],
        out_specs=[
            pl.BlockSpec((PER_STEP, rows, cols), lambda s: (s, 0, 0)),
            pl.BlockSpec((PER_STEP, rows // 2, cols // 2), lambda s: (s, 0, 0)),
        ],
        out_shape=[
            jax.ShapeDtypeStruct((count, rows, cols), jnp.float32),
            jax.ShapeDtypeStruct((count, rows // 2, cols // 2), jnp.float32),
        ],
        scratch_shapes=[
            pltpu.VMEM((ext_x, width), jnp.int32),
            pltpu.VMEM((width // 128, ext_x, 128), jnp.float32),
            pltpu.VMEM((cols // 128, rows, 128), jnp.float32),
        ],
        compiler_params=pltpu.CompilerParams(dimension_semantics=("arbitrary",)),
    )(sample_seeds, perm_levels, source, perm_classes, rows_halo, high, low)
    return solution_block, correction_block


def solution(mesh):
    placed = (P("sa", "gx", "gy"), P("sa"), P("sa", None), P("gx", "gy"))
    return jax.shard_map(
        shards,
        mesh=mesh,
        in_specs=placed,
        out_specs=(P("sa", "gx", "gy"), P("sa", "gx", "gy")),
        check_vma=False,
    )
```

```python
import jax
import jax.numpy as jnp
from jax import lax
from jax.experimental import pallas as pl
from jax.experimental.pallas import tpu as pltpu
from jax.sharding import PartitionSpec as P

SWEEPS = 4
DAMPING = 0.8
HALO = 8
LANE_PAD = 128
HI = lax.Precision.HIGHEST
PER_STEP = 8


def swap_exchange(last, first, axis):
    n = lax.axis_size(axis)
    even = lax.axis_index(axis) % 2 == 0
    inner = [(k, k ^ 1) for k in range(n) if k ^ 1 < n]
    outer = [(k, k + 1) for k in range(1, n - 1, 2)] + [(k + 1, k) for k in range(1, n - 1, 2)]
    one = lax.ppermute(jnp.where(even, last, first), axis, inner)
    two = lax.ppermute(jnp.where(even, first, last), axis, outer)
    return jnp.where(even, two, one), jnp.where(even, one, two)


def halo_pieces(source, classes, width):
    stack = lambda a, b: jnp.concatenate([a, (b + 1).astype(a.dtype)[None]], axis=0)
    low, high = swap_exchange(
        stack(source[:, -width:, :], classes[-width:, :]),
        stack(source[:, :width, :], classes[:width, :]),
        "gx",
    )
    rows_halo = jnp.concatenate([high, low], axis=1)

    def packed(strip, halo_strip):
        planes = jnp.concatenate([strip, halo_strip], axis=1)
        count, rows, _ = planes.shape
        flat = jnp.transpose(planes, (1, 0, 2)).reshape(rows, count * width)
        return jnp.pad(flat, ((0, 0), (0, LANE_PAD - count * width)))

    last = packed(stack(source[:, :, -width:], classes[:, -width:]), rows_halo[:, :, -width:])
    first = packed(stack(source[:, :, :width], classes[:, :width]), rows_halo[:, :, :width])
    low, high = swap_exchange(last, first, "gy")
    return rows_halo, high, low


def rolled(v, step):
    rows, cols = v.shape
    down, across = step
    return (
        pltpu.roll(v, rows - down, 0),
        pltpu.roll(v, down, 0),
        pltpu.roll(v, cols - across, 1),
        pltpu.roll(v, across, 1),
    )


def couplings(perm, step):
    down, up, right, left = rolled(perm, step)
    twice = 2.0 * perm
    south = twice * down / (perm + down)
    east = twice * right / (perm + right)
    linkage = (
        jnp.where(down > 0.0, south, twice),
        jnp.where(up > 0.0, pltpu.roll(south, step[0], 0), twice),
        jnp.where(right > 0.0, east, twice),
        jnp.where(left > 0.0, pltpu.roll(east, step[1], 1), twice),
    )
    diagonal = linkage[0] + linkage[1] + linkage[2] + linkage[3]
    return linkage, diagonal


def operator(linkage, diagonal, current, step):
    beside_all = rolled(current, step)
    return diagonal * current - (
        linkage[0] * beside_all[0]
        + linkage[1] * beside_all[1]
        + linkage[2] * beside_all[2]
        + linkage[3] * beside_all[3]
    )


def lane_tiles(high_ref, low_ref, plane):
    high = high_ref[...]
    low = low_ref[...]
    lane = lax.broadcasted_iota(jnp.int32, high.shape, 1)
    after = pltpu.roll(high, (LANE_PAD - HALO * plane) % LANE_PAD, 1)
    before = pltpu.roll(low, (LANE_PAD - HALO - HALO * plane) % LANE_PAD, 1)
    zero = jnp.zeros_like(high)
    return jnp.where(lane < HALO, after, zero), jnp.where(lane >= LANE_PAD - HALO, before, zero)


def base_layout(own, halo_rows, after, before, width):
    top = jnp.concatenate([own, halo_rows], axis=0)
    gap = jnp.zeros((top.shape[0], width - top.shape[1] - 2 * LANE_PAD), top.dtype)
    return jnp.concatenate([top, after, gap, before], axis=1)


def smooth_kernel(
    seeds_ref, levels_ref, src_ref, cls_ref, rows_ref, high_ref, low_ref,
    sol_ref, corr_ref, codes_pk, spare, wide, sol_v, corr_v, written,
):
    s = pl.program_id(0)
    count = PER_STEP * pl.num_programs(0)
    rows, cols = sol_ref.shape[1], sol_ref.shape[2]
    ext_x, width = codes_pk.shape
    span = cols + 2 * HALO
    lane = lax.broadcasted_iota(jnp.int32, (ext_x, width), 1)

    def packed(pieces):
        out = None
        for j, piece in enumerate(pieces):
            moved = pltpu.roll(piece, (j * span + HALO) % width, 1)
            out = moved if out is None else jnp.where(lane >= j * span, moved, out)
        return out

    @pl.when(s == 0)
    def _():
        after, before = lane_tiles(high_ref, low_ref, count)
        own = base_layout(
            cls_ref[...] + 1, rows_ref[count].astype(jnp.int32),
            after.astype(jnp.int32), before.astype(jnp.int32), width,
        )
        codes_pk[...] = packed([own] * PER_STEP)

    pieces = []
    for j in range(PER_STEP):
        plane = PER_STEP * s + j
        after, before = lane_tiles(high_ref, low_ref, plane)
        pieces.append(base_layout(src_ref[j], rows_ref[plane], after, before, width))
    source = packed(pieces)
    codes = codes_pk[...]
    valid = codes > 0
    classes = (codes - 1).reshape(ext_x // 8, 8, width)
    row_lane = lax.broadcasted_iota(jnp.int32, (8, width), 1)
    level = []
    for category in range(levels_ref.shape[1]):
        row = jnp.full((8, width), levels_ref[seeds_ref[PER_STEP * s], category], jnp.float32)
        for j in range(1, PER_STEP):
            pick_level = levels_ref[seeds_ref[PER_STEP * s + j], category]
            row = jnp.where(row_lane >= j * span, pick_level, row)
        level.append(row[None])
    bit0 = (classes & 1) != 0
    bit1 = (classes & 2) != 0
    bit2 = (classes & 4) != 0
    low = jnp.where(bit1, jnp.where(bit0, level[3], level[2]), jnp.where(bit0, level[1], level[0]))
    high = jnp.where(bit1, jnp.where(bit0, level[7], level[6]), jnp.where(bit0, level[5], level[4]))
    perm = jnp.where(valid, jnp.where(bit2, high, low).reshape(ext_x, width), 0.0)
    linkage, diagonal = couplings(perm, (1, 1))
    inverse = 1.0 / jnp.where(valid, diagonal, 1.0)
    current = (DAMPING * source) * inverse
    for sweep_index in range(SWEEPS):
        residual = source - operator(linkage, diagonal, current, (1, 1))
        if sweep_index + 1 < SWEEPS:
            current = current + (DAMPING * residual) * inverse

    def even_rows(v):
        parts = []
        for k in range(width // 128):
            spare[k] = v[:, k * 128 : (k + 1) * 128]
            parts.append(spare[k, pl.ds(0, ext_x // 2, stride=2), :])
        return jnp.concatenate(parts, axis=1)

    pairs = residual + pltpu.roll(residual, ext_x - 1, 0)
    coarse_rhs = even_rows(pairs + pltpu.roll(pairs, width - 1, 1))
    pairs = perm + pltpu.roll(perm, ext_x - 1, 0)
    coarse_perm = 0.25 * even_rows(pairs + pltpu.roll(pairs, width - 1, 1))
    coarse_links, coarse_diagonal = couplings(coarse_perm, (1, 2))
    coarse_inverse = 1.0 / jnp.where(coarse_perm > 0.0, coarse_diagonal, 1.0)
    first = (DAMPING * coarse_rhs) * coarse_inverse
    correction = first + (
        DAMPING * (coarse_rhs - operator(coarse_links, coarse_diagonal, first, (1, 2)))
    ) * coarse_inverse
    pick = (
        lax.broadcasted_iota(jnp.int32, (cols, cols // 2), 0)
        == 2 * lax.broadcasted_iota(jnp.int32, (cols, cols // 2), 1)
    ).astype(jnp.float32)
    odd_col = (lax.broadcasted_iota(jnp.int32, (rows, cols), 1) & 1) == 1
    copies = []
    for j in range(PER_STEP):
        back = (width - j * span - HALO) % width
        own = pltpu.roll(correction, back, 1)[: rows // 2, :cols]
        corr_v[j] = jnp.dot(own, pick, precision=HI, preferred_element_type=jnp.float32)
        copies.append(
            pltpu.make_async_copy(corr_v.at[j], corr_ref.at[PER_STEP * s + j], written.at[0, j])
        )
        copies[-1].start()
        for k in range(cols // 128):
            piece = own[:, k * 128 : (k + 1) * 128]
            wide[k, pl.ds(0, rows // 2, stride=2), :] = piece
            wide[k, pl.ds(1, rows // 2, stride=2), :] = piece
        spread = jnp.concatenate([wide[k] for k in range(cols // 128)], axis=1)
        spread = jnp.where(odd_col, pltpu.roll(spread, 1, 1), spread)
        sol_v[j] = pltpu.roll(current, back, 1)[:rows, :cols] + spread
        copies.append(
            pltpu.make_async_copy(sol_v.at[j], sol_ref.at[PER_STEP * s + j], written.at[1, j])
        )
        copies[-1].start()
    for copy in copies:
        copy.wait()


def shards(source, sample_seeds, perm_levels, perm_classes):
    h = HALO
    count, rows, cols = source.shape
    ext_x = rows + 2 * h
    width = -(-(PER_STEP * (cols + 2 * h)) // 128) * 128
    rows_halo, high, low = halo_pieces(source, perm_classes, h)
    smem = pl.BlockSpec(memory_space=pltpu.MemorySpace.SMEM)
    vmem = pl.BlockSpec(memory_space=pltpu.MemorySpace.VMEM)
    whole = lambda shape: pl.BlockSpec(shape, lambda s: (0,) * len(shape))
    solution_block, correction_block = pl.pallas_call(
        smooth_kernel,
        grid=(count // PER_STEP,),
        in_specs=[
            smem,
            smem,
            pl.BlockSpec((PER_STEP, rows, cols), lambda s: (s, 0, 0)),
            whole((rows, cols)),
            vmem,
            vmem,
            vmem,
        ],
        out_specs=[
            pl.BlockSpec(memory_space=pl.ANY),
            pl.BlockSpec(memory_space=pl.ANY),
        ],
        out_shape=[
            jax.ShapeDtypeStruct((count, rows, cols), jnp.float32),
            jax.ShapeDtypeStruct((count, rows // 2, cols // 2), jnp.float32),
        ],
        scratch_shapes=[
            pltpu.VMEM((ext_x, width), jnp.int32),
            pltpu.VMEM((width // 128, ext_x, 128), jnp.float32),
            pltpu.VMEM((cols // 128, rows, 128), jnp.float32),
            pltpu.VMEM((PER_STEP, rows, cols), jnp.float32),
            pltpu.VMEM((PER_STEP, rows // 2, cols // 2), jnp.float32),
            pltpu.SemaphoreType.DMA((2, PER_STEP)),
        ],
        compiler_params=pltpu.CompilerParams(dimension_semantics=("arbitrary",)),
    )(sample_seeds, perm_levels, source, perm_classes, rows_halo, high, low)
    return solution_block, correction_block


def solution(mesh):
    placed = (P("sa", "gx", "gy"), P("sa"), P("sa", None), P("gx", "gy"))
    return jax.shard_map(
        shards,
        mesh=mesh,
        in_specs=placed,
        out_specs=(P("sa", "gx", "gy"), P("sa", "gx", "gy")),
        check_vma=False,
    )
```

```python
import jax
import jax.numpy as jnp
from jax import lax
from jax.experimental import pallas as pl
from jax.experimental.pallas import tpu as pltpu
from jax.sharding import PartitionSpec as P

SWEEPS = 4
DAMPING = 0.8
HALO = 8
LANE_PAD = 128
HI = lax.Precision.HIGHEST
PER_STEP = 8


def swap_exchange(last, first, axis):
    n = lax.axis_size(axis)
    even = lax.axis_index(axis) % 2 == 0
    inner = [(k, k ^ 1) for k in range(n) if k ^ 1 < n]
    outer = [(k, k + 1) for k in range(1, n - 1, 2)] + [(k + 1, k) for k in range(1, n - 1, 2)]
    one = lax.ppermute(jnp.where(even, last, first), axis, inner)
    two = lax.ppermute(jnp.where(even, first, last), axis, outer)
    return jnp.where(even, two, one), jnp.where(even, one, two)


def halo_pieces(source, classes, width):
    stack = lambda a, b: jnp.concatenate([a, (b + 1).astype(a.dtype)[None]], axis=0)
    low, high = swap_exchange(
        stack(source[:, -width:, :], classes[-width:, :]),
        stack(source[:, :width, :], classes[:width, :]),
        "gx",
    )
    rows_halo = jnp.concatenate([high, low], axis=1)

    def packed(strip, halo_strip):
        planes = jnp.concatenate([strip, halo_strip], axis=1)
        count, rows, _ = planes.shape
        flat = jnp.transpose(planes, (1, 0, 2)).reshape(rows, count * width)
        return jnp.pad(flat, ((0, 0), (0, LANE_PAD - count * width)))

    last = packed(stack(source[:, :, -width:], classes[:, -width:]), rows_halo[:, :, -width:])
    first = packed(stack(source[:, :, :width], classes[:, :width]), rows_halo[:, :, :width])
    low, high = swap_exchange(last, first, "gy")
    return rows_halo, high, low


def rolled(v, step):
    rows, cols = v.shape
    down, across = step
    return (
        pltpu.roll(v, rows - down, 0),
        pltpu.roll(v, down, 0),
        pltpu.roll(v, cols - across, 1),
        pltpu.roll(v, across, 1),
    )


def couplings(perm, step):
    down, up, right, left = rolled(perm, step)
    twice = 2.0 * perm
    south = twice * down / (perm + down)
    east = twice * right / (perm + right)
    linkage = (
        jnp.where(down > 0.0, south, twice),
        jnp.where(up > 0.0, pltpu.roll(south, step[0], 0), twice),
        jnp.where(right > 0.0, east, twice),
        jnp.where(left > 0.0, pltpu.roll(east, step[1], 1), twice),
    )
    diagonal = linkage[0] + linkage[1] + linkage[2] + linkage[3]
    return linkage, diagonal


def operator(linkage, diagonal, current, step):
    beside_all = rolled(current, step)
    return diagonal * current - (
        linkage[0] * beside_all[0]
        + linkage[1] * beside_all[1]
        + linkage[2] * beside_all[2]
        + linkage[3] * beside_all[3]
    )


def lane_tiles(high_ref, low_ref, plane):
    high = high_ref[...]
    low = low_ref[...]
    lane = lax.broadcasted_iota(jnp.int32, high.shape, 1)
    after = pltpu.roll(high, (LANE_PAD - HALO * plane) % LANE_PAD, 1)
    before = pltpu.roll(low, (LANE_PAD - HALO - HALO * plane) % LANE_PAD, 1)
    zero = jnp.zeros_like(high)
    return jnp.where(lane < HALO, after, zero), jnp.where(lane >= LANE_PAD - HALO, before, zero)


def base_layout(own, halo_rows, after, before, width):
    top = jnp.concatenate([own, halo_rows], axis=0)
    gap = jnp.zeros((top.shape[0], width - top.shape[1] - 2 * LANE_PAD), top.dtype)
    return jnp.concatenate([top, after, gap, before], axis=1)


def smooth_kernel(
    seeds_ref, levels_ref, src_ref, cls_ref, rows_ref, high_ref, low_ref,
    sol_ref, corr_ref, codes_pk, spare, wide, sol_v, corr_v, written,
):
    s = pl.program_id(0)
    count = PER_STEP * pl.num_programs(0)
    rows, cols = sol_ref.shape[1], sol_ref.shape[2]
    ext_x, width = codes_pk.shape
    span = cols + 2 * HALO
    lane = lax.broadcasted_iota(jnp.int32, (ext_x, width), 1)

    def packed(pieces):
        moved = [pltpu.roll(piece, (j * span + HALO) % width, 1) for j, piece in enumerate(pieces)]
        chunk_lane = lax.broadcasted_iota(jnp.int32, (ext_x, 128), 1)
        chunks = []
        for low_edge in range(0, width, 128):
            first = min(low_edge // span, len(pieces) - 1)
            out = moved[first][:, low_edge : low_edge + 128]
            for j in range(first + 1, len(pieces)):
                if j * span < low_edge + 128:
                    out = jnp.where(
                        chunk_lane >= j * span - low_edge, moved[j][:, low_edge : low_edge + 128], out
                    )
            chunks.append(out)
        return jnp.concatenate(chunks, axis=1)

    @pl.when(s == 0)
    def _():
        after, before = lane_tiles(high_ref, low_ref, count)
        own = base_layout(
            cls_ref[...] + 1, rows_ref[count].astype(jnp.int32),
            after.astype(jnp.int32), before.astype(jnp.int32), width,
        )
        codes_pk[...] = packed([own] * PER_STEP)

    pieces = []
    for j in range(PER_STEP):
        plane = PER_STEP * s + j
        after, before = lane_tiles(high_ref, low_ref, plane)
        pieces.append(base_layout(src_ref[j], rows_ref[plane], after, before, width))
    source = packed(pieces)
    codes = codes_pk[...]
    valid = codes > 0
    classes = (codes - 1).reshape(ext_x // 8, 8, width)
    row_lane = lax.broadcasted_iota(jnp.int32, (8, width), 1)
    level = []
    for category in range(levels_ref.shape[1]):
        row = jnp.full((8, width), levels_ref[seeds_ref[PER_STEP * s], category], jnp.float32)
        for j in range(1, PER_STEP):
            pick_level = levels_ref[seeds_ref[PER_STEP * s + j], category]
            row = jnp.where(row_lane >= j * span, pick_level, row)
        level.append(row[None])
    bit0 = (classes & 1) != 0
    bit1 = (classes & 2) != 0
    bit2 = (classes & 4) != 0
    low = jnp.where(bit1, jnp.where(bit0, level[3], level[2]), jnp.where(bit0, level[1], level[0]))
    high = jnp.where(bit1, jnp.where(bit0, level[7], level[6]), jnp.where(bit0, level[5], level[4]))
    perm = jnp.where(valid, jnp.where(bit2, high, low).reshape(ext_x, width), 0.0)
    linkage, diagonal = couplings(perm, (1, 1))
    inverse = DAMPING / jnp.where(valid, diagonal, 1.0)
    current = source * inverse
    for sweep_index in range(SWEEPS):
        residual = source - operator(linkage, diagonal, current, (1, 1))
        if sweep_index + 1 < SWEEPS:
            current = current + residual * inverse

    def even_rows(v):
        parts = []
        for k in range(width // 128):
            spare[k] = v[:, k * 128 : (k + 1) * 128]
            parts.append(spare[k, pl.ds(0, ext_x // 2, stride=2), :])
        return jnp.concatenate(parts, axis=1)

    pairs = residual + pltpu.roll(residual, ext_x - 1, 0)
    coarse_rhs = even_rows(pairs + pltpu.roll(pairs, width - 1, 1))
    pairs = perm + pltpu.roll(perm, ext_x - 1, 0)
    coarse_perm = 0.25 * even_rows(pairs + pltpu.roll(pairs, width - 1, 1))
    coarse_links, coarse_diagonal = couplings(coarse_perm, (1, 2))
    coarse_inverse = DAMPING / jnp.where(coarse_perm > 0.0, coarse_diagonal, 1.0)
    first = coarse_rhs * coarse_inverse
    correction = first + (
        coarse_rhs - operator(coarse_links, coarse_diagonal, first, (1, 2))
    ) * coarse_inverse
    pick = (
        lax.broadcasted_iota(jnp.int32, (cols, cols // 2), 0)
        == 2 * lax.broadcasted_iota(jnp.int32, (cols, cols // 2), 1)
    ).astype(jnp.float32)
    odd_col = (lax.broadcasted_iota(jnp.int32, (rows, cols), 1) & 1) == 1
    copies = []
    for j in range(PER_STEP):
        back = (width - j * span - HALO) % width
        own = pltpu.roll(correction, back, 1)[: rows // 2, :cols]
        corr_v[j] = jnp.dot(own, pick, precision=HI, preferred_element_type=jnp.float32)
        copies.append(
            pltpu.make_async_copy(corr_v.at[j], corr_ref.at[PER_STEP * s + j], written.at[0, j])
        )
        copies[-1].start()
        for k in range(cols // 128):
            piece = own[:, k * 128 : (k + 1) * 128]
            wide[k, pl.ds(0, rows // 2, stride=2), :] = piece
            wide[k, pl.ds(1, rows // 2, stride=2), :] = piece
        spread = jnp.concatenate([wide[k] for k in range(cols // 128)], axis=1)
        spread = jnp.where(odd_col, pltpu.roll(spread, 1, 1), spread)
        sol_v[j] = pltpu.roll(current, back, 1)[:rows, :cols] + spread
        copies.append(
            pltpu.make_async_copy(sol_v.at[j], sol_ref.at[PER_STEP * s + j], written.at[1, j])
        )
        copies[-1].start()
    for copy in copies:
        copy.wait()


def shards(source, sample_seeds, perm_levels, perm_classes):
    h = HALO
    count, rows, cols = source.shape
    ext_x = rows + 2 * h
    width = -(-(PER_STEP * (cols + 2 * h)) // 128) * 128
    rows_halo, high, low = halo_pieces(source, perm_classes, h)
    smem = pl.BlockSpec(memory_space=pltpu.MemorySpace.SMEM)
    vmem = pl.BlockSpec(memory_space=pltpu.MemorySpace.VMEM)
    whole = lambda shape: pl.BlockSpec(shape, lambda s: (0,) * len(shape))
    solution_block, correction_block = pl.pallas_call(
        smooth_kernel,
        grid=(count // PER_STEP,),
        in_specs=[
            smem,
            smem,
            pl.BlockSpec((PER_STEP, rows, cols), lambda s: (s, 0, 0)),
            whole((rows, cols)),
            vmem,
            vmem,
            vmem,
        ],
        out_specs=[
            pl.BlockSpec(memory_space=pl.ANY),
            pl.BlockSpec(memory_space=pl.ANY),
        ],
        out_shape=[
            jax.ShapeDtypeStruct((count, rows, cols), jnp.float32),
            jax.ShapeDtypeStruct((count, rows // 2, cols // 2), jnp.float32),
        ],
        scratch_shapes=[
            pltpu.VMEM((ext_x, width), jnp.int32),
            pltpu.VMEM((width // 128, ext_x, 128), jnp.float32),
            pltpu.VMEM((cols // 128, rows, 128), jnp.float32),
            pltpu.VMEM((PER_STEP, rows, cols), jnp.float32),
            pltpu.VMEM((PER_STEP, rows // 2, cols // 2), jnp.float32),
            pltpu.SemaphoreType.DMA((2, PER_STEP)),
        ],
        compiler_params=pltpu.CompilerParams(dimension_semantics=("arbitrary",)),
    )(sample_seeds, perm_levels, source, perm_classes, rows_halo, high, low)
    return solution_block, correction_block


def solution(mesh):
    placed = (P("sa", "gx", "gy"), P("sa"), P("sa", None), P("gx", "gy"))
    return jax.shard_map(
        shards,
        mesh=mesh,
        in_specs=placed,
        out_specs=(P("sa", "gx", "gy"), P("sa", "gx", "gy")),
        check_vma=False,
    )
```

```python
import jax
import jax.numpy as jnp
from jax import lax
from jax.experimental import pallas as pl
from jax.experimental.pallas import tpu as pltpu
from jax.sharding import PartitionSpec as P

SWEEPS = 4
DAMPING = 0.8
HALO = 8
LANE_PAD = 128
HI = lax.Precision.HIGHEST
PER_STEP = 8


def swap_exchange(last, first, axis):
    n = lax.axis_size(axis)
    even = lax.axis_index(axis) % 2 == 0
    inner = [(k, k ^ 1) for k in range(n) if k ^ 1 < n]
    outer = [(k, k + 1) for k in range(1, n - 1, 2)] + [(k + 1, k) for k in range(1, n - 1, 2)]
    two = lax.ppermute(jnp.where(even, first, last), axis, outer)
    one = lax.ppermute(jnp.where(even, last, first), axis, inner)
    return jnp.where(even, two, one), jnp.where(even, one, two)


def halo_pieces(source, classes, width):
    stack = lambda a, b: jnp.concatenate([a, (b + 1).astype(a.dtype)[None]], axis=0)
    low, high = swap_exchange(
        stack(source[:, -width:, :], classes[-width:, :]),
        stack(source[:, :width, :], classes[:width, :]),
        "gx",
    )
    rows_halo = jnp.concatenate([high, low], axis=1)

    def packed(strip, halo_strip):
        planes = jnp.concatenate([strip, halo_strip], axis=1)
        count, rows, _ = planes.shape
        flat = jnp.transpose(planes, (1, 0, 2)).reshape(rows, count * width)
        return jnp.pad(flat, ((0, 0), (0, LANE_PAD - count * width)))

    last = packed(stack(source[:, :, -width:], classes[:, -width:]), rows_halo[:, :, -width:])
    first = packed(stack(source[:, :, :width], classes[:, :width]), rows_halo[:, :, :width])
    low, high = swap_exchange(last, first, "gy")
    return rows_halo, high, low


def rolled(v, step):
    rows, cols = v.shape
    down, across = step
    return (
        pltpu.roll(v, rows - down, 0),
        pltpu.roll(v, down, 0),
        pltpu.roll(v, cols - across, 1),
        pltpu.roll(v, across, 1),
    )


def couplings(perm, step):
    down, up, right, left = rolled(perm, step)
    twice = 2.0 * perm
    south = twice * down / (perm + down)
    east = twice * right / (perm + right)
    linkage = (
        jnp.where(down > 0.0, south, twice),
        jnp.where(up > 0.0, pltpu.roll(south, step[0], 0), twice),
        jnp.where(right > 0.0, east, twice),
        jnp.where(left > 0.0, pltpu.roll(east, step[1], 1), twice),
    )
    diagonal = linkage[0] + linkage[1] + linkage[2] + linkage[3]
    return linkage, diagonal


def operator(linkage, diagonal, current, step):
    beside_all = rolled(current, step)
    return diagonal * current - (
        linkage[0] * beside_all[0]
        + linkage[1] * beside_all[1]
        + linkage[2] * beside_all[2]
        + linkage[3] * beside_all[3]
    )


def lane_tiles(high_ref, low_ref, plane):
    high = high_ref[...]
    low = low_ref[...]
    lane = lax.broadcasted_iota(jnp.int32, high.shape, 1)
    after = pltpu.roll(high, (LANE_PAD - HALO * plane) % LANE_PAD, 1)
    before = pltpu.roll(low, (LANE_PAD - HALO - HALO * plane) % LANE_PAD, 1)
    zero = jnp.zeros_like(high)
    return jnp.where(lane < HALO, after, zero), jnp.where(lane >= LANE_PAD - HALO, before, zero)


def base_layout(own, halo_rows, after, before, width):
    top = jnp.concatenate([own, halo_rows], axis=0)
    gap = jnp.zeros((top.shape[0], width - top.shape[1] - 2 * LANE_PAD), top.dtype)
    return jnp.concatenate([top, after, gap, before], axis=1)


def smooth_kernel(
    seeds_ref, levels_ref, src_ref, cls_ref, rows_ref, high_ref, low_ref,
    sol_ref, corr_ref, codes_pk, spare, wide,
):
    s = pl.program_id(0)
    count = PER_STEP * pl.num_programs(0)
    rows, cols = sol_ref.shape[1], sol_ref.shape[2]
    ext_x, width = codes_pk.shape
    span = cols + 2 * HALO
    lane = lax.broadcasted_iota(jnp.int32, (ext_x, width), 1)

    def packed(pieces):
        out = None
        for j, piece in enumerate(pieces):
            moved = pltpu.roll(piece, (j * span + HALO) % width, 1)
            out = moved if out is None else jnp.where(lane >= j * span, moved, out)
        return out

    @pl.when(s == 0)
    def _():
        after, before = lane_tiles(high_ref, low_ref, count)
        own = base_layout(
            cls_ref[...] + 1, rows_ref[count].astype(jnp.int32),
            after.astype(jnp.int32), before.astype(jnp.int32), width,
        )
        codes_pk[...] = packed([own] * PER_STEP)

    pieces = []
    for j in range(PER_STEP):
        plane = PER_STEP * s + j
        after, before = lane_tiles(high_ref, low_ref, plane)
        pieces.append(base_layout(src_ref[j], rows_ref[plane], after, before, width))
    source = packed(pieces)
    codes = codes_pk[...]
    valid = codes > 0
    classes = (codes - 1).reshape(ext_x // 8, 8, width)
    row_lane = lax.broadcasted_iota(jnp.int32, (8, width), 1)
    level = []
    for category in range(levels_ref.shape[1]):
        row = jnp.full((8, width), levels_ref[seeds_ref[PER_STEP * s], category], jnp.float32)
        for j in range(1, PER_STEP):
            pick_level = levels_ref[seeds_ref[PER_STEP * s + j], category]
            row = jnp.where(row_lane >= j * span, pick_level, row)
        level.append(row[None])
    bit0 = (classes & 1) != 0
    bit1 = (classes & 2) != 0
    bit2 = (classes & 4) != 0
    low = jnp.where(bit1, jnp.where(bit0, level[3], level[2]), jnp.where(bit0, level[1], level[0]))
    high = jnp.where(bit1, jnp.where(bit0, level[7], level[6]), jnp.where(bit0, level[5], level[4]))
    perm = jnp.where(valid, jnp.where(bit2, high, low).reshape(ext_x, width), 0.0)
    linkage, diagonal = couplings(perm, (1, 1))
    inverse = 1.0 / jnp.where(valid, diagonal, 1.0)
    current = (DAMPING * source) * inverse
    for sweep_index in range(SWEEPS):
        residual = source - operator(linkage, diagonal, current, (1, 1))
        if sweep_index + 1 < SWEEPS:
            current = current + (DAMPING * residual) * inverse

    def even_rows(v):
        parts = []
        for k in range(width // 128):
            spare[k] = v[:, k * 128 : (k + 1) * 128]
            parts.append(spare[k, pl.ds(0, ext_x // 2, stride=2), :])
        return jnp.concatenate(parts, axis=1)

    pairs = residual + pltpu.roll(residual, ext_x - 1, 0)
    coarse_rhs = even_rows(pairs + pltpu.roll(pairs, width - 1, 1))
    pairs = perm + pltpu.roll(perm, ext_x - 1, 0)
    coarse_perm = 0.25 * even_rows(pairs + pltpu.roll(pairs, width - 1, 1))
    coarse_links, coarse_diagonal = couplings(coarse_perm, (1, 2))
    coarse_inverse = 1.0 / jnp.where(coarse_perm > 0.0, coarse_diagonal, 1.0)
    first = (DAMPING * coarse_rhs) * coarse_inverse
    correction = first + (
        DAMPING * (coarse_rhs - operator(coarse_links, coarse_diagonal, first, (1, 2)))
    ) * coarse_inverse
    pick = (
        lax.broadcasted_iota(jnp.int32, (cols, cols // 2), 0)
        == 2 * lax.broadcasted_iota(jnp.int32, (cols, cols // 2), 1)
    ).astype(jnp.float32)
    odd_col = (lax.broadcasted_iota(jnp.int32, (rows, cols), 1) & 1) == 1
    for j in range(PER_STEP):
        back = (width - j * span - HALO) % width
        own = pltpu.roll(correction, back, 1)[: rows // 2, :cols]
        corr_ref[j] = jnp.dot(own, pick, precision=HI, preferred_element_type=jnp.float32)
        for k in range(cols // 128):
            piece = own[:, k * 128 : (k + 1) * 128]
            wide[k, pl.ds(0, rows // 2, stride=2), :] = piece
            wide[k, pl.ds(1, rows // 2, stride=2), :] = piece
        spread = jnp.concatenate([wide[k] for k in range(cols // 128)], axis=1)
        spread = jnp.where(odd_col, pltpu.roll(spread, 1, 1), spread)
        sol_ref[j] = pltpu.roll(current, back, 1)[:rows, :cols] + spread


def shards(source, sample_seeds, perm_levels, perm_classes):
    h = HALO
    count, rows, cols = source.shape
    ext_x = rows + 2 * h
    width = -(-(PER_STEP * (cols + 2 * h)) // 128) * 128
    rows_halo, high, low = halo_pieces(source, perm_classes, h)
    smem = pl.BlockSpec(memory_space=pltpu.MemorySpace.SMEM)
    vmem = pl.BlockSpec(memory_space=pltpu.MemorySpace.VMEM)
    whole = lambda shape: pl.BlockSpec(shape, lambda s: (0,) * len(shape))
    solution_block, correction_block = pl.pallas_call(
        smooth_kernel,
        grid=(count // PER_STEP,),
        in_specs=[
            smem,
            smem,
            pl.BlockSpec((PER_STEP, rows, cols), lambda s: (s, 0, 0)),
            whole((rows, cols)),
            vmem,
            vmem,
            vmem,
        ],
        out_specs=[
            pl.BlockSpec((PER_STEP, rows, cols), lambda s: (s, 0, 0)),
            pl.BlockSpec((PER_STEP, rows // 2, cols // 2), lambda s: (s, 0, 0)),
        ],
        out_shape=[
            jax.ShapeDtypeStruct((count, rows, cols), jnp.float32),
            jax.ShapeDtypeStruct((count, rows // 2, cols // 2), jnp.float32),
        ],
        scratch_shapes=[
            pltpu.VMEM((ext_x, width), jnp.int32),
            pltpu.VMEM((width // 128, ext_x, 128), jnp.float32),
            pltpu.VMEM((cols // 128, rows, 128), jnp.float32),
        ],
        compiler_params=pltpu.CompilerParams(dimension_semantics=("arbitrary",)),
    )(sample_seeds, perm_levels, source, perm_classes, rows_halo, high, low)
    return solution_block, correction_block


def solution(mesh):
    placed = (P("sa", "gx", "gy"), P("sa"), P("sa", None), P("gx", "gy"))
    return jax.shard_map(
        shards,
        mesh=mesh,
        in_specs=placed,
        out_specs=(P("sa", "gx", "gy"), P("sa", "gx", "gy")),
        check_vma=False,
    )
```
